32 devices in a mesh: date: 16 (over z, x, core), strip: 2 (over y).
Axes of the slice: x: 2, y: 2, z: 4, core: 2. Of those that a mesh axis runs over, the one named last changes fastest.
Arguments:
- slc: bfloat16 [128, 2, 512, 384], P('date', None, 'strip'), as said below
- offsets: int32 [128, 3], P('date'), may hold values from 1 to 3
- owner: int32 [16], replicated, may hold values from 0 to 15, each once
Outputs:
- interferograms: float32 [128, 3, 2, 32, 96], P('date', None, None, 'strip')
- coherence: float32 [128, 3, 32, 96], P('date', None, 'strip')
- network_mean: float32 [16, 2, 32, 6], P('date', None, 'strip')
The draws below stay inside these ranges and needn't reach their ends.
Inputs may be any that keep to these rules, and one draw needn't show every extreme that they name: `slc`: each image is a common scene turned by a phase of its date plus noise of its date.
All inputs are finite; a program needn't handle non-finite values.
Results may differ from the reference program's by a relative error of at most 0.0003.
Values may be sent and summed in bfloat16 or wider, within the bound.
No kernel may reach another device: no remote copies, remote signals or barrier semaphores. Data moves between devices by JAX's collectives and lax.ppermute only.
A program may use at most 128 MiB of HBM per device.

```python
import math
import jax
import jax.numpy as jnp
from jax import lax

AZ = 384
NB = 3
LR = 16
LA = 4
DATES = 128
RANGE = 512
RL = 32
TILES = 16
TW = 6


def draw_slc(key, part):
    keys = jax.random.split(jax.random.fold_in(key, 11), 4)
    scene = jax.random.normal(keys[0], (2, RANGE, AZ), jnp.float32)
    phase = jax.random.uniform(keys[1], (DATES, 1, 1), jnp.float32, -math.pi, math.pi)
    sigma = jnp.exp(jax.random.uniform(keys[2], (DATES, 1, 1), jnp.float32, math.log(0.3), math.log(3.0)))
    noise = jax.random.normal(keys[3], (DATES, 2, RANGE, AZ), jnp.float32)
    cosine = jnp.cos(phase)
    sine = jnp.sin(phase)
    real_part = scene[0][None] * cosine - scene[1][None] * sine + sigma * noise[:, 0]
    imag_part = scene[0][None] * sine + scene[1][None] * cosine + sigma * noise[:, 1]
    return jnp.stack([real_part, imag_part], 1).astype(jnp.bfloat16)


def place_ends(values, key, smallest, largest):
    shape = values.shape
    place = [jax.random.randint(jax.random.fold_in(key, axis), (), 0, shape[axis]) for axis in range(len(shape))]
    values = values.at[tuple(place)].set(smallest)
    longest = shape.index(max(shape))
    place[longest] = (place[longest] + 1) % shape[longest]
    return values.at[tuple(place)].set(largest)


def setup_inputs(seed: int = 0) -> dict:
    key_of = jax.random.split(jax.random.key(seed), 4)
    slc = draw_slc(jax.random.fold_in(key_of[3], 71), 0)
    offsets = place_ends(jax.random.randint(key_of[1], (DATES, NB), 1, NB + 1), jax.random.fold_in(key_of[1], 1), 1, NB).astype(jnp.int32)
    owner = jax.random.permutation(key_of[2], TILES).astype(jnp.int32)
    return dict(slc=slc, offsets=offsets, owner=owner)


def looks(field):
    rows, cols = field.shape
    return field.reshape(rows // LR, LR, cols // LA, LA).sum((1, 3)) * (1.0 / (LR * LA))

def per_date(slc, offsets, date):
    own = lax.dynamic_index_in_dim(slc, date, 0, keepdims=False).astype(jnp.float32)
    pairs = []
    coher = []
    for slot in range(NB):
        partner_idx = ((date + offsets[date, slot]) % DATES).astype(jnp.int32)
        other = lax.dynamic_index_in_dim(slc, partner_idx, 0, keepdims=False).astype(jnp.float32)
        real_part = looks(own[0] * other[0] + own[1] * other[1])
        imag_part = looks(own[1] * other[0] - own[0] * other[1])
        power_a = looks(own[0] * own[0] + own[1] * own[1])
        power_b = looks(other[0] * other[0] + other[1] * other[1])
        pairs.append(jnp.stack([real_part, imag_part], 0))
        coher.append(jnp.sqrt(real_part * real_part + imag_part * imag_part) / jnp.sqrt(power_a * power_b + 1e-06))
    return (jnp.stack(pairs, 0), jnp.stack(coher, 0))

def reference(slc, offsets, owner):
    dates_all = jnp.arange(DATES, dtype=jnp.int32)
    interferograms, coherence = lax.map(lambda date: per_date(slc, offsets, date), dates_all)
    weighted = (coherence[:, :, None] * interferograms).sum((0, 1))
    weight_total = coherence.sum((0, 1))
    mean_field = weighted / (1.0 + weight_total)[None]
    tiled = mean_field.reshape(2, RL, TILES, TW).transpose(2, 0, 1, 3)
    network_mean = jnp.zeros_like(tiled).at[owner].set(tiled)
    return (interferograms, coherence, network_mean)
```

```python
import jax
import jax.numpy as jnp
from jax import lax
from jax.experimental import pallas as pl
from jax.experimental.pallas import tpu as pltpu
from jax.sharding import PartitionSpec as P

NB = 3
LR = 16
LA = 4


def shifted(value, axis, steps):
    count = lax.axis_size(axis)
    pairs = [(source, (source + steps) % count) for source in range(count)]
    return lax.ppermute(value, axis, pairs)


def split_pool(field, pool):
    hi = field.astype(jnp.bfloat16)
    rest = field - hi.astype(jnp.float32)
    mid = rest.astype(jnp.bfloat16)
    lo = (rest - mid.astype(jnp.float32)).astype(jnp.bfloat16)
    out = jnp.dot(hi, pool, preferred_element_type=jnp.float32)
    out = out + jnp.dot(mid, pool, preferred_element_type=jnp.float32)
    return out + jnp.dot(lo, pool, preferred_element_type=jnp.float32)


def make_kernel(count, rim_count, rows, cols):
    groups = rows // LR
    cells = cols // LA
    total = count + rim_count
    ctiles = cols // 128

    def kernel(off_ref, slc_ref, rim_ref, ifg_ref, coh_ref, ws_ref, xf, pacc, racc, pw):
        def conv_own(j, c):
            for ct in range(ctiles):
                xf[j, :, ct] = slc_ref[j, :, :, pl.ds(ct * 128, 128)].astype(jnp.float32)
            return c

        lax.fori_loop(0, count, conv_own, 0)

        def conv_rim(j, c):
            for ct in range(ctiles):
                xf[count + j, :, ct] = rim_ref[j, :, :, pl.ds(ct * 128, 128)].astype(jnp.float32)
            return c

        lax.fori_loop(0, rim_count, conv_rim, 0)

        lines = lax.broadcasted_iota(jnp.int32, (cols, cells), 0)
        cell = lax.broadcasted_iota(jnp.int32, (cols, cells), 1)
        pool = jnp.where(lines // LA == cell, 1.0 / (LR * LA), 0.0).astype(jnp.bfloat16)

        def strided(j, comp, s, ct):
            return xf[j, comp, ct, pl.ds(s, groups, stride=LR), :]

        def power(j, c):
            for ct in range(ctiles):
                acc = jnp.zeros((groups, 128), jnp.float32)
                for s in range(LR):
                    x0 = strided(j, 0, s, ct)
                    x1 = strided(j, 1, s, ct)
                    acc = acc + (x0 * x0 + x1 * x1)
                pacc[j, :, pl.ds(ct * 128, 128)] = acc
            return c

        lax.fori_loop(0, total, power, 0)
        pw[...] = split_pool(pacc[...].reshape(total * groups, cols), pool).reshape(total, groups, cells)

        def pairs(i, c):
            parts = [jnp.clip(i + off_ref[i, k], 0, total - 1) for k in range(NB)]
            for ct in range(ctiles):
                re = [jnp.zeros((groups, 128), jnp.float32) for _ in range(NB)]
                im = [jnp.zeros((groups, 128), jnp.float32) for _ in range(NB)]
                for s in range(LR):
                    a0 = strided(i, 0, s, ct)
                    a1 = strided(i, 1, s, ct)
                    for k in range(NB):
                        b0 = strided(parts[k], 0, s, ct)
                        b1 = strided(parts[k], 1, s, ct)
                        re[k] = re[k] + (a0 * b0 + a1 * b1)
                        im[k] = im[k] + (a1 * b0 - a0 * b1)
                for k in range(NB):
                    racc[i, k, 0, :, pl.ds(ct * 128, 128)] = re[k]
                    racc[i, k, 1, :, pl.ds(ct * 128, 128)] = im[k]
            return c

        lax.fori_loop(0, count, pairs, 0)
        pooled = split_pool(racc[...].reshape(count * NB * 2 * groups, cols), pool)
        ifg_ref[...] = pooled.reshape(count, NB, 2, groups, cells)

        def coher(i, ws):
            wr, wi, wc = ws
            pa = pw[i]
            for k in range(NB):
                j = jnp.clip(i + off_ref[i, k], 0, total - 1)
                pb = pw[j]
                re = ifg_ref[i, k, 0]
                im = ifg_ref[i, k, 1]
                co = jnp.sqrt(re * re + im * im) / jnp.sqrt(pa * pb + 1e-06)
                coh_ref[i, k] = co
                wr = wr + co * re
                wi = wi + co * im
                wc = wc + co
            return (wr, wi, wc)

        zero = jnp.zeros((groups, cells), jnp.float32)
        wr, wi, wc = lax.fori_loop(0, count, coher, (zero, zero, zero))
        ws_ref[0] = wr
        ws_ref[1] = wi
        ws_ref[2] = wc

    return kernel


def local_math(slc, rim, offsets):
    count, _, rows, cols = slc.shape
    rim_count = rim.shape[0]
    groups = rows // LR
    cells = cols // LA
    total = count + rim_count
    vmem = pltpu.VMEM
    return pl.pallas_call(
        make_kernel(count, rim_count, rows, cols),
        out_shape=(
            jax.ShapeDtypeStruct((count, NB, 2, groups, cells), jnp.float32),
            jax.ShapeDtypeStruct((count, NB, groups, cells), jnp.float32),
            jax.ShapeDtypeStruct((3, groups, cells), jnp.float32),
        ),
        in_specs=[
            pl.BlockSpec(memory_space=pltpu.SMEM),
            pl.BlockSpec(memory_space=vmem),
            pl.BlockSpec(memory_space=vmem),
        ],
        out_specs=(
            pl.BlockSpec(memory_space=vmem),
            pl.BlockSpec(memory_space=vmem),
            pl.BlockSpec(memory_space=vmem),
        ),
        scratch_shapes=[
            pltpu.VMEM((total, 2, cols // 128, rows, 128), jnp.float32),
            pltpu.VMEM((total, groups, cols), jnp.float32),
            pltpu.VMEM((count, NB, 2, groups, cols), jnp.float32),
            pltpu.VMEM((total, groups, cells), jnp.float32),
        ],
        compiler_params=pltpu.CompilerParams(vmem_limit_bytes=48 * 1024 * 1024),
    )(offsets, slc, rim)


def on_device(slc, offsets, owner):
    rim = shifted(slc[:NB], "date", -1)
    interferograms, coherence, ws = local_math(slc, rim, offsets)
    tile_count = owner.shape[0]
    rows_loc = ws.shape[1]
    width = ws.shape[2] // tile_count
    tiles = ws.reshape(3, rows_loc, tile_count, width).transpose(2, 0, 1, 3)
    slotted = jnp.zeros_like(tiles).at[owner].set(tiles)
    sums = lax.all_to_all(slotted, "date", split_axis=0, concat_axis=0, tiled=True).sum(0)
    network_mean = (sums[:2] / (1.0 + sums[2:3]))[None]
    return (interferograms, coherence, network_mean)


def solution(mesh):
    placed = (P("date", None, "strip", None), P("date", None), P())
    return jax.shard_map(
        on_device,
        mesh=mesh,
        in_specs=placed,
        out_specs=(
            P("date", None, None, "strip", None),
            P("date", None, "strip", None),
            P("date", None, "strip", None),
        ),
        check_vma=False,
    )
```

```python
import jax
import jax.numpy as jnp
from jax import lax
from jax.experimental import pallas as pl
from jax.experimental.pallas import tpu as pltpu
from jax.sharding import PartitionSpec as P

NB = 3
LR = 16
LA = 4


def shifted(value, axis, steps):
    count = lax.axis_size(axis)
    pairs = [(source, (source + steps) % count) for source in range(count)]
    return lax.ppermute(value, axis, pairs)


def split_pool(field, pool):
    hi = field.astype(jnp.bfloat16)
    rest = field - hi.astype(jnp.float32)
    mid = rest.astype(jnp.bfloat16)
    lo = (rest - mid.astype(jnp.float32)).astype(jnp.bfloat16)
    out = jnp.dot(hi, pool, preferred_element_type=jnp.float32)
    out = out + jnp.dot(mid, pool, preferred_element_type=jnp.float32)
    return out + jnp.dot(lo, pool, preferred_element_type=jnp.float32)


def make_kernel(images, first, dates, rows, cols):
    groups = rows // LR
    cells = cols // LA
    total = len(images)
    ctiles = cols // 128

    def kernel(off_ref, *refs):
        srcs = refs[:-9]
        ifg_ref, coh_ref, ws_ref, raw, xf, pacc, racc, pw, sem = refs[-9:]
        copies = []
        for t, (src, lead) in enumerate(images):
            cp = pltpu.make_async_copy(srcs[src].at[lead], raw.at[t], sem.at[t])
            cp.start()
            copies.append(cp)
        for t in range(total):
            copies[t].wait()
            for ct in range(ctiles):
                xf[t, :, ct] = raw[t, :, :, pl.ds(ct * 128, 128)].astype(jnp.float32)

        lines = lax.broadcasted_iota(jnp.int32, (cols, cells), 0)
        cell = lax.broadcasted_iota(jnp.int32, (cols, cells), 1)
        pool = jnp.where(lines // LA == cell, 1.0 / (LR * LA), 0.0).astype(jnp.bfloat16)

        def strided(j, comp, s, ct):
            return xf[j, comp, ct, pl.ds(s, groups, stride=LR), :]

        def power(j, c):
            for ct in range(ctiles):
                acc = jnp.zeros((groups, 128), jnp.float32)
                for s in range(LR):
                    x0 = strided(j, 0, s, ct)
                    x1 = strided(j, 1, s, ct)
                    acc = acc + (x0 * x0 + x1 * x1)
                pacc[j, :, pl.ds(ct * 128, 128)] = acc
            return c

        lax.fori_loop(0, total, power, 0)
        pw[...] = split_pool(pacc[...].reshape(total * groups, cols), pool).reshape(total, groups, cells)

        def partner(i, k):
            return jnp.clip(first + i + off_ref[i, k], 0, total - 1)

        def pairs(i, c):
            parts = [partner(i, k) for k in range(NB)]
            for ct in range(ctiles):
                re = [jnp.zeros((groups, 128), jnp.float32) for _ in range(NB)]
                im = [jnp.zeros((groups, 128), jnp.float32) for _ in range(NB)]
                for s in range(LR):
                    a0 = strided(first + i, 0, s, ct)
                    a1 = strided(first + i, 1, s, ct)
                    for k in range(NB):
                        b0 = strided(parts[k], 0, s, ct)
                        b1 = strided(parts[k], 1, s, ct)
                        re[k] = re[k] + (a0 * b0 + a1 * b1)
                        im[k] = im[k] + (a1 * b0 - a0 * b1)
                for k in range(NB):
                    racc[i, k, 0, :, pl.ds(ct * 128, 128)] = re[k]
                    racc[i, k, 1, :, pl.ds(ct * 128, 128)] = im[k]
            return c

        lax.fori_loop(0, dates, pairs, 0)
        pooled = split_pool(racc[...].reshape(dates * NB * 2 * groups, cols), pool)
        ifg_ref[...] = pooled.reshape(dates, NB, 2, groups, cells)

        def coher(i, ws):
            wr, wi, wc = ws
            pa = pw[first + i]
            for k in range(NB):
                pb = pw[partner(i, k)]
                re = ifg_ref[i, k, 0]
                im = ifg_ref[i, k, 1]
                co = jnp.sqrt(re * re + im * im) / jnp.sqrt(pa * pb + 1e-06)
                coh_ref[i, k] = co
                wr = wr + co * re
                wi = wi + co * im
                wc = wc + co
            return (wr, wi, wc)

        zero = jnp.zeros((groups, cells), jnp.float32)
        wr, wi, wc = lax.fori_loop(0, dates, coher, (zero, zero, zero))
        ws_ref[0] = wr
        ws_ref[1] = wi
        ws_ref[2] = wc

    return kernel


def local_math(offsets, sources, images, first, dates):
    _, _, rows, cols = sources[0].shape
    groups = rows // LR
    cells = cols // LA
    total = len(images)
    vmem = pltpu.VMEM
    return pl.pallas_call(
        make_kernel(images, first, dates, rows, cols),
        out_shape=(
            jax.ShapeDtypeStruct((dates, NB, 2, groups, cells), jnp.float32),
            jax.ShapeDtypeStruct((dates, NB, groups, cells), jnp.float32),
            jax.ShapeDtypeStruct((3, groups, cells), jnp.float32),
        ),
        in_specs=[pl.BlockSpec(memory_space=pltpu.SMEM)]
        + [pl.BlockSpec(memory_space=pl.ANY) for _ in sources],
        out_specs=(
            pl.BlockSpec(memory_space=vmem),
            pl.BlockSpec(memory_space=vmem),
            pl.BlockSpec(memory_space=vmem),
        ),
        scratch_shapes=[
            pltpu.VMEM((total, 2, rows, cols), jnp.bfloat16),
            pltpu.VMEM((total, 2, cols // 128, rows, 128), jnp.float32),
            pltpu.VMEM((total, groups, cols), jnp.float32),
            pltpu.VMEM((dates, NB, 2, groups, cols), jnp.float32),
            pltpu.VMEM((total, groups, cells), jnp.float32),
            pltpu.SemaphoreType.DMA((total,)),
        ],
        compiler_params=pltpu.CompilerParams(vmem_limit_bytes=48 * 1024 * 1024),
    )(offsets, *sources)


def on_device(slc, offsets, owner):
    count = slc.shape[0]
    inner = count - NB
    rim = shifted(slc[:NB], "date", -1)
    ifg_a, coh_a, ws_a = local_math(
        offsets[:inner], [slc], [(0, t) for t in range(count)], 0, inner
    )
    ifg_b, coh_b, ws_b = local_math(
        offsets[inner:],
        [slc, rim],
        [(0, inner + t) for t in range(NB)] + [(1, t) for t in range(NB)],
        0,
        NB,
    )
    interferograms = jnp.concatenate([ifg_a, ifg_b], 0)
    coherence = jnp.concatenate([coh_a, coh_b], 0)
    ws = ws_a + ws_b
    tile_count = owner.shape[0]
    rows_loc = ws.shape[1]
    width = ws.shape[2] // tile_count
    tiles = ws.reshape(3, rows_loc, tile_count, width).transpose(2, 0, 1, 3)
    slotted = jnp.zeros_like(tiles).at[owner].set(tiles)
    sums = lax.all_to_all(slotted, "date", split_axis=0, concat_axis=0, tiled=True).sum(0)
    network_mean = (sums[:2] / (1.0 + sums[2:3]))[None]
    return (interferograms, coherence, network_mean)


def solution(mesh):
    placed = (P("date", None, "strip", None), P("date", None), P())
    return jax.shard_map(
        on_device,
        mesh=mesh,
        in_specs=placed,
        out_specs=(
            P("date", None, None, "strip", None),
            P("date", None, "strip", None),
            P("date", None, "strip", None),
        ),
        check_vma=False,
    )
```

```python
import jax
import jax.numpy as jnp
from jax import lax
from jax.experimental import pallas as pl
from jax.experimental.pallas import tpu as pltpu
from jax.sharding import PartitionSpec as P

NB = 3
LR = 16
LA = 4


def shifted(value, axis, steps):
    count = lax.axis_size(axis)
    pairs = [(source, (source + steps) % count) for source in range(count)]
    return lax.ppermute(value, axis, pairs)


def split_pool(field, pool):
    hi = field.astype(jnp.bfloat16)
    rest = field - hi.astype(jnp.float32)
    mid = rest.astype(jnp.bfloat16)
    lo = (rest - mid.astype(jnp.float32)).astype(jnp.bfloat16)
    out = jnp.dot(hi, pool, preferred_element_type=jnp.float32)
    out = out + jnp.dot(mid, pool, preferred_element_type=jnp.float32)
    return out + jnp.dot(lo, pool, preferred_element_type=jnp.float32)


def make_kernel(images, first, dates, rows, cols):
    groups = rows // LR
    cells = cols // LA
    total = len(images)
    ctiles = cols // 128

    def kernel(off_ref, *refs):
        srcs = refs[:-9]
        ifg_ref, coh_ref, ws_ref, raw, xf, pacc, racc, pw, sem = refs[-9:]
        copies = []
        for t, (src, lead) in enumerate(images):
            cp = pltpu.make_async_copy(srcs[src].at[lead], raw.at[t], sem.at[t])
            cp.start()
            copies.append(cp)
        for t in range(total):
            copies[t].wait()
            xf[t] = raw[t].astype(jnp.float32)

        lines = lax.broadcasted_iota(jnp.int32, (cols, cells), 0)
        cell = lax.broadcasted_iota(jnp.int32, (cols, cells), 1)
        pool = jnp.where(lines // LA == cell, 1.0 / (LR * LA), 0.0).astype(jnp.bfloat16)
        sub = lax.broadcasted_iota(jnp.int32, (8, 128), 0)
        masks = {k: (sub % (2 * k)) < k for k in (4, 2, 1)}

        def combine(x, y, k):
            m = masks[k]
            return jnp.where(m, x + pltpu.roll(x, 8 - k, 0), y + pltpu.roll(y, k, 0))

        def fold(parts):
            q = [combine(parts[g], parts[g + 4], 4) for g in range(4)]
            r = [combine(q[0], q[2], 2), combine(q[1], q[3], 2)]
            return combine(r[0], r[1], 1)

        def rows_of(j, comp, g, ct):
            return xf[j, comp, pl.ds(g * LR, LR), pl.ds(ct * 128, 128)]

        def half(v):
            return v[:8] + v[8:]

        def power(j, c):
            for ct in range(ctiles):
                for blk in range(groups // 8):
                    parts = []
                    for g in range(blk * 8, blk * 8 + 8):
                        x0 = rows_of(j, 0, g, ct)
                        x1 = rows_of(j, 1, g, ct)
                        parts.append(half(x0 * x0 + x1 * x1))
                    pacc[j, pl.ds(blk * 8, 8), pl.ds(ct * 128, 128)] = fold(parts)
            return c

        lax.fori_loop(0, total, power, 0)
        pw[...] = split_pool(pacc[...].reshape(total * groups, cols), pool).reshape(total, groups, cells)

        def partner(i, k):
            return jnp.clip(first + i + off_ref[i, k], 0, total - 1)

        def pairs(i, c):
            for k in range(NB):
                j = partner(i, k)
                for ct in range(ctiles):
                    for blk in range(groups // 8):
                        re = []
                        im = []
                        for g in range(blk * 8, blk * 8 + 8):
                            a0 = rows_of(first + i, 0, g, ct)
                            a1 = rows_of(first + i, 1, g, ct)
                            b0 = rows_of(j, 0, g, ct)
                            b1 = rows_of(j, 1, g, ct)
                            re.append(half(a0 * b0 + a1 * b1))
                            im.append(half(a1 * b0 - a0 * b1))
                        racc[i, k, 0, pl.ds(blk * 8, 8), pl.ds(ct * 128, 128)] = fold(re)
                        racc[i, k, 1, pl.ds(blk * 8, 8), pl.ds(ct * 128, 128)] = fold(im)
            return c

        lax.fori_loop(0, dates, pairs, 0)
        pooled = split_pool(racc[...].reshape(dates * NB * 2 * groups, cols), pool)
        ifg_ref[...] = pooled.reshape(dates, NB, 2, groups, cells)

        def coher(i, ws):
            wr, wi, wc = ws
            pa = pw[first + i]
            for k in range(NB):
                pb = pw[partner(i, k)]
                re = ifg_ref[i, k, 0]
                im = ifg_ref[i, k, 1]
                co = jnp.sqrt(re * re + im * im) / jnp.sqrt(pa * pb + 1e-06)
                coh_ref[i, k] = co
                wr = wr + co * re
                wi = wi + co * im
                wc = wc + co
            return (wr, wi, wc)

        zero = jnp.zeros((groups, cells), jnp.float32)
        wr, wi, wc = lax.fori_loop(0, dates, coher, (zero, zero, zero))
        ws_ref[0] = wr
        ws_ref[1] = wi
        ws_ref[2] = wc

    return kernel


def local_math(offsets, sources, images, first, dates):
    _, _, rows, cols = sources[0].shape
    groups = rows // LR
    cells = cols // LA
    total = len(images)
    vmem = pltpu.VMEM
    return pl.pallas_call(
        make_kernel(images, first, dates, rows, cols),
        out_shape=(
            jax.ShapeDtypeStruct((dates, NB, 2, groups, cells), jnp.float32),
            jax.ShapeDtypeStruct((dates, NB, groups, cells), jnp.float32),
            jax.ShapeDtypeStruct((3, groups, cells), jnp.float32),
        ),
        in_specs=[pl.BlockSpec(memory_space=pltpu.SMEM)]
        + [pl.BlockSpec(memory_space=pl.ANY) for _ in sources],
        out_specs=(
            pl.BlockSpec(memory_space=vmem),
            pl.BlockSpec(memory_space=vmem),
            pl.BlockSpec(memory_space=vmem),
        ),
        scratch_shapes=[
            pltpu.VMEM((total, 2, rows, cols), jnp.bfloat16),
            pltpu.VMEM((total, 2, rows, cols), jnp.float32),
            pltpu.VMEM((total, groups, cols), jnp.float32),
            pltpu.VMEM((dates, NB, 2, groups, cols), jnp.float32),
            pltpu.VMEM((total, groups, cells), jnp.float32),
            pltpu.SemaphoreType.DMA((total,)),
        ],
        compiler_params=pltpu.CompilerParams(vmem_limit_bytes=48 * 1024 * 1024),
    )(offsets, *sources)


def on_device(slc, offsets, owner):
    count = slc.shape[0]
    inner = count - NB
    rim = shifted(slc[:NB], "date", -1)
    ifg_a, coh_a, ws_a = local_math(
        offsets[:inner], [slc], [(0, t) for t in range(count)], 0, inner
    )
    ifg_b, coh_b, ws_b = local_math(
        offsets[inner:],
        [slc, rim],
        [(0, inner + t) for t in range(NB)] + [(1, t) for t in range(NB)],
        0,
        NB,
    )
    interferograms = jnp.concatenate([ifg_a, ifg_b], 0)
    coherence = jnp.concatenate([coh_a, coh_b], 0)
    ws = ws_a + ws_b
    tile_count = owner.shape[0]
    rows_loc = ws.shape[1]
    width = ws.shape[2] // tile_count
    tiles = ws.reshape(3, rows_loc, tile_count, width).transpose(2, 0, 1, 3)
    slotted = jnp.zeros_like(tiles).at[owner].set(tiles)
    sums = lax.all_to_all(slotted, "date", split_axis=0, concat_axis=0, tiled=True).sum(0)
    network_mean = (sums[:2] / (1.0 + sums[2:3]))[None]
    return (interferograms, coherence, network_mean)


def solution(mesh):
    placed = (P("date", None, "strip", None), P("date", None), P())
    return jax.shard_map(
        on_device,
        mesh=mesh,
        in_specs=placed,
        out_specs=(
            P("date", None, None, "strip", None),
            P("date", None, "strip", None),
            P("date", None, "strip", None),
        ),
        check_vma=False,
    )
```

```python
import jax
import jax.numpy as jnp
from jax import lax
from jax.experimental import pallas as pl
from jax.experimental.pallas import tpu as pltpu
from jax.sharding import PartitionSpec as P

NB = 3
LR = 16
LA = 4


def shifted(value, axis, steps):
    count = lax.axis_size(axis)
    pairs = [(source, (source + steps) % count) for source in range(count)]
    return lax.ppermute(value, axis, pairs)


def split_pool(field, pool):
    hi = field.astype(jnp.bfloat16)
    rest = field - hi.astype(jnp.float32)
    mid = rest.astype(jnp.bfloat16)
    lo = (rest - mid.astype(jnp.float32)).astype(jnp.bfloat16)
    out = jnp.dot(hi, pool, preferred_element_type=jnp.float32)
    out = out + jnp.dot(mid, pool, preferred_element_type=jnp.float32)
    return out + jnp.dot(lo, pool, preferred_element_type=jnp.float32)


def make_kernel(images, first, dates, rows, cols, known, tiles):
    groups = rows // LR
    cells = cols // LA
    total = len(images)
    ctiles = cols // 128
    lanes = 128
    nsrc = len(set(src for src, _ in images))

    def kernel(*refs):
        off_ref = refs[0]
        if known:
            owner_ref, pw_in, ws_in = refs[1:4]
            srcs = refs[4 : 4 + nsrc]
            rest = refs[4 + nsrc :]
        else:
            srcs = refs[1 : 1 + nsrc]
            rest = refs[1 + nsrc :]
        ifg_ref, coh_ref, last_ref = rest[:3]
        if known:
            raw, xf, pacc, racc, pw, racc_pooled, sem = rest[3:]
        else:
            pw_out = rest[3]
            raw, xf, pacc, racc, pw, racc_pooled, sem = rest[4:]
        copies = []
        for t, (src, lead) in enumerate(images):
            cp = pltpu.make_async_copy(srcs[src].at[lead], raw.at[t], sem.at[t])
            cp.start()
            copies.append(cp)
        for t in range(total):
            copies[t].wait()
            xf[t] = raw[t].astype(jnp.float32)

        line = lax.broadcasted_iota(jnp.int32, (cols, lanes), 0)
        cell = lax.broadcasted_iota(jnp.int32, (cols, lanes), 1)
        pool = jnp.where(line // LA == cell, 1.0 / (LR * LA), 0.0).astype(jnp.bfloat16)
        sub = lax.broadcasted_iota(jnp.int32, (8, 128), 0)
        masks = {k: (sub % (2 * k)) < k for k in (4, 2, 1)}

        def combine(x, y, k):
            m = masks[k]
            return jnp.where(m, x + pltpu.roll(x, 8 - k, 0), y + pltpu.roll(y, k, 0))

        def fold(parts):
            q = [combine(parts[g], parts[g + 4], 4) for g in range(4)]
            r = [combine(q[0], q[2], 2), combine(q[1], q[3], 2)]
            return combine(r[0], r[1], 1)

        def rows_of(j, comp, g, ct):
            return xf[j, comp, pl.ds(g * LR, LR), pl.ds(ct * 128, 128)]

        def half(v):
            return v[:8] + v[8:]

        def power(j, c):
            for ct in range(ctiles):
                for blk in range(groups // 8):
                    parts = []
                    for g in range(blk * 8, blk * 8 + 8):
                        x0 = rows_of(j, 0, g, ct)
                        x1 = rows_of(j, 1, g, ct)
                        parts.append(half(x0 * x0 + x1 * x1))
                    pacc[j - known, pl.ds(blk * 8, 8), pl.ds(ct * 128, 128)] = fold(parts)
            return c

        lax.fori_loop(known, total, power, 0)
        fresh = total - known
        pw[pl.ds(known, fresh)] = split_pool(pacc[...].reshape(fresh * groups, cols), pool).reshape(
            fresh, groups, lanes
        )
        if known:
            pw[pl.ds(0, known)] = pw_in[...]
        else:
            pw_out[...] = pw[...]

        def partner(i, k):
            return jnp.clip(first + i + off_ref[i, k], 0, total - 1)

        def pairs(i, c):
            for k in range(NB):
                j = partner(i, k)
                for ct in range(ctiles):
                    for blk in range(groups // 8):
                        re = []
                        im = []
                        for g in range(blk * 8, blk * 8 + 8):
                            a0 = rows_of(first + i, 0, g, ct)
                            a1 = rows_of(first + i, 1, g, ct)
                            b0 = rows_of(j, 0, g, ct)
                            b1 = rows_of(j, 1, g, ct)
                            re.append(half(a0 * b0 + a1 * b1))
                            im.append(half(a1 * b0 - a0 * b1))
                        racc[i, k, 0, pl.ds(blk * 8, 8), pl.ds(ct * 128, 128)] = fold(re)
                        racc[i, k, 1, pl.ds(blk * 8, 8), pl.ds(ct * 128, 128)] = fold(im)
            return c

        lax.fori_loop(0, dates, pairs, 0)
        pooled = split_pool(racc[...].reshape(dates * NB * 2 * groups, cols), pool)
        pooled = pooled.reshape(dates, NB, 2, groups, lanes)
        ifg_ref[...] = pooled[..., :cells]

        def coher(i, ws):
            wr, wi, wc = ws
            pa = pw[first + i]
            for k in range(NB):
                pb = pw[partner(i, k)]
                re = pooled_at(i, k, 0)
                im = pooled_at(i, k, 1)
                co = jnp.sqrt(re * re + im * im) / jnp.sqrt(pa * pb + 1e-06)
                coh_ref[i, k] = co[:, :cells]
                wr = wr + co * re
                wi = wi + co * im
                wc = wc + co
            return (wr, wi, wc)

        racc_pooled[...] = pooled

        def pooled_at(i, k, comp):
            return racc_pooled[i, k, comp]

        zero = jnp.zeros((groups, lanes), jnp.float32)
        if known:
            start = (ws_in[0], ws_in[1], ws_in[2])
        else:
            start = (zero, zero, zero)
        wr, wi, wc = lax.fori_loop(0, dates, coher, start)
        if not known:
            last_ref[0] = wr
            last_ref[1] = wi
            last_ref[2] = wc
            return
        width = cells // tiles
        lane = lax.broadcasted_iota(jnp.int32, (groups, lanes), 1)
        for t in range(tiles):
            base = t * width
            block = jnp.where(
                lane < width,
                pltpu.roll(wr, (lanes - base) % lanes, 1),
                jnp.where(
                    lane < 2 * width,
                    pltpu.roll(wi, (lanes + width - base) % lanes, 1),
                    jnp.where(lane < 3 * width, pltpu.roll(wc, (lanes + 2 * width - base) % lanes, 1), 0.0),
                ),
            )
            last_ref[owner_ref[t]] = block

    return kernel


def local_math(offsets, sources, images, first, dates, known=None):
    _, _, rows, cols = sources[0].shape
    groups = rows // LR
    cells = cols // LA
    total = len(images)
    lanes = 128
    vmem = pltpu.VMEM
    smem = pltpu.SMEM
    if known is None:
        nknown, tiles, extra = 0, 0, []
        last = jax.ShapeDtypeStruct((3, groups, lanes), jnp.float32)
        outs_extra = [jax.ShapeDtypeStruct((total, groups, lanes), jnp.float32)]
    else:
        owner, pw_in, ws_in = known
        nknown, tiles, extra = pw_in.shape[0], owner.shape[0], [owner, pw_in, ws_in]
        last = jax.ShapeDtypeStruct((tiles, groups, lanes), jnp.float32)
        outs_extra = []
    out_shape = [
        jax.ShapeDtypeStruct((dates, NB, 2, groups, cells), jnp.float32),
        jax.ShapeDtypeStruct((dates, NB, groups, cells), jnp.float32),
        last,
    ] + outs_extra
    in_specs = [pl.BlockSpec(memory_space=smem)]
    if known is not None:
        in_specs += [pl.BlockSpec(memory_space=smem), pl.BlockSpec(memory_space=vmem), pl.BlockSpec(memory_space=vmem)]
    in_specs += [pl.BlockSpec(memory_space=pl.ANY) for _ in sources]
    return pl.pallas_call(
        make_kernel(images, first, dates, rows, cols, nknown, tiles),
        out_shape=tuple(out_shape),
        in_specs=in_specs,
        out_specs=tuple(pl.BlockSpec(memory_space=vmem) for _ in out_shape),
        scratch_shapes=[
            pltpu.VMEM((total, 2, rows, cols), jnp.bfloat16),
            pltpu.VMEM((total, 2, rows, cols), jnp.float32),
            pltpu.VMEM((total - nknown, groups, cols), jnp.float32),
            pltpu.VMEM((dates, NB, 2, groups, cols), jnp.float32),
            pltpu.VMEM((total, groups, lanes), jnp.float32),
            pltpu.VMEM((dates, NB, 2, groups, lanes), jnp.float32),
            pltpu.SemaphoreType.DMA((total,)),
        ],
        compiler_params=pltpu.CompilerParams(vmem_limit_bytes=48 * 1024 * 1024),
    )(offsets, *extra, *sources)


def on_device(slc, offsets, owner):
    count = slc.shape[0]
    inner = count - NB
    rim = shifted(slc[:NB], "date", -1)
    ifg_a, coh_a, ws_a, pw_a = local_math(
        offsets[:inner], [slc], [(0, t) for t in range(count)], 0, inner
    )
    ifg_b, coh_b, slotted = local_math(
        offsets[inner:],
        [slc, rim],
        [(0, inner + t) for t in range(NB)] + [(1, t) for t in range(NB)],
        0,
        NB,
        known=(owner, pw_a[inner:], ws_a),
    )
    interferograms = jnp.concatenate([ifg_a, ifg_b], 0)
    coherence = jnp.concatenate([coh_a, coh_b], 0)
    width = ifg_a.shape[-1] // owner.shape[0]
    sums = lax.all_to_all(slotted, "date", split_axis=0, concat_axis=0, tiled=True).sum(0)
    network_mean = (
        jnp.stack([sums[:, :width], sums[:, width : 2 * width]], 0) / (1.0 + sums[:, 2 * width : 3 * width])
    )[None]
    return (interferograms, coherence, network_mean)


def solution(mesh):
    placed = (P("date", None, "strip", None), P("date", None), P())
    return jax.shard_map(
        on_device,
        mesh=mesh,
        in_specs=placed,
        out_specs=(
            P("date", None, None, "strip", None),
            P("date", None, "strip", None),
            P("date", None, "strip", None),
        ),
        check_vma=False,
    )
```

```python
import jax
import jax.numpy as jnp
from jax import lax
from jax.experimental import pallas as pl
from jax.experimental.pallas import tpu as pltpu
from jax.sharding import PartitionSpec as P

NB = 3
LR = 16
LA = 4


def shifted(value, axis, steps):
    count = lax.axis_size(axis)
    pairs = [(source, (source + steps) % count) for source in range(count)]
    return lax.ppermute(value, axis, pairs)


def split_pool(field, pool):
    hi = field.astype(jnp.bfloat16)
    rest = field - hi.astype(jnp.float32)
    mid = rest.astype(jnp.bfloat16)
    lo = (rest - mid.astype(jnp.float32)).astype(jnp.bfloat16)
    out = jnp.dot(hi, pool, preferred_element_type=jnp.float32)
    out = out + jnp.dot(mid, pool, preferred_element_type=jnp.float32)
    return out + jnp.dot(lo, pool, preferred_element_type=jnp.float32)


def make_kernel(images, first, dates, rows, cols, known, tiles, date0, pw_base):
    groups = rows // LR
    cells = cols // LA
    total = len(images)
    ctiles = cols // 128
    lanes = 128
    nsrc = len(set(src for src, _ in images))

    def kernel(*refs):
        off_ref = refs[0]
        if known:
            owner_ref, pw_in, ws_in = refs[1:4]
            srcs = refs[6 : 6 + nsrc]
            rest = refs[6 + nsrc :]
            ifg_ref, coh_ref, last_ref = rest[:3]
            raw, xf, pacc, racc, pw, racc_pooled, ifg_s, coh_s, pay, ws_s, sem, osem = rest[3:]
        else:
            srcs = refs[1 : 1 + nsrc]
            rest = refs[1 + nsrc :]
            ifg_ref, coh_ref, last_ref, pw_out = rest[:4]
            raw, xf, pacc, racc, pw, racc_pooled, ifg_s, coh_s, sem, osem = rest[4:]
        if known:
            pw_cp = pltpu.make_async_copy(pw_in.at[pl.ds(pw_base, known)], pw.at[pl.ds(0, known)], osem.at[0])
            ws_cp = pltpu.make_async_copy(ws_in, ws_s, osem.at[1])
            pw_cp.start()
            ws_cp.start()
        copies = []
        for t, (src, lead) in enumerate(images):
            cp = pltpu.make_async_copy(srcs[src].at[lead], raw.at[t], sem.at[t])
            cp.start()
            copies.append(cp)
        for t in range(total):
            copies[t].wait()
            xf[t] = raw[t].astype(jnp.float32)

        line = lax.broadcasted_iota(jnp.int32, (cols, lanes), 0)
        cell = lax.broadcasted_iota(jnp.int32, (cols, lanes), 1)
        pool = jnp.where(line // LA == cell, 1.0 / (LR * LA), 0.0).astype(jnp.bfloat16)
        sub = lax.broadcasted_iota(jnp.int32, (8, 128), 0)
        masks = {k: (sub % (2 * k)) < k for k in (4, 2, 1)}

        def combine(x, y, k):
            m = masks[k]
            return jnp.where(m, x + pltpu.roll(x, 8 - k, 0), y + pltpu.roll(y, k, 0))

        def fold(parts):
            q = [combine(parts[g], parts[g + 4], 4) for g in range(4)]
            r = [combine(q[0], q[2], 2), combine(q[1], q[3], 2)]
            return combine(r[0], r[1], 1)

        def rows_of(j, comp, g, ct):
            return xf[j, comp, pl.ds(g * LR, LR), pl.ds(ct * 128, 128)]

        def half(v):
            return v[:8] + v[8:]

        def power(j, c):
            for ct in range(ctiles):
                for blk in range(groups // 8):
                    parts = []
                    for g in range(blk * 8, blk * 8 + 8):
                        x0 = rows_of(j, 0, g, ct)
                        x1 = rows_of(j, 1, g, ct)
                        parts.append(half(x0 * x0 + x1 * x1))
                    pacc[j - known, pl.ds(blk * 8, 8), pl.ds(ct * 128, 128)] = fold(parts)
            return c

        lax.fori_loop(known, total, power, 0)
        fresh = total - known
        pw[pl.ds(known, fresh)] = split_pool(pacc[...].reshape(fresh * groups, cols), pool).reshape(
            fresh, groups, lanes
        )
        if known:
            pw_cp.wait()
        else:
            pw_out[...] = pw[...]

        def partner(i, k):
            return jnp.clip(first + i + off_ref[i, k], 0, total - 1)

        def pairs(i, c):
            for k in range(NB):
                j = partner(i, k)
                for ct in range(ctiles):
                    for blk in range(groups // 8):
                        re = []
                        im = []
                        for g in range(blk * 8, blk * 8 + 8):
                            a0 = rows_of(first + i, 0, g, ct)
                            a1 = rows_of(first + i, 1, g, ct)
                            b0 = rows_of(j, 0, g, ct)
                            b1 = rows_of(j, 1, g, ct)
                            re.append(half(a0 * b0 + a1 * b1))
                            im.append(half(a1 * b0 - a0 * b1))
                        racc[i, k, 0, pl.ds(blk * 8, 8), pl.ds(ct * 128, 128)] = fold(re)
                        racc[i, k, 1, pl.ds(blk * 8, 8), pl.ds(ct * 128, 128)] = fold(im)
            return c

        lax.fori_loop(0, dates, pairs, 0)
        pooled = split_pool(racc[...].reshape(dates * NB * 2 * groups, cols), pool)
        pooled = pooled.reshape(dates, NB, 2, groups, lanes)
        ifg_s[...] = pooled[..., :cells]

        def coher(i, ws):
            wr, wi, wc = ws
            pa = pw[first + i]
            for k in range(NB):
                pb = pw[partner(i, k)]
                re = pooled_at(i, k, 0)
                im = pooled_at(i, k, 1)
                co = jnp.sqrt(re * re + im * im) / jnp.sqrt(pa * pb + 1e-06)
                coh_s[i, k] = co[:, :cells]
                wr = wr + co * re
                wi = wi + co * im
                wc = wc + co
            return (wr, wi, wc)

        racc_pooled[...] = pooled

        def pooled_at(i, k, comp):
            return racc_pooled[i, k, comp]

        zero = jnp.zeros((groups, lanes), jnp.float32)
        if known:
            ws_cp.wait()
            start = (ws_s[0], ws_s[1], ws_s[2])
        else:
            start = (zero, zero, zero)
        wr, wi, wc = lax.fori_loop(0, dates, coher, start)
        outs = [
            pltpu.make_async_copy(ifg_s, ifg_ref.at[pl.ds(date0, dates)], osem.at[2]),
            pltpu.make_async_copy(coh_s, coh_ref.at[pl.ds(date0, dates)], osem.at[3]),
        ]
        for cp in outs:
            cp.start()
        if not known:
            last_ref[0] = wr
            last_ref[1] = wi
            last_ref[2] = wc
            for cp in outs:
                cp.wait()
            return
        width = cells // tiles
        lane = lax.broadcasted_iota(jnp.int32, (groups, lanes), 1)
        for t in range(tiles):
            base = t * width
            block = jnp.where(
                lane < width,
                pltpu.roll(wr, (lanes - base) % lanes, 1),
                jnp.where(
                    lane < 2 * width,
                    pltpu.roll(wi, (lanes + width - base) % lanes, 1),
                    jnp.where(lane < 3 * width, pltpu.roll(wc, (lanes + 2 * width - base) % lanes, 1), 0.0),
                ),
            )
            pay[owner_ref[t]] = block
        pay_cp = pltpu.make_async_copy(pay, last_ref, osem.at[4])
        pay_cp.start()
        for cp in outs:
            cp.wait()
        pay_cp.wait()

    return kernel


def local_math(offsets, sources, images, first, dates, count, date0, known=None):
    _, _, rows, cols = sources[0].shape
    groups = rows // LR
    cells = cols // LA
    total = len(images)
    lanes = 128
    vmem = pltpu.VMEM
    smem = pltpu.SMEM
    anyspace = pl.BlockSpec(memory_space=pl.ANY)
    hbm = pl.BlockSpec(memory_space=pltpu.HBM)
    full = [
        jax.ShapeDtypeStruct((count, NB, 2, groups, cells), jnp.float32),
        jax.ShapeDtypeStruct((count, NB, groups, cells), jnp.float32),
    ]
    scratch = [
        pltpu.VMEM((total, 2, rows, cols), jnp.bfloat16),
        pltpu.VMEM((total, 2, rows, cols), jnp.float32),
        None,
        pltpu.VMEM((dates, NB, 2, groups, cols), jnp.float32),
        pltpu.VMEM((total, groups, lanes), jnp.float32),
        pltpu.VMEM((dates, NB, 2, groups, lanes), jnp.float32),
        pltpu.VMEM((dates, NB, 2, groups, cells), jnp.float32),
        pltpu.VMEM((dates, NB, groups, cells), jnp.float32),
    ]
    if known is None:
        nknown, tiles, pw_base = 0, 0, 0
        out_shape = full + [
            jax.ShapeDtypeStruct((3, groups, lanes), jnp.float32),
            jax.ShapeDtypeStruct((total, groups, lanes), jnp.float32),
        ]
        out_specs = [anyspace, anyspace, pl.BlockSpec(memory_space=vmem), pl.BlockSpec(memory_space=vmem)]
        in_specs = [pl.BlockSpec(memory_space=smem)] + [hbm for _ in sources]
        extra = []
        aliases = {}
    else:
        owner, pw_in, ws_in, ifg_in, coh_in, pw_base = known
        nknown, tiles = NB, owner.shape[0]
        out_shape = full + [jax.ShapeDtypeStruct((tiles, groups, lanes), jnp.float32)]
        out_specs = [anyspace, anyspace, anyspace]
        in_specs = [pl.BlockSpec(memory_space=smem), pl.BlockSpec(memory_space=smem)] + [
            anyspace for _ in range(4)
        ] + [hbm for _ in sources]
        extra = [owner, pw_in, ws_in, ifg_in, coh_in]
        aliases = {4: 0, 5: 1}
        scratch += [pltpu.VMEM((tiles, groups, lanes), jnp.float32), pltpu.VMEM((3, groups, lanes), jnp.float32)]
    scratch[2] = pltpu.VMEM((total - nknown, groups, cols), jnp.float32)
    scratch += [pltpu.SemaphoreType.DMA((total,)), pltpu.SemaphoreType.DMA((5,))]
    return pl.pallas_call(
        make_kernel(images, first, dates, rows, cols, nknown, tiles, date0, pw_base),
        out_shape=tuple(out_shape),
        in_specs=in_specs,
        out_specs=tuple(out_specs),
        scratch_shapes=scratch,
        input_output_aliases=aliases,
        compiler_params=pltpu.CompilerParams(vmem_limit_bytes=48 * 1024 * 1024),
    )(offsets, *extra, *sources)


def on_device(slc, offsets, owner):
    count = slc.shape[0]
    inner = count - NB
    rim = shifted(slc[:NB], "date", -1)
    ifg_a, coh_a, ws_a, pw_a = local_math(
        offsets[:inner], [slc], [(0, t) for t in range(count)], 0, inner, count, 0
    )
    interferograms, coherence, slotted = local_math(
        offsets[inner:],
        [slc, rim],
        [(0, inner + t) for t in range(NB)] + [(1, t) for t in range(NB)],
        0,
        NB,
        count,
        inner,
        known=(owner, pw_a, ws_a, ifg_a, coh_a, inner),
    )
    width = ifg_a.shape[-1] // owner.shape[0]
    sums = lax.all_to_all(slotted, "date", split_axis=0, concat_axis=0, tiled=True).sum(0)
    network_mean = (
        jnp.stack([sums[:, :width], sums[:, width : 2 * width]], 0) / (1.0 + sums[:, 2 * width : 3 * width])
    )[None]
    return (interferograms, coherence, network_mean)


def solution(mesh):
    placed = (P("date", None, "strip", None), P("date", None), P())
    return jax.shard_map(
        on_device,
        mesh=mesh,
        in_specs=placed,
        out_specs=(
            P("date", None, None, "strip", None),
            P("date", None, "strip", None),
            P("date", None, "strip", None),
        ),
        check_vma=False,
    )
```

```python
import jax
import jax.numpy as jnp
from jax import lax
from jax.experimental import pallas as pl
from jax.experimental.pallas import tpu as pltpu
from jax.sharding import PartitionSpec as P

NB = 3
LR = 16
LA = 4


def shifted(value, axis, steps):
    count = lax.axis_size(axis)
    pairs = [(source, (source + steps) % count) for source in range(count)]
    return lax.ppermute(value, axis, pairs)


def split_pool(field, pool):
    hi = field.astype(jnp.bfloat16)
    rest = field - hi.astype(jnp.float32)
    mid = rest.astype(jnp.bfloat16)
    lo = (rest - mid.astype(jnp.float32)).astype(jnp.bfloat16)
    out = jnp.dot(hi, pool, preferred_element_type=jnp.float32)
    out = out + jnp.dot(mid, pool, preferred_element_type=jnp.float32)
    return out + jnp.dot(lo, pool, preferred_element_type=jnp.float32)


def make_kernel(images, first, dates, rows, cols, known, tiles, date0, pw_base):
    groups = rows // LR
    cells = cols // LA
    total = len(images)
    ctiles = cols // 128
    lanes = 128
    nsrc = len(set(src for src, _ in images))

    def kernel(*refs):
        off_ref = refs[0]
        if known:
            owner_ref, pw_in, ws_in = refs[1:4]
            srcs = refs[6 : 6 + nsrc]
            rest = refs[6 + nsrc :]
            ifg_ref, coh_ref, last_ref = rest[:3]
            raw, xf, pacc, racc, pw, racc_pooled, ifg_s, coh_s, pay, ws_s, sem, osem = rest[3:]
        else:
            srcs = refs[1 : 1 + nsrc]
            rest = refs[1 + nsrc :]
            ifg_ref, coh_ref, last_ref, pw_out = rest[:4]
            raw, xf, pacc, racc, pw, racc_pooled, ifg_s, coh_s, sem, osem = rest[4:]
        if known:
            pw_cp = pltpu.make_async_copy(pw_in.at[pl.ds(pw_base, known)], pw.at[pl.ds(0, known)], osem.at[0])
            ws_cp = pltpu.make_async_copy(ws_in, ws_s, osem.at[1])
            pw_cp.start()
            ws_cp.start()
        copies = []
        for t, (src, lead) in enumerate(images):
            cp = pltpu.make_async_copy(srcs[src].at[lead], raw.at[t], sem.at[t])
            cp.start()
            copies.append(cp)
        for t in range(total):
            copies[t].wait()
            xf[t] = raw[t].astype(jnp.float32)

        line = lax.broadcasted_iota(jnp.int32, (cols, lanes), 0)
        cell = lax.broadcasted_iota(jnp.int32, (cols, lanes), 1)
        pool = jnp.where(line // LA == cell, 1.0 / (LR * LA), 0.0).astype(jnp.bfloat16)
        sub = lax.broadcasted_iota(jnp.int32, (8, 128), 0)
        masks = {k: (sub % (2 * k)) < k for k in (4, 2, 1)}

        def combine(x, y, k):
            m = masks[k]
            return jnp.where(m, x + pltpu.roll(x, 8 - k, 0), y + pltpu.roll(y, k, 0))

        def fold(parts):
            q = [combine(parts[g], parts[g + 4], 4) for g in range(4)]
            r = [combine(q[0], q[2], 2), combine(q[1], q[3], 2)]
            return combine(r[0], r[1], 1)

        def rows_of(j, comp, g, ct):
            return xf[j, comp, pl.ds(g * LR, LR), pl.ds(ct * 128, 128)]

        def half(v):
            return v[:8] + v[8:]

        def power(j, c):
            for ct in range(ctiles):
                for blk in range(groups // 8):
                    parts = []
                    for g in range(blk * 8, blk * 8 + 8):
                        x0 = rows_of(j, 0, g, ct)
                        x1 = rows_of(j, 1, g, ct)
                        parts.append(half(x0 * x0 + x1 * x1))
                    pacc[j - known, pl.ds(blk * 8, 8), pl.ds(ct * 128, 128)] = fold(parts)
            return c

        lax.fori_loop(known, total, power, 0)
        fresh = total - known
        pw[pl.ds(known, fresh)] = split_pool(pacc[...].reshape(fresh * groups, cols), pool).reshape(
            fresh, groups, lanes
        )
        if known:
            pw_cp.wait()
        else:
            pw_out[...] = pw[...]

        def partner(i, k):
            return jnp.clip(first + i + off_ref[i, k], 0, total - 1)

        def pairs(i, c):
            for k in range(NB):
                j = partner(i, k)
                for ct in range(ctiles):
                    for blk in range(groups // 8):
                        re = []
                        im = []
                        for g in range(blk * 8, blk * 8 + 8):
                            a0 = rows_of(first + i, 0, g, ct)
                            a1 = rows_of(first + i, 1, g, ct)
                            b0 = rows_of(j, 0, g, ct)
                            b1 = rows_of(j, 1, g, ct)
                            re.append(half(a0 * b0 + a1 * b1))
                            im.append(half(a1 * b0 - a0 * b1))
                        racc[i, k, 0, pl.ds(blk * 8, 8), pl.ds(ct * 128, 128)] = fold(re)
                        racc[i, k, 1, pl.ds(blk * 8, 8), pl.ds(ct * 128, 128)] = fold(im)
            return c

        lax.fori_loop(0, dates, pairs, 0)
        pooled = split_pool(racc[...].reshape(dates * NB * 2 * groups, cols), pool)
        pooled = pooled.reshape(dates, NB, 2, groups, lanes)
        ifg_s[...] = pooled[..., :cells]

        def coher(i, ws):
            wr, wi, wc = ws
            pa = pw[first + i]
            for k in range(NB):
                pb = pw[partner(i, k)]
                re = pooled_at(i, k, 0)
                im = pooled_at(i, k, 1)
                co = jnp.sqrt(re * re + im * im) / jnp.sqrt(pa * pb + 1e-06)
                coh_s[i, k] = co[:, :cells]
                wr = wr + co * re
                wi = wi + co * im
                wc = wc + co
            return (wr, wi, wc)

        racc_pooled[...] = pooled

        def pooled_at(i, k, comp):
            return racc_pooled[i, k, comp]

        zero = jnp.zeros((groups, lanes), jnp.float32)
        if known:
            ws_cp.wait()
            start = (ws_s[0], ws_s[1], ws_s[2])
        else:
            start = (zero, zero, zero)
        wr, wi, wc = lax.fori_loop(0, dates, coher, start)
        outs = [
            pltpu.make_async_copy(ifg_s, ifg_ref.at[pl.ds(date0, dates)], osem.at[2]),
            pltpu.make_async_copy(coh_s, coh_ref.at[pl.ds(date0, dates)], osem.at[3]),
        ]
        for cp in outs:
            cp.start()
        if not known:
            last_ref[0] = wr
            last_ref[1] = wi
            last_ref[2] = wc
            for cp in outs:
                cp.wait()
            return
        width = cells // tiles
        lane = lax.broadcasted_iota(jnp.int32, (groups, lanes), 1)
        for t in range(tiles):
            base = t * width
            block = jnp.where(
                lane < width,
                pltpu.roll(wr, (lanes - base) % lanes, 1),
                jnp.where(
                    lane < 2 * width,
                    pltpu.roll(wi, (lanes + width - base) % lanes, 1),
                    jnp.where(lane < 3 * width, pltpu.roll(wc, (lanes + 2 * width - base) % lanes, 1), 0.0),
                ),
            )
            pay[owner_ref[t]] = block
        pay_cp = pltpu.make_async_copy(pay, last_ref, osem.at[4])
        pay_cp.start()
        for cp in outs:
            cp.wait()
        pay_cp.wait()

    return kernel


def local_math(offsets, sources, images, first, dates, count, date0, known=None):
    _, _, rows, cols = sources[0].shape
    groups = rows // LR
    cells = cols // LA
    total = len(images)
    lanes = 128
    vmem = pltpu.VMEM
    smem = pltpu.SMEM
    anyspace = pl.BlockSpec(memory_space=pl.ANY)
    hbm = pl.BlockSpec(memory_space=pltpu.HBM)
    full = [
        jax.ShapeDtypeStruct((count, NB, 2, groups, cells), jnp.float32),
        jax.ShapeDtypeStruct((count, NB, groups, cells), jnp.float32),
    ]
    scratch = [
        pltpu.VMEM((total, 2, rows, cols), jnp.bfloat16),
        pltpu.VMEM((total, 2, rows, cols), jnp.float32),
        None,
        pltpu.VMEM((dates, NB, 2, groups, cols), jnp.float32),
        pltpu.VMEM((total, groups, lanes), jnp.float32),
        pltpu.VMEM((dates, NB, 2, groups, lanes), jnp.float32),
        pltpu.VMEM((dates, NB, 2, groups, cells), jnp.float32),
        pltpu.VMEM((dates, NB, groups, cells), jnp.float32),
    ]
    if known is None:
        nknown, tiles, pw_base = 0, 0, 0
        out_shape = full + [
            jax.ShapeDtypeStruct((3, groups, lanes), jnp.float32),
            jax.ShapeDtypeStruct((total, groups, lanes), jnp.float32),
        ]
        out_specs = [anyspace, anyspace, pl.BlockSpec(memory_space=vmem), pl.BlockSpec(memory_space=vmem)]
        in_specs = [pl.BlockSpec(memory_space=smem)] + [hbm for _ in sources]
        extra = []
        aliases = {}
    else:
        owner, pw_in, ws_in, ifg_in, coh_in, pw_base = known
        nknown, tiles = NB, owner.shape[0]
        out_shape = full + [jax.ShapeDtypeStruct((tiles, groups, lanes), jnp.float32)]
        out_specs = [anyspace, anyspace, anyspace]
        in_specs = [pl.BlockSpec(memory_space=smem), pl.BlockSpec(memory_space=smem)] + [
            anyspace for _ in range(4)
        ] + [hbm for _ in sources]
        extra = [owner, pw_in, ws_in, ifg_in, coh_in]
        aliases = {4: 0, 5: 1}
        scratch += [pltpu.VMEM((tiles, groups, lanes), jnp.float32), pltpu.VMEM((3, groups, lanes), jnp.float32)]
    scratch[2] = pltpu.VMEM((total - nknown, groups, cols), jnp.float32)
    scratch += [pltpu.SemaphoreType.DMA((total,)), pltpu.SemaphoreType.DMA((5,))]
    return pl.pallas_call(
        make_kernel(images, first, dates, rows, cols, nknown, tiles, date0, pw_base),
        out_shape=tuple(out_shape),
        in_specs=in_specs,
        out_specs=tuple(out_specs),
        scratch_shapes=scratch,
        input_output_aliases=aliases,
        compiler_params=pltpu.CompilerParams(vmem_limit_bytes=48 * 1024 * 1024),
    )(offsets, *extra, *sources)


def head_of(slc):
    def kernel(src, out, sem):
        cp = pltpu.make_async_copy(src.at[pl.ds(0, NB)], out, sem.at[0])
        cp.start()
        cp.wait()

    return pl.pallas_call(
        kernel,
        out_shape=jax.ShapeDtypeStruct((NB,) + slc.shape[1:], slc.dtype),
        in_specs=[pl.BlockSpec(memory_space=pltpu.HBM)],
        out_specs=pl.BlockSpec(memory_space=pl.ANY),
        scratch_shapes=[pltpu.SemaphoreType.DMA((1,))],
    )(slc)


def on_device(slc, offsets, owner):
    count = slc.shape[0]
    inner = count - NB
    rim = shifted(head_of(slc), "date", -1)
    ifg_a, coh_a, ws_a, pw_a = local_math(
        offsets[:inner], [slc], [(0, t) for t in range(count)], 0, inner, count, 0
    )
    interferograms, coherence, slotted = local_math(
        offsets[inner:],
        [slc, rim],
        [(0, inner + t) for t in range(NB)] + [(1, t) for t in range(NB)],
        0,
        NB,
        count,
        inner,
        known=(owner, pw_a, ws_a, ifg_a, coh_a, inner),
    )
    width = ifg_a.shape[-1] // owner.shape[0]
    sums = lax.all_to_all(slotted, "date", split_axis=0, concat_axis=0, tiled=True).sum(0)
    network_mean = (
        jnp.stack([sums[:, :width], sums[:, width : 2 * width]], 0) / (1.0 + sums[:, 2 * width : 3 * width])
    )[None]
    return (interferograms, coherence, network_mean)


def solution(mesh):
    placed = (P("date", None, "strip", None), P("date", None), P())
    return jax.shard_map(
        on_device,
        mesh=mesh,
        in_specs=placed,
        out_specs=(
            P("date", None, None, "strip", None),
            P("date", None, "strip", None),
            P("date", None, "strip", None),
        ),
        check_vma=False,
    )
```

```python
import jax
import jax.numpy as jnp
from jax import lax
from jax.experimental import pallas as pl
from jax.experimental.pallas import tpu as pltpu
from jax.sharding import PartitionSpec as P

NB = 3
LR = 16
LA = 4


def shifted(value, axis, steps):
    count = lax.axis_size(axis)
    pairs = [(source, (source + steps) % count) for source in range(count)]
    return lax.ppermute(value, axis, pairs)


def split_pool(field, pool):
    hi = field.astype(jnp.bfloat16)
    rest = field - hi.astype(jnp.float32)
    mid = rest.astype(jnp.bfloat16)
    lo = (rest - mid.astype(jnp.float32)).astype(jnp.bfloat16)
    out = jnp.dot(hi, pool, preferred_element_type=jnp.float32)
    out = out + jnp.dot(mid, pool, preferred_element_type=jnp.float32)
    return out + jnp.dot(lo, pool, preferred_element_type=jnp.float32)


def make_kernel(images, first, dates, rows, cols, known, tiles, date0, pw_base):
    groups = rows // LR
    cells = cols // LA
    total = len(images)
    ctiles = cols // 128
    lanes = 128
    nsrc = len(set(src for src, _ in images))

    def kernel(*refs):
        off_ref = refs[0]
        if known:
            owner_ref, pw_in, ws_in, rx_in = refs[1:5]
            srcs = refs[7 : 7 + nsrc]
            rest = refs[7 + nsrc :]
            ifg_ref, coh_ref, last_ref = rest[:3]
            raw, xf, pacc, racc, pw, racc_pooled, ifg_s, coh_s, pay, ws_s, sem, osem = rest[3:]
        else:
            srcs = refs[1 : 1 + nsrc]
            rest = refs[1 + nsrc :]
            ifg_ref, coh_ref, last_ref, pw_out, racc_x = rest[:5]
            raw, xf, pacc, racc, pw, racc_pooled, ifg_s, coh_s, sem, osem = rest[5:]
        if known:
            pw_cp = pltpu.make_async_copy(pw_in.at[pl.ds(pw_base, known)], pw.at[pl.ds(0, known)], osem.at[0])
            ws_cp = pltpu.make_async_copy(ws_in, ws_s, osem.at[1])
            rx_cp = pltpu.make_async_copy(rx_in, racc, osem.at[2])
            pw_cp.start()
            ws_cp.start()
            rx_cp.start()
        copies = []
        for t, (src, lead) in enumerate(images):
            cp = pltpu.make_async_copy(srcs[src].at[lead], raw.at[t], sem.at[t])
            cp.start()
            copies.append(cp)
        for t in range(total):
            copies[t].wait()
            xf[t] = raw[t].astype(jnp.float32)

        line = lax.broadcasted_iota(jnp.int32, (cols, lanes), 0)
        cell = lax.broadcasted_iota(jnp.int32, (cols, lanes), 1)
        pool = jnp.where(line // LA == cell, 1.0 / (LR * LA), 0.0).astype(jnp.bfloat16)
        sub = lax.broadcasted_iota(jnp.int32, (8, 128), 0)
        masks = {k: (sub % (2 * k)) < k for k in (4, 2, 1)}

        def combine(x, y, k):
            m = masks[k]
            return jnp.where(m, x + pltpu.roll(x, 8 - k, 0), y + pltpu.roll(y, k, 0))

        def fold(parts):
            q = [combine(parts[g], parts[g + 4], 4) for g in range(4)]
            r = [combine(q[0], q[2], 2), combine(q[1], q[3], 2)]
            return combine(r[0], r[1], 1)

        def rows_of(j, comp, g, ct):
            return xf[j, comp, pl.ds(g * LR, LR), pl.ds(ct * 128, 128)]

        def half(v):
            return v[:8] + v[8:]

        def power(j, c):
            for ct in range(ctiles):
                for blk in range(groups // 8):
                    parts = []
                    for g in range(blk * 8, blk * 8 + 8):
                        x0 = rows_of(j, 0, g, ct)
                        x1 = rows_of(j, 1, g, ct)
                        parts.append(half(x0 * x0 + x1 * x1))
                    pacc[j - known, pl.ds(blk * 8, 8), pl.ds(ct * 128, 128)] = fold(parts)
            return c

        lax.fori_loop(known, total, power, 0)
        fresh = total - known
        pw[pl.ds(known, fresh)] = split_pool(pacc[...].reshape(fresh * groups, cols), pool).reshape(
            fresh, groups, lanes
        )
        if known:
            pw_cp.wait()
        else:
            pw_out[...] = pw[...]

        def partner(i, k):
            return jnp.clip(first + i + off_ref[i, k], 0, total - 1)

        def wanted(i, k):
            reach = first + i + off_ref[i, k]
            if known:
                return reach >= known
            return jnp.logical_or(i < dates, reach <= total - 1)

        def pairs(i, c):
            for k in range(NB):
                j = partner(i, k)

                @pl.when(wanted(i, k))
                def _():
                    for ct in range(ctiles):
                        for blk in range(groups // 8):
                            re = []
                            im = []
                            for g in range(blk * 8, blk * 8 + 8):
                                a0 = rows_of(first + i, 0, g, ct)
                                a1 = rows_of(first + i, 1, g, ct)
                                b0 = rows_of(j, 0, g, ct)
                                b1 = rows_of(j, 1, g, ct)
                                re.append(half(a0 * b0 + a1 * b1))
                                im.append(half(a1 * b0 - a0 * b1))
                            racc[i, k, 0, pl.ds(blk * 8, 8), pl.ds(ct * 128, 128)] = fold(re)
                            racc[i, k, 1, pl.ds(blk * 8, 8), pl.ds(ct * 128, 128)] = fold(im)

            return c

        if known:
            rx_cp.wait()
        lax.fori_loop(0, racc.shape[0], pairs, 0)
        if not known:
            racc_x[...] = racc[pl.ds(dates, racc.shape[0] - dates)]
        pooled = split_pool(racc[pl.ds(0, dates)].reshape(dates * NB * 2 * groups, cols), pool)
        pooled = pooled.reshape(dates, NB, 2, groups, lanes)
        ifg_s[...] = pooled[..., :cells]

        def coher(i, ws):
            wr, wi, wc = ws
            pa = pw[first + i]
            for k in range(NB):
                pb = pw[partner(i, k)]
                re = pooled_at(i, k, 0)
                im = pooled_at(i, k, 1)
                co = jnp.sqrt(re * re + im * im) / jnp.sqrt(pa * pb + 1e-06)
                coh_s[i, k] = co[:, :cells]
                wr = wr + co * re
                wi = wi + co * im
                wc = wc + co
            return (wr, wi, wc)

        racc_pooled[...] = pooled

        def pooled_at(i, k, comp):
            return racc_pooled[i, k, comp]

        zero = jnp.zeros((groups, lanes), jnp.float32)
        if known:
            ws_cp.wait()
            start = (ws_s[0], ws_s[1], ws_s[2])
        else:
            start = (zero, zero, zero)
        wr, wi, wc = lax.fori_loop(0, dates, coher, start)
        outs = [
            pltpu.make_async_copy(ifg_s, ifg_ref.at[pl.ds(date0, dates)], osem.at[3]),
            pltpu.make_async_copy(coh_s, coh_ref.at[pl.ds(date0, dates)], osem.at[4]),
        ]
        for cp in outs:
            cp.start()
        if not known:
            last_ref[0] = wr
            last_ref[1] = wi
            last_ref[2] = wc
            for cp in outs:
                cp.wait()
            return
        width = cells // tiles
        lane = lax.broadcasted_iota(jnp.int32, (groups, lanes), 1)
        for t in range(tiles):
            base = t * width
            block = jnp.where(
                lane < width,
                pltpu.roll(wr, (lanes - base) % lanes, 1),
                jnp.where(
                    lane < 2 * width,
                    pltpu.roll(wi, (lanes + width - base) % lanes, 1),
                    jnp.where(lane < 3 * width, pltpu.roll(wc, (lanes + 2 * width - base) % lanes, 1), 0.0),
                ),
            )
            pay[owner_ref[t]] = block
        pay_cp = pltpu.make_async_copy(pay, last_ref, osem.at[5])
        pay_cp.start()
        for cp in outs:
            cp.wait()
        pay_cp.wait()

    return kernel


def local_math(offsets, sources, images, first, dates, count, date0, known=None):
    pair_dates = offsets.shape[0]
    _, _, rows, cols = sources[0].shape
    groups = rows // LR
    cells = cols // LA
    total = len(images)
    lanes = 128
    vmem = pltpu.VMEM
    smem = pltpu.SMEM
    anyspace = pl.BlockSpec(memory_space=pl.ANY)
    hbm = pl.BlockSpec(memory_space=pltpu.HBM)
    full = [
        jax.ShapeDtypeStruct((count, NB, 2, groups, cells), jnp.float32),
        jax.ShapeDtypeStruct((count, NB, groups, cells), jnp.float32),
    ]
    scratch = [
        pltpu.VMEM((total, 2, rows, cols), jnp.bfloat16),
        pltpu.VMEM((total, 2, rows, cols), jnp.float32),
        None,
        pltpu.VMEM((pair_dates, NB, 2, groups, cols), jnp.float32),
        pltpu.VMEM((total, groups, lanes), jnp.float32),
        pltpu.VMEM((dates, NB, 2, groups, lanes), jnp.float32),
        pltpu.VMEM((dates, NB, 2, groups, cells), jnp.float32),
        pltpu.VMEM((dates, NB, groups, cells), jnp.float32),
    ]
    if known is None:
        nknown, tiles, pw_base = 0, 0, 0
        out_shape = full + [
            jax.ShapeDtypeStruct((3, groups, lanes), jnp.float32),
            jax.ShapeDtypeStruct((total, groups, lanes), jnp.float32),
            jax.ShapeDtypeStruct((pair_dates - dates, NB, 2, groups, cols), jnp.float32),
        ]
        out_specs = [anyspace, anyspace] + [pl.BlockSpec(memory_space=vmem) for _ in range(3)]
        in_specs = [pl.BlockSpec(memory_space=smem)] + [hbm for _ in sources]
        extra = []
        aliases = {}
    else:
        owner, pw_in, ws_in, rx_in, ifg_in, coh_in, pw_base = known
        nknown, tiles = NB, owner.shape[0]
        out_shape = full + [jax.ShapeDtypeStruct((tiles, groups, lanes), jnp.float32)]
        out_specs = [anyspace, anyspace, anyspace]
        in_specs = [pl.BlockSpec(memory_space=smem), pl.BlockSpec(memory_space=smem)] + [
            anyspace for _ in range(5)
        ] + [hbm for _ in sources]
        extra = [owner, pw_in, ws_in, rx_in, ifg_in, coh_in]
        aliases = {5: 0, 6: 1}
        scratch += [pltpu.VMEM((tiles, groups, lanes), jnp.float32), pltpu.VMEM((3, groups, lanes), jnp.float32)]
    scratch[2] = pltpu.VMEM((total - nknown, groups, cols), jnp.float32)
    scratch += [pltpu.SemaphoreType.DMA((total,)), pltpu.SemaphoreType.DMA((6,))]
    return pl.pallas_call(
        make_kernel(images, first, dates, rows, cols, nknown, tiles, date0, pw_base),
        out_shape=tuple(out_shape),
        in_specs=in_specs,
        out_specs=tuple(out_specs),
        scratch_shapes=scratch,
        input_output_aliases=aliases,
        compiler_params=pltpu.CompilerParams(vmem_limit_bytes=48 * 1024 * 1024),
    )(offsets, *extra, *sources)


def on_device(slc, offsets, owner):
    count = slc.shape[0]
    inner = count - NB
    rim = shifted(slc[:NB], "date", -1)
    ifg_a, coh_a, ws_a, pw_a, rx_a = local_math(
        offsets, [slc], [(0, t) for t in range(count)], 0, inner, count, 0
    )
    interferograms, coherence, slotted = local_math(
        offsets[inner:],
        [slc, rim],
        [(0, inner + t) for t in range(NB)] + [(1, t) for t in range(NB)],
        0,
        NB,
        count,
        inner,
        known=(owner, pw_a, ws_a, rx_a, ifg_a, coh_a, inner),
    )
    width = ifg_a.shape[-1] // owner.shape[0]
    sums = lax.all_to_all(slotted, "date", split_axis=0, concat_axis=0, tiled=True).sum(0)
    network_mean = (
        jnp.stack([sums[:, :width], sums[:, width : 2 * width]], 0) / (1.0 + sums[:, 2 * width : 3 * width])
    )[None]
    return (interferograms, coherence, network_mean)


def solution(mesh):
    placed = (P("date", None, "strip", None), P("date", None), P())
    return jax.shard_map(
        on_device,
        mesh=mesh,
        in_specs=placed,
        out_specs=(
            P("date", None, None, "strip", None),
            P("date", None, "strip", None),
            P("date", None, "strip", None),
        ),
        check_vma=False,
    )
```

```python
import jax
import jax.numpy as jnp
from jax import lax
from jax.experimental import pallas as pl
from jax.experimental.pallas import tpu as pltpu
from jax.sharding import PartitionSpec as P

NB = 3
LR = 16
LA = 4


def shifted(value, axis, steps):
    count = lax.axis_size(axis)
    pairs = [(source, (source + steps) % count) for source in range(count)]
    return lax.ppermute(value, axis, pairs)


def split_pool(field, pool):
    hi = field.astype(jnp.bfloat16)
    rest = field - hi.astype(jnp.float32)
    mid = rest.astype(jnp.bfloat16)
    lo = (rest - mid.astype(jnp.float32)).astype(jnp.bfloat16)
    out = jnp.dot(hi, pool, preferred_element_type=jnp.float32)
    out = out + jnp.dot(mid, pool, preferred_element_type=jnp.float32)
    return out + jnp.dot(lo, pool, preferred_element_type=jnp.float32)


def make_kernel(images, first, dates, rows, cols, known, tiles, date0, pw_base):
    groups = rows // LR
    cells = cols // LA
    total = len(images)
    ctiles = cols // 128
    lanes = 128
    nsrc = len(set(src for src, _ in images))

    def kernel(*refs):
        off_ref = refs[0]
        if known:
            owner_ref, pw_in, ws_in, rx_in = refs[1:5]
            srcs = refs[7 : 7 + nsrc]
            rest = refs[7 + nsrc :]
            ifg_ref, coh_ref, last_ref = rest[:3]
            xf, pacc, racc, pw, racc_pooled, ifg_s, coh_s, pay, ws_s, osem = rest[3:]
        else:
            srcs = refs[1 : 1 + nsrc]
            rest = refs[1 + nsrc :]
            ifg_ref, coh_ref, last_ref, pw_out, racc_x = rest[:5]
            xf, pacc, racc, pw, racc_pooled, ifg_s, coh_s, osem = rest[5:]
        if known:
            pw_cp = pltpu.make_async_copy(pw_in.at[pl.ds(pw_base, known)], pw.at[pl.ds(0, known)], osem.at[0])
            ws_cp = pltpu.make_async_copy(ws_in, ws_s, osem.at[1])
            rx_cp = pltpu.make_async_copy(rx_in, racc, osem.at[2])
            pw_cp.start()
            ws_cp.start()
            rx_cp.start()
        for t, (src, lead) in enumerate(images):
            xf[t] = srcs[src][lead].astype(jnp.float32)

        line = lax.broadcasted_iota(jnp.int32, (cols, lanes), 0)
        cell = lax.broadcasted_iota(jnp.int32, (cols, lanes), 1)
        pool = jnp.where(line // LA == cell, 1.0 / (LR * LA), 0.0).astype(jnp.bfloat16)
        sub = lax.broadcasted_iota(jnp.int32, (8, 128), 0)
        masks = {k: (sub % (2 * k)) < k for k in (4, 2, 1)}

        def combine(x, y, k):
            m = masks[k]
            return jnp.where(m, x + pltpu.roll(x, 8 - k, 0), y + pltpu.roll(y, k, 0))

        def fold(parts):
            q = [combine(parts[g], parts[g + 4], 4) for g in range(4)]
            r = [combine(q[0], q[2], 2), combine(q[1], q[3], 2)]
            return combine(r[0], r[1], 1)

        def rows_of(j, comp, g, ct):
            return xf[j, comp, pl.ds(g * LR, LR), pl.ds(ct * 128, 128)]

        def half(v):
            return v[:8] + v[8:]

        def power(j, c):
            for ct in range(ctiles):
                for blk in range(groups // 8):
                    parts = []
                    for g in range(blk * 8, blk * 8 + 8):
                        x0 = rows_of(j, 0, g, ct)
                        x1 = rows_of(j, 1, g, ct)
                        parts.append(half(x0 * x0 + x1 * x1))
                    pacc[j - known, pl.ds(blk * 8, 8), pl.ds(ct * 128, 128)] = fold(parts)
            return c

        lax.fori_loop(known, total, power, 0)
        fresh = total - known
        pw[pl.ds(known, fresh)] = split_pool(pacc[...].reshape(fresh * groups, cols), pool).reshape(
            fresh, groups, lanes
        )
        if known:
            pw_cp.wait()
        else:
            pw_out[...] = pw[...]

        def partner(i, k):
            return jnp.clip(first + i + off_ref[i, k], 0, total - 1)

        def wanted(i, k):
            reach = first + i + off_ref[i, k]
            if known:
                return reach >= known
            return jnp.logical_or(i < dates, reach <= total - 1)

        def pairs(i, c):
            for k in range(NB):
                j = partner(i, k)

                @pl.when(wanted(i, k))
                def _():
                    for ct in range(ctiles):
                        for blk in range(groups // 8):
                            re = []
                            im = []
                            for g in range(blk * 8, blk * 8 + 8):
                                a0 = rows_of(first + i, 0, g, ct)
                                a1 = rows_of(first + i, 1, g, ct)
                                b0 = rows_of(j, 0, g, ct)
                                b1 = rows_of(j, 1, g, ct)
                                re.append(half(a0 * b0 + a1 * b1))
                                im.append(half(a1 * b0 - a0 * b1))
                            racc[i, k, 0, pl.ds(blk * 8, 8), pl.ds(ct * 128, 128)] = fold(re)
                            racc[i, k, 1, pl.ds(blk * 8, 8), pl.ds(ct * 128, 128)] = fold(im)

            return c

        if known:
            rx_cp.wait()
        lax.fori_loop(0, racc.shape[0], pairs, 0)
        if not known:
            racc_x[...] = racc[pl.ds(dates, racc.shape[0] - dates)]
        pooled = split_pool(racc[pl.ds(0, dates)].reshape(dates * NB * 2 * groups, cols), pool)
        pooled = pooled.reshape(dates, NB, 2, groups, lanes)
        ifg_s[...] = pooled[..., :cells]

        def coher(i, ws):
            wr, wi, wc = ws
            pa = pw[first + i]
            for k in range(NB):
                pb = pw[partner(i, k)]
                re = pooled_at(i, k, 0)
                im = pooled_at(i, k, 1)
                co = jnp.sqrt(re * re + im * im) / jnp.sqrt(pa * pb + 1e-06)
                coh_s[i, k] = co[:, :cells]
                wr = wr + co * re
                wi = wi + co * im
                wc = wc + co
            return (wr, wi, wc)

        racc_pooled[...] = pooled

        def pooled_at(i, k, comp):
            return racc_pooled[i, k, comp]

        zero = jnp.zeros((groups, lanes), jnp.float32)
        if known:
            ws_cp.wait()
            start = (ws_s[0], ws_s[1], ws_s[2])
        else:
            start = (zero, zero, zero)
        wr, wi, wc = lax.fori_loop(0, dates, coher, start)
        outs = [
            pltpu.make_async_copy(ifg_s, ifg_ref.at[pl.ds(date0, dates)], osem.at[3]),
            pltpu.make_async_copy(coh_s, coh_ref.at[pl.ds(date0, dates)], osem.at[4]),
        ]
        for cp in outs:
            cp.start()
        if not known:
            last_ref[0] = wr
            last_ref[1] = wi
            last_ref[2] = wc
            for cp in outs:
                cp.wait()
            return
        width = cells // tiles
        lane = lax.broadcasted_iota(jnp.int32, (groups, lanes), 1)
        for t in range(tiles):
            base = t * width
            block = jnp.where(
                lane < width,
                pltpu.roll(wr, (lanes - base) % lanes, 1),
                jnp.where(
                    lane < 2 * width,
                    pltpu.roll(wi, (lanes + width - base) % lanes, 1),
                    jnp.where(lane < 3 * width, pltpu.roll(wc, (lanes + 2 * width - base) % lanes, 1), 0.0),
                ),
            )
            pay[owner_ref[t]] = block
        pay_cp = pltpu.make_async_copy(pay, last_ref, osem.at[5])
        pay_cp.start()
        for cp in outs:
            cp.wait()
        pay_cp.wait()

    return kernel


def local_math(offsets, sources, images, first, dates, count, date0, known=None):
    pair_dates = offsets.shape[0]
    _, _, rows, cols = sources[0].shape
    groups = rows // LR
    cells = cols // LA
    total = len(images)
    lanes = 128
    vmem = pltpu.VMEM
    smem = pltpu.SMEM
    anyspace = pl.BlockSpec(memory_space=pl.ANY)
    hbm = pl.BlockSpec(memory_space=vmem)
    full = [
        jax.ShapeDtypeStruct((count, NB, 2, groups, cells), jnp.float32),
        jax.ShapeDtypeStruct((count, NB, groups, cells), jnp.float32),
    ]
    scratch = [
        pltpu.VMEM((total, 2, rows, cols), jnp.float32),
        None,
        pltpu.VMEM((pair_dates, NB, 2, groups, cols), jnp.float32),
        pltpu.VMEM((total, groups, lanes), jnp.float32),
        pltpu.VMEM((dates, NB, 2, groups, lanes), jnp.float32),
        pltpu.VMEM((dates, NB, 2, groups, cells), jnp.float32),
        pltpu.VMEM((dates, NB, groups, cells), jnp.float32),
    ]
    if known is None:
        nknown, tiles, pw_base = 0, 0, 0
        out_shape = full + [
            jax.ShapeDtypeStruct((3, groups, lanes), jnp.float32),
            jax.ShapeDtypeStruct((total, groups, lanes), jnp.float32),
            jax.ShapeDtypeStruct((pair_dates - dates, NB, 2, groups, cols), jnp.float32),
        ]
        out_specs = [anyspace, anyspace] + [pl.BlockSpec(memory_space=vmem) for _ in range(3)]
        in_specs = [pl.BlockSpec(memory_space=smem)] + [hbm for _ in sources]
        extra = []
        aliases = {}
    else:
        owner, pw_in, ws_in, rx_in, ifg_in, coh_in, pw_base = known
        nknown, tiles = NB, owner.shape[0]
        out_shape = full + [jax.ShapeDtypeStruct((tiles, groups, lanes), jnp.float32)]
        out_specs = [anyspace, anyspace, anyspace]
        in_specs = [pl.BlockSpec(memory_space=smem), pl.BlockSpec(memory_space=smem)] + [
            anyspace for _ in range(5)
        ] + [hbm for _ in sources]
        extra = [owner, pw_in, ws_in, rx_in, ifg_in, coh_in]
        aliases = {5: 0, 6: 1}
        scratch += [pltpu.VMEM((tiles, groups, lanes), jnp.float32), pltpu.VMEM((3, groups, lanes), jnp.float32)]
    scratch[1] = pltpu.VMEM((total - nknown, groups, cols), jnp.float32)
    scratch += [pltpu.SemaphoreType.DMA((6,))]
    return pl.pallas_call(
        make_kernel(images, first, dates, rows, cols, nknown, tiles, date0, pw_base),
        out_shape=tuple(out_shape),
        in_specs=in_specs,
        out_specs=tuple(out_specs),
        scratch_shapes=scratch,
        input_output_aliases=aliases,
        compiler_params=pltpu.CompilerParams(vmem_limit_bytes=48 * 1024 * 1024),
    )(offsets, *extra, *sources)


def on_device(slc, offsets, owner):
    count = slc.shape[0]
    inner = count - NB
    rim = shifted(slc[:NB], "date", -1)
    ifg_a, coh_a, ws_a, pw_a, rx_a = local_math(
        offsets, [slc], [(0, t) for t in range(count)], 0, inner, count, 0
    )
    interferograms, coherence, slotted = local_math(
        offsets[inner:],
        [slc, rim],
        [(0, inner + t) for t in range(NB)] + [(1, t) for t in range(NB)],
        0,
        NB,
        count,
        inner,
        known=(owner, pw_a, ws_a, rx_a, ifg_a, coh_a, inner),
    )
    width = ifg_a.shape[-1] // owner.shape[0]
    sums = lax.all_to_all(slotted, "date", split_axis=0, concat_axis=0, tiled=True).sum(0)
    network_mean = (
        jnp.stack([sums[:, :width], sums[:, width : 2 * width]], 0) / (1.0 + sums[:, 2 * width : 3 * width])
    )[None]
    return (interferograms, coherence, network_mean)


def solution(mesh):
    placed = (P("date", None, "strip", None), P("date", None), P())
    return jax.shard_map(
        on_device,
        mesh=mesh,
        in_specs=placed,
        out_specs=(
            P("date", None, None, "strip", None),
            P("date", None, "strip", None),
            P("date", None, "strip", None),
        ),
        check_vma=False,
    )
```

```python
import jax
import jax.numpy as jnp
from jax import lax
from jax.experimental import pallas as pl
from jax.experimental.pallas import tpu as pltpu
from jax.sharding import PartitionSpec as P

NB = 3
LR = 16
LA = 4


def shifted(value, axis, steps):
    count = lax.axis_size(axis)
    pairs = [(source, (source + steps) % count) for source in range(count)]
    return lax.ppermute(value, axis, pairs)


def split_pool(field, pool):
    hi = field.astype(jnp.bfloat16)
    rest = field - hi.astype(jnp.float32)
    mid = rest.astype(jnp.bfloat16)
    lo = (rest - mid.astype(jnp.float32)).astype(jnp.bfloat16)
    out = jnp.dot(hi, pool, preferred_element_type=jnp.float32)
    out = out + jnp.dot(mid, pool, preferred_element_type=jnp.float32)
    return out + jnp.dot(lo, pool, preferred_element_type=jnp.float32)


def make_kernel(images, first, dates, rows, cols, known, tiles, date0, pw_base):
    groups = rows // LR
    cells = cols // LA
    total = len(images)
    ctiles = cols // 128
    lanes = 128
    nsrc = len(set(src for src, _ in images))

    def kernel(*refs):
        off_ref = refs[0]
        if known:
            owner_ref, pw_in, ws_in, rx_in = refs[1:5]
            srcs = refs[7 : 7 + nsrc]
            rest = refs[7 + nsrc :]
            ifg_ref, coh_ref, last_ref = rest[:3]
            xf, pacc, racc, pw, racc_pooled, ifg_s, coh_s, pay, ws_s, osem = rest[3:]
        else:
            srcs = refs[1 : 1 + nsrc]
            rest = refs[1 + nsrc :]
            ifg_ref, coh_ref, last_ref, pw_out, racc_x = rest[:5]
            xf, pacc, racc, pw, racc_pooled, ifg_s, coh_s, osem = rest[5:]
        if known:
            pw_cp = pltpu.make_async_copy(pw_in.at[pl.ds(pw_base, known)], pw.at[pl.ds(0, known)], osem.at[0])
            ws_cp = pltpu.make_async_copy(ws_in, ws_s, osem.at[1])
            rx_cp = pltpu.make_async_copy(rx_in, racc, osem.at[2])
            pw_cp.start()
            ws_cp.start()
            rx_cp.start()
        for t, (src, lead) in enumerate(images):
            xf[t] = srcs[src][lead].astype(jnp.float32)

        line = lax.broadcasted_iota(jnp.int32, (cols, lanes), 0)
        cell = lax.broadcasted_iota(jnp.int32, (cols, lanes), 1)
        pool = jnp.where(line // LA == cell, 1.0 / (LR * LA), 0.0).astype(jnp.bfloat16)
        sub = lax.broadcasted_iota(jnp.int32, (8, 128), 0)
        masks = {k: (sub % (2 * k)) < k for k in (4, 2, 1)}

        def combine(x, y, k):
            m = masks[k]
            return jnp.where(m, x + pltpu.roll(x, 8 - k, 0), y + pltpu.roll(y, k, 0))

        def fold(parts):
            q = [combine(parts[g], parts[g + 4], 4) for g in range(4)]
            r = [combine(q[0], q[2], 2), combine(q[1], q[3], 2)]
            return combine(r[0], r[1], 1)

        def rows_of(j, comp, g, ct):
            return xf[j, comp, pl.ds(g * LR, LR), pl.ds(ct * 128, 128)]

        def half(v):
            return v[:8] + v[8:]

        def power(j, c):
            for ct in range(ctiles):
                for blk in range(groups // 8):
                    parts = []
                    for g in range(blk * 8, blk * 8 + 8):
                        x0 = rows_of(j, 0, g, ct)
                        x1 = rows_of(j, 1, g, ct)
                        parts.append(half(x0 * x0 + x1 * x1))
                    pacc[j - known, pl.ds(blk * 8, 8), pl.ds(ct * 128, 128)] = fold(parts)
            return c

        lax.fori_loop(known, total, power, 0)
        fresh = total - known
        pw[pl.ds(known, fresh)] = split_pool(pacc[...].reshape(fresh * groups, cols), pool).reshape(
            fresh, groups, lanes
        )
        if known:
            pw_cp.wait()
        else:
            pw_out[...] = pw[...]

        def partner(i, k):
            return jnp.clip(first + i + off_ref[i, k], 0, total - 1)

        def wanted(i, k):
            reach = first + i + off_ref[i, k]
            if known:
                return reach >= known
            return jnp.logical_or(i < dates, reach <= total - 1)

        def pairs(i, c):
            for k in range(NB):
                j = partner(i, k)

                @pl.when(wanted(i, k))
                def _():
                    for ct in range(ctiles):
                        for blk in range(groups // 8):
                            re = []
                            im = []
                            for g in range(blk * 8, blk * 8 + 8):
                                a0 = rows_of(first + i, 0, g, ct)
                                a1 = rows_of(first + i, 1, g, ct)
                                b0 = rows_of(j, 0, g, ct)
                                b1 = rows_of(j, 1, g, ct)
                                re.append(half(a0 * b0 + a1 * b1))
                                im.append(half(a1 * b0 - a0 * b1))
                            racc[i, k, 0, pl.ds(blk * 8, 8), pl.ds(ct * 128, 128)] = fold(re)
                            racc[i, k, 1, pl.ds(blk * 8, 8), pl.ds(ct * 128, 128)] = fold(im)

            return c

        if known:
            rx_cp.wait()
        lax.fori_loop(0, racc.shape[0], pairs, 0)
        if not known:
            racc_x[...] = racc[pl.ds(dates, racc.shape[0] - dates)]
        pooled = split_pool(racc[pl.ds(0, dates)].reshape(dates * NB * 2 * groups, cols), pool)
        pooled = pooled.reshape(dates, NB, 2, groups, lanes)
        ifg_s[...] = pooled[..., :cells]

        def coher(i, ws):
            wr, wi, wc = ws
            pa = pw[first + i]
            for k in range(NB):
                pb = pw[partner(i, k)]
                re = pooled_at(i, k, 0)
                im = pooled_at(i, k, 1)
                co = jnp.sqrt(re * re + im * im) / jnp.sqrt(pa * pb + 1e-06)
                coh_s[i, k] = co[:, :cells]
                wr = wr + co * re
                wi = wi + co * im
                wc = wc + co
            return (wr, wi, wc)

        racc_pooled[...] = pooled

        def pooled_at(i, k, comp):
            return racc_pooled[i, k, comp]

        zero = jnp.zeros((groups, lanes), jnp.float32)
        if known:
            ws_cp.wait()
            start = (ws_s[0], ws_s[1], ws_s[2])
        else:
            start = (zero, zero, zero)
        wr, wi, wc = lax.fori_loop(0, dates, coher, start)
        outs = [
            pltpu.make_async_copy(ifg_s, ifg_ref.at[pl.ds(date0, dates)], osem.at[3]),
            pltpu.make_async_copy(coh_s, coh_ref.at[pl.ds(date0, dates)], osem.at[4]),
        ]
        for cp in outs:
            cp.start()
        if not known:
            last_ref[0] = wr
            last_ref[1] = wi
            last_ref[2] = wc
            for cp in outs:
                cp.wait()
            return
        width = cells // tiles
        lane = lax.broadcasted_iota(jnp.int32, (8, lanes), 1)
        sums = (wr, wi, wc)
        for t in range(tiles):
            base = t * width
            block = jnp.zeros((8, lanes), jnp.float32)
            for h in range(groups // 8):
                for f in range(3):
                    at = (h * 3 + f) * width
                    moved = pltpu.roll(sums[f][h * 8 : h * 8 + 8], (lanes + at - base) % lanes, 1)
                    block = jnp.where((lane >= at) & (lane < at + width), moved, block)
            pay[owner_ref[t]] = block
        pay_cp = pltpu.make_async_copy(pay, last_ref, osem.at[5])
        pay_cp.start()
        for cp in outs:
            cp.wait()
        pay_cp.wait()

    return kernel


def local_math(offsets, sources, images, first, dates, count, date0, known=None):
    pair_dates = offsets.shape[0]
    _, _, rows, cols = sources[0].shape
    groups = rows // LR
    cells = cols // LA
    total = len(images)
    lanes = 128
    vmem = pltpu.VMEM
    smem = pltpu.SMEM
    anyspace = pl.BlockSpec(memory_space=pl.ANY)
    hbm = pl.BlockSpec(memory_space=vmem)
    full = [
        jax.ShapeDtypeStruct((count, NB, 2, groups, cells), jnp.float32),
        jax.ShapeDtypeStruct((count, NB, groups, cells), jnp.float32),
    ]
    scratch = [
        pltpu.VMEM((total, 2, rows, cols), jnp.float32),
        None,
        pltpu.VMEM((pair_dates, NB, 2, groups, cols), jnp.float32),
        pltpu.VMEM((total, groups, lanes), jnp.float32),
        pltpu.VMEM((dates, NB, 2, groups, lanes), jnp.float32),
        pltpu.VMEM((dates, NB, 2, groups, cells), jnp.float32),
        pltpu.VMEM((dates, NB, groups, cells), jnp.float32),
    ]
    if known is None:
        nknown, tiles, pw_base = 0, 0, 0
        out_shape = full + [
            jax.ShapeDtypeStruct((3, groups, lanes), jnp.float32),
            jax.ShapeDtypeStruct((total, groups, lanes), jnp.float32),
            jax.ShapeDtypeStruct((pair_dates - dates, NB, 2, groups, cols), jnp.float32),
        ]
        out_specs = [anyspace, anyspace] + [pl.BlockSpec(memory_space=vmem) for _ in range(3)]
        in_specs = [pl.BlockSpec(memory_space=smem)] + [hbm for _ in sources]
        extra = []
        aliases = {}
    else:
        owner, pw_in, ws_in, rx_in, ifg_in, coh_in, pw_base = known
        nknown, tiles = NB, owner.shape[0]
        out_shape = full + [jax.ShapeDtypeStruct((tiles, 8, lanes), jnp.float32)]
        out_specs = [anyspace, anyspace, anyspace]
        in_specs = [pl.BlockSpec(memory_space=smem), pl.BlockSpec(memory_space=smem)] + [
            anyspace for _ in range(5)
        ] + [hbm for _ in sources]
        extra = [owner, pw_in, ws_in, rx_in, ifg_in, coh_in]
        aliases = {5: 0, 6: 1}
        scratch += [pltpu.VMEM((tiles, 8, lanes), jnp.float32), pltpu.VMEM((3, groups, lanes), jnp.float32)]
    scratch[1] = pltpu.VMEM((total - nknown, groups, cols), jnp.float32)
    scratch += [pltpu.SemaphoreType.DMA((6,))]
    return pl.pallas_call(
        make_kernel(images, first, dates, rows, cols, nknown, tiles, date0, pw_base),
        out_shape=tuple(out_shape),
        in_specs=in_specs,
        out_specs=tuple(out_specs),
        scratch_shapes=scratch,
        input_output_aliases=aliases,
        compiler_params=pltpu.CompilerParams(vmem_limit_bytes=48 * 1024 * 1024),
    )(offsets, *extra, *sources)


def on_device(slc, offsets, owner):
    count = slc.shape[0]
    inner = count - NB
    rim = shifted(slc[:NB], "date", -1)
    ifg_a, coh_a, ws_a, pw_a, rx_a = local_math(
        offsets, [slc], [(0, t) for t in range(count)], 0, inner, count, 0
    )
    interferograms, coherence, slotted = local_math(
        offsets[inner:],
        [slc, rim],
        [(0, inner + t) for t in range(NB)] + [(1, t) for t in range(NB)],
        0,
        NB,
        count,
        inner,
        known=(owner, pw_a, ws_a, rx_a, ifg_a, coh_a, inner),
    )
    width = ifg_a.shape[-1] // owner.shape[0]
    sums = lax.all_to_all(slotted, "date", split_axis=0, concat_axis=0, tiled=True).sum(0)
    halves = ifg_a.shape[3] // 8

    def field(f):
        return jnp.concatenate(
            [sums[:, (h * 3 + f) * width : (h * 3 + f + 1) * width] for h in range(halves)], 0
        )

    network_mean = (jnp.stack([field(0), field(1)], 0) / (1.0 + field(2)))[None]
    return (interferograms, coherence, network_mean)


def solution(mesh):
    placed = (P("date", None, "strip", None), P("date", None), P())
    return jax.shard_map(
        on_device,
        mesh=mesh,
        in_specs=placed,
        out_specs=(
            P("date", None, None, "strip", None),
            P("date", None, "strip", None),
            P("date", None, "strip", None),
        ),
        check_vma=False,
    )
```

```python
import jax
import jax.numpy as jnp
from jax import lax
from jax.experimental import pallas as pl
from jax.experimental.pallas import tpu as pltpu
from jax.sharding import PartitionSpec as P

NB = 3
LR = 16
LA = 4
SLOT = 4


def shifted(value, axis, steps):
    count = lax.axis_size(axis)
    pairs = [(source, (source + steps) % count) for source in range(count)]
    return lax.ppermute(value, axis, pairs)


def split_pool(field, pool):
    hi = field.astype(jnp.bfloat16)
    rest = field - hi.astype(jnp.float32)
    mid = rest.astype(jnp.bfloat16)
    lo = (rest - mid.astype(jnp.float32)).astype(jnp.bfloat16)
    out = jnp.dot(hi, pool, preferred_element_type=jnp.float32)
    out = out + jnp.dot(mid, pool, preferred_element_type=jnp.float32)
    return out + jnp.dot(lo, pool, preferred_element_type=jnp.float32)


def make_kernel(images, first, dates, rows, cols, known, tiles, date0, pw_base):
    groups = rows // LR
    cells = cols // LA
    total = len(images)
    ctiles = cols // 128
    lanes = 128
    nsrc = len(set(src for src, _ in images))

    def kernel(*refs):
        off_ref = refs[0]
        if known:
            owner_ref, pw_in, ws_in, rx_in = refs[1:5]
            srcs = refs[7 : 7 + nsrc]
            rest = refs[7 + nsrc :]
            ifg_ref, coh_ref, last_ref = rest[:3]
            xf, pacc, racc, pw, racc_pooled, ifg_s, coh_s, pay, ws_s, osem = rest[3:]
        else:
            srcs = refs[1 : 1 + nsrc]
            rest = refs[1 + nsrc :]
            ifg_ref, coh_ref, last_ref, pw_out, racc_x = rest[:5]
            xf, pacc, racc, pw, racc_pooled, ifg_s, coh_s, osem = rest[5:]
        if known:
            pw_cp = pltpu.make_async_copy(pw_in.at[pl.ds(pw_base, known)], pw.at[pl.ds(0, known)], osem.at[0])
            ws_cp = pltpu.make_async_copy(ws_in, ws_s, osem.at[1])
            rx_cp = pltpu.make_async_copy(rx_in, racc, osem.at[2])
            pw_cp.start()
            ws_cp.start()
            rx_cp.start()
        for t, (src, lead) in enumerate(images):
            xf[t] = srcs[src][lead].astype(jnp.float32)

        line = lax.broadcasted_iota(jnp.int32, (cols, lanes), 0)
        cell = lax.broadcasted_iota(jnp.int32, (cols, lanes), 1)
        pool = jnp.where(line // LA == cell, 1.0 / (LR * LA), 0.0).astype(jnp.bfloat16)
        sub = lax.broadcasted_iota(jnp.int32, (8, 128), 0)
        masks = {k: (sub % (2 * k)) < k for k in (4, 2, 1)}

        def combine(x, y, k):
            m = masks[k]
            return jnp.where(m, x + pltpu.roll(x, 8 - k, 0), y + pltpu.roll(y, k, 0))

        def fold(parts):
            q = [combine(parts[g], parts[g + 4], 4) for g in range(4)]
            r = [combine(q[0], q[2], 2), combine(q[1], q[3], 2)]
            return combine(r[0], r[1], 1)

        def rows_of(j, comp, g, ct):
            return xf[j, comp, pl.ds(g * LR, LR), pl.ds(ct * 128, 128)]

        def half(v):
            return v[:8] + v[8:]

        def power(j, c):
            for ct in range(ctiles):
                for blk in range(groups // 8):
                    parts = []
                    for g in range(blk * 8, blk * 8 + 8):
                        x0 = rows_of(j, 0, g, ct)
                        x1 = rows_of(j, 1, g, ct)
                        parts.append(half(x0 * x0 + x1 * x1))
                    pacc[j - known, pl.ds(blk * 8, 8), pl.ds(ct * 128, 128)] = fold(parts)
            return c

        lax.fori_loop(known, total, power, 0)
        fresh = total - known
        pw[pl.ds(known, fresh)] = split_pool(pacc[...].reshape(fresh * groups, cols), pool).reshape(
            fresh, groups, lanes
        )
        if known:
            pw_cp.wait()
        else:
            pw_out[...] = pw[...]

        def partner(i, k):
            return jnp.clip(first + i + off_ref[i, k], 0, total - 1)

        def wanted(i, k):
            reach = first + i + off_ref[i, k]
            if known:
                return reach >= known
            return jnp.logical_or(i < dates, reach <= total - 1)

        def pairs(i, c):
            for k in range(NB):
                j = partner(i, k)

                @pl.when(wanted(i, k))
                def _():
                    for ct in range(ctiles):
                        for blk in range(groups // 8):
                            re = []
                            im = []
                            for g in range(blk * 8, blk * 8 + 8):
                                a0 = rows_of(first + i, 0, g, ct)
                                a1 = rows_of(first + i, 1, g, ct)
                                b0 = rows_of(j, 0, g, ct)
                                b1 = rows_of(j, 1, g, ct)
                                re.append(half(a0 * b0 + a1 * b1))
                                im.append(half(a1 * b0 - a0 * b1))
                            racc[i, k, 0, pl.ds(blk * 8, 8), pl.ds(ct * 128, 128)] = fold(re)
                            racc[i, k, 1, pl.ds(blk * 8, 8), pl.ds(ct * 128, 128)] = fold(im)

            return c

        if known:
            rx_cp.wait()
        lax.fori_loop(0, racc.shape[0], pairs, 0)
        if not known:
            racc_x[...] = racc[pl.ds(dates, racc.shape[0] - dates)]
        pooled = split_pool(racc[pl.ds(0, dates)].reshape(dates * NB * 2 * groups, cols), pool)
        pooled = pooled.reshape(dates, NB, 2, groups, lanes)
        ifg_s[...] = pooled[..., :cells]

        def coher(i, ws):
            wr, wi, wc = ws
            pa = pw[first + i]
            for k in range(NB):
                pb = pw[partner(i, k)]
                re = pooled_at(i, k, 0)
                im = pooled_at(i, k, 1)
                co = jnp.sqrt(re * re + im * im) / jnp.sqrt(pa * pb + 1e-06)
                coh_s[i, k] = co[:, :cells]
                wr = wr + co * re
                wi = wi + co * im
                wc = wc + co
            return (wr, wi, wc)

        racc_pooled[...] = pooled

        def pooled_at(i, k, comp):
            return racc_pooled[i, k, comp]

        zero = jnp.zeros((groups, lanes), jnp.float32)
        if known:
            ws_cp.wait()
            start = (ws_s[0], ws_s[1], ws_s[2])
        else:
            start = (zero, zero, zero)
        wr, wi, wc = lax.fori_loop(0, dates, coher, start)
        outs = [
            pltpu.make_async_copy(ifg_s, ifg_ref.at[pl.ds(date0, dates)], osem.at[3]),
            pltpu.make_async_copy(coh_s, coh_ref.at[pl.ds(date0, dates)], osem.at[4]),
        ]
        for cp in outs:
            cp.start()
        if not known:
            last_ref[0] = wr
            last_ref[1] = wi
            last_ref[2] = wc
            for cp in outs:
                cp.wait()
            return
        width = cells // tiles
        lane = lax.broadcasted_iota(jnp.int32, (SLOT, lanes), 1)
        sums = (wr, wi, wc)
        for t in range(tiles):
            base = t * width
            block = jnp.zeros((SLOT, lanes), jnp.float32)
            for h in range(groups // SLOT):
                for f in range(3):
                    at = (h * 3 + f) * width
                    moved = pltpu.roll(sums[f][h * SLOT : h * SLOT + SLOT], (lanes + at - base) % lanes, 1)
                    block = jnp.where((lane >= at) & (lane < at + width), moved, block)
            pay[owner_ref[t]] = block
        pay_cp = pltpu.make_async_copy(pay, last_ref, osem.at[5])
        pay_cp.start()
        for cp in outs:
            cp.wait()
        pay_cp.wait()

    return kernel


def local_math(offsets, sources, images, first, dates, count, date0, known=None):
    pair_dates = offsets.shape[0]
    _, _, rows, cols = sources[0].shape
    groups = rows // LR
    cells = cols // LA
    total = len(images)
    lanes = 128
    vmem = pltpu.VMEM
    smem = pltpu.SMEM
    anyspace = pl.BlockSpec(memory_space=pl.ANY)
    hbm = pl.BlockSpec(memory_space=vmem)
    full = [
        jax.ShapeDtypeStruct((count, NB, 2, groups, cells), jnp.float32),
        jax.ShapeDtypeStruct((count, NB, groups, cells), jnp.float32),
    ]
    scratch = [
        pltpu.VMEM((total, 2, rows, cols), jnp.float32),
        None,
        pltpu.VMEM((pair_dates, NB, 2, groups, cols), jnp.float32),
        pltpu.VMEM((total, groups, lanes), jnp.float32),
        pltpu.VMEM((dates, NB, 2, groups, lanes), jnp.float32),
        pltpu.VMEM((dates, NB, 2, groups, cells), jnp.float32),
        pltpu.VMEM((dates, NB, groups, cells), jnp.float32),
    ]
    if known is None:
        nknown, tiles, pw_base = 0, 0, 0
        out_shape = full + [
            jax.ShapeDtypeStruct((3, groups, lanes), jnp.float32),
            jax.ShapeDtypeStruct((total, groups, lanes), jnp.float32),
            jax.ShapeDtypeStruct((pair_dates - dates, NB, 2, groups, cols), jnp.float32),
        ]
        out_specs = [anyspace, anyspace] + [pl.BlockSpec(memory_space=vmem) for _ in range(3)]
        in_specs = [pl.BlockSpec(memory_space=smem)] + [hbm for _ in sources]
        extra = []
        aliases = {}
    else:
        owner, pw_in, ws_in, rx_in, ifg_in, coh_in, pw_base = known
        nknown, tiles = NB, owner.shape[0]
        out_shape = full + [jax.ShapeDtypeStruct((tiles, SLOT, lanes), jnp.float32)]
        out_specs = [anyspace, anyspace, anyspace]
        in_specs = [pl.BlockSpec(memory_space=smem), pl.BlockSpec(memory_space=smem)] + [
            anyspace for _ in range(5)
        ] + [hbm for _ in sources]
        extra = [owner, pw_in, ws_in, rx_in, ifg_in, coh_in]
        aliases = {5: 0, 6: 1}
        scratch += [pltpu.VMEM((tiles, SLOT, lanes), jnp.float32), pltpu.VMEM((3, groups, lanes), jnp.float32)]
    scratch[1] = pltpu.VMEM((total - nknown, groups, cols), jnp.float32)
    scratch += [pltpu.SemaphoreType.DMA((6,))]
    return pl.pallas_call(
        make_kernel(images, first, dates, rows, cols, nknown, tiles, date0, pw_base),
        out_shape=tuple(out_shape),
        in_specs=in_specs,
        out_specs=tuple(out_specs),
        scratch_shapes=scratch,
        input_output_aliases=aliases,
        compiler_params=pltpu.CompilerParams(vmem_limit_bytes=48 * 1024 * 1024),
    )(offsets, *extra, *sources)


def on_device(slc, offsets, owner):
    count = slc.shape[0]
    inner = count - NB
    rim = shifted(slc[:NB], "date", -1)
    ifg_a, coh_a, ws_a, pw_a, rx_a = local_math(
        offsets, [slc], [(0, t) for t in range(count)], 0, inner, count, 0
    )
    interferograms, coherence, slotted = local_math(
        offsets[inner:],
        [slc, rim],
        [(0, inner + t) for t in range(NB)] + [(1, t) for t in range(NB)],
        0,
        NB,
        count,
        inner,
        known=(owner, pw_a, ws_a, rx_a, ifg_a, coh_a, inner),
    )
    width = ifg_a.shape[-1] // owner.shape[0]
    sums = lax.all_to_all(slotted, "date", split_axis=0, concat_axis=0, tiled=True).sum(0)
    halves = ifg_a.shape[3] // SLOT

    def field(f):
        return jnp.concatenate(
            [sums[:, (h * 3 + f) * width : (h * 3 + f + 1) * width] for h in range(halves)], 0
        )

    network_mean = (jnp.stack([field(0), field(1)], 0) / (1.0 + field(2)))[None]
    return (interferograms, coherence, network_mean)


def solution(mesh):
    placed = (P("date", None, "strip", None), P("date", None), P())
    return jax.shard_map(
        on_device,
        mesh=mesh,
        in_specs=placed,
        out_specs=(
            P("date", None, None, "strip", None),
            P("date", None, "strip", None),
            P("date", None, "strip", None),
        ),
        check_vma=False,
    )
```

```python
import jax
import jax.numpy as jnp
from jax import lax
from jax.experimental import pallas as pl
from jax.experimental.pallas import tpu as pltpu
from jax.sharding import PartitionSpec as P

NB = 3
LR = 16
LA = 4
SLOT = 4


def shifted(value, axis, steps):
    count = lax.axis_size(axis)
    pairs = [(source, (source + steps) % count) for source in range(count)]
    return lax.ppermute(value, axis, pairs)


def split_pool(field, pool):
    hi = field.astype(jnp.bfloat16)
    rest = field - hi.astype(jnp.float32)
    mid = rest.astype(jnp.bfloat16)
    lo = (rest - mid.astype(jnp.float32)).astype(jnp.bfloat16)
    out = jnp.dot(hi, pool, preferred_element_type=jnp.float32)
    out = out + jnp.dot(mid, pool, preferred_element_type=jnp.float32)
    return out + jnp.dot(lo, pool, preferred_element_type=jnp.float32)


def make_kernel(images, first, dates, rows, cols, known, tiles, date0, pw_base):
    groups = rows // LR
    cells = cols // LA
    total = len(images)
    ctiles = cols // 128
    lanes = 128
    nsrc = len(set(src for src, _ in images))

    def kernel(*refs):
        off_ref = refs[0]
        if known:
            owner_ref, pw_in, ws_in, rx_in = refs[1:5]
            srcs = refs[7 : 7 + nsrc]
            rest = refs[7 + nsrc :]
            ifg_ref, coh_ref, last_ref = rest[:3]
            xf, pacc, racc, pw, racc_pooled, ifg_s, coh_s, pay, ws_s, osem = rest[3:]
        else:
            srcs = refs[1 : 1 + nsrc]
            rest = refs[1 + nsrc :]
            ifg_ref, coh_ref, last_ref, pw_out, racc_x = rest[:5]
            xf, pacc, racc, pw, racc_pooled, ifg_s, coh_s, osem = rest[5:]
        if known:
            pw_cp = pltpu.make_async_copy(pw_in.at[pl.ds(pw_base, known)], pw.at[pl.ds(0, known)], osem.at[0])
            ws_cp = pltpu.make_async_copy(ws_in, ws_s, osem.at[1])
            rx_cp = pltpu.make_async_copy(rx_in, racc, osem.at[2])
            pw_cp.start()
            ws_cp.start()
            rx_cp.start()
        for t, (src, lead) in enumerate(images):
            xf[t] = srcs[src][lead].astype(jnp.float32)

        line = lax.broadcasted_iota(jnp.int32, (cols, lanes), 0)
        cell = lax.broadcasted_iota(jnp.int32, (cols, lanes), 1)
        pool = jnp.where(line // LA == cell, 1.0 / (LR * LA), 0.0).astype(jnp.bfloat16)
        sub = lax.broadcasted_iota(jnp.int32, (8, 128), 0)
        masks = {k: (sub % (2 * k)) < k for k in (4, 2, 1)}

        def combine(x, y, k):
            m = masks[k]
            return jnp.where(m, x + pltpu.roll(x, 8 - k, 0), y + pltpu.roll(y, k, 0))

        def fold(parts):
            q = [combine(parts[g], parts[g + 4], 4) for g in range(4)]
            r = [combine(q[0], q[2], 2), combine(q[1], q[3], 2)]
            return combine(r[0], r[1], 1)

        def rows_of(j, comp, g, ct):
            return xf[j, comp, pl.ds(g * LR, LR), pl.ds(ct * 128, 128)]

        def half(v):
            return v[:8] + v[8:]

        def power(j, c):
            for ct in range(ctiles):
                for blk in range(groups // 8):
                    parts = []
                    for g in range(blk * 8, blk * 8 + 8):
                        x0 = rows_of(j, 0, g, ct)
                        x1 = rows_of(j, 1, g, ct)
                        parts.append(half(x0 * x0 + x1 * x1))
                    pacc[j - known, pl.ds(blk * 8, 8), pl.ds(ct * 128, 128)] = fold(parts)
            return c

        lax.fori_loop(known, total, power, 0)
        fresh = total - known
        pw[pl.ds(known, fresh)] = split_pool(pacc[...].reshape(fresh * groups, cols), pool).reshape(
            fresh, groups, lanes
        )
        if known:
            pw_cp.wait()
        else:
            pw_out[...] = pw[...]

        def partner(i, k):
            return jnp.clip(first + i + off_ref[i, k], 0, total - 1)

        def wanted(i, k):
            reach = first + i + off_ref[i, k]
            if known:
                return reach >= known
            return jnp.logical_or(i < dates, reach <= total - 1)

        def pairs(i, c):
            for k in range(NB):
                j = partner(i, k)

                @pl.when(wanted(i, k))
                def _():
                    for ct in range(ctiles):
                        for blk in range(groups // 8):
                            re = []
                            im = []
                            for g in range(blk * 8, blk * 8 + 8):
                                a0 = rows_of(first + i, 0, g, ct)
                                a1 = rows_of(first + i, 1, g, ct)
                                b0 = rows_of(j, 0, g, ct)
                                b1 = rows_of(j, 1, g, ct)
                                re.append(half(a0 * b0 + a1 * b1))
                                im.append(half(a1 * b0 - a0 * b1))
                            racc[i, k, 0, pl.ds(blk * 8, 8), pl.ds(ct * 128, 128)] = fold(re)
                            racc[i, k, 1, pl.ds(blk * 8, 8), pl.ds(ct * 128, 128)] = fold(im)

            return c

        if known:
            rx_cp.wait()
        lax.fori_loop(0, racc.shape[0], pairs, 0)
        if not known:
            racc_x[...] = racc[pl.ds(dates, racc.shape[0] - dates)]
        pooled = split_pool(racc[pl.ds(0, dates)].reshape(dates * NB * 2 * groups, cols), pool)
        pooled = pooled.reshape(dates, NB, 2, groups, lanes)
        ifg_s[...] = pooled[..., :cells]

        def coher(i, ws):
            wr, wi, wc = ws
            pa = pw[first + i]
            for k in range(NB):
                pb = pw[partner(i, k)]
                re = pooled_at(i, k, 0)
                im = pooled_at(i, k, 1)
                co = jnp.sqrt(re * re + im * im) / jnp.sqrt(pa * pb + 1e-06)
                coh_s[i, k] = co[:, :cells]
                wr = wr + co * re
                wi = wi + co * im
                wc = wc + co
            return (wr, wi, wc)

        racc_pooled[...] = pooled

        def pooled_at(i, k, comp):
            return racc_pooled[i, k, comp]

        zero = jnp.zeros((groups, lanes), jnp.float32)
        if known:
            ws_cp.wait()
            start = (ws_s[0], ws_s[1], ws_s[2])
        else:
            start = (zero, zero, zero)
        wr, wi, wc = lax.fori_loop(0, dates, coher, start)
        outs = [
            pltpu.make_async_copy(ifg_s, ifg_ref.at[pl.ds(date0, dates)], osem.at[3]),
            pltpu.make_async_copy(coh_s, coh_ref.at[pl.ds(date0, dates)], osem.at[4]),
        ]
        for cp in outs:
            cp.start()
        if not known:
            last_ref[0] = wr
            last_ref[1] = wi
            last_ref[2] = wc
            for cp in outs:
                cp.wait()
            return
        width = cells // tiles
        lane = lax.broadcasted_iota(jnp.int32, (SLOT, lanes), 1)
        sums = (wr, wi, wc)
        for t in range(tiles):
            base = t * width
            block = jnp.zeros((SLOT, lanes), jnp.float32)
            for h in range(groups // SLOT):
                for f in range(3):
                    at = (h * 3 + f) * width
                    moved = pltpu.roll(sums[f][h * SLOT : h * SLOT + SLOT], (lanes + at - base) % lanes, 1)
                    block = jnp.where((lane >= at) & (lane < at + width), moved, block)
            pay[owner_ref[t]] = block
        pay_cp = pltpu.make_async_copy(pay, last_ref, osem.at[5])
        pay_cp.start()
        for cp in outs:
            cp.wait()
        pay_cp.wait()

    return kernel


def local_math(offsets, sources, images, first, dates, count, date0, known=None):
    pair_dates = offsets.shape[0]
    _, _, rows, cols = sources[0].shape
    groups = rows // LR
    cells = cols // LA
    total = len(images)
    lanes = 128
    vmem = pltpu.VMEM
    smem = pltpu.SMEM
    anyspace = pl.BlockSpec(memory_space=pl.ANY)
    hbm = pl.BlockSpec(memory_space=vmem)
    full = [
        jax.ShapeDtypeStruct((count, NB, 2, groups, cells), jnp.float32),
        jax.ShapeDtypeStruct((count, NB, groups, cells), jnp.float32),
    ]
    scratch = [
        pltpu.VMEM((total, 2, rows, cols), jnp.float32),
        None,
        pltpu.VMEM((pair_dates, NB, 2, groups, cols), jnp.float32),
        pltpu.VMEM((total, groups, lanes), jnp.float32),
        pltpu.VMEM((dates, NB, 2, groups, lanes), jnp.float32),
        pltpu.VMEM((dates, NB, 2, groups, cells), jnp.float32),
        pltpu.VMEM((dates, NB, groups, cells), jnp.float32),
    ]
    if known is None:
        nknown, tiles, pw_base = 0, 0, 0
        out_shape = full + [
            jax.ShapeDtypeStruct((3, groups, lanes), jnp.float32),
            jax.ShapeDtypeStruct((total, groups, lanes), jnp.float32),
            jax.ShapeDtypeStruct((pair_dates - dates, NB, 2, groups, cols), jnp.float32),
        ]
        out_specs = [anyspace, anyspace] + [pl.BlockSpec(memory_space=vmem) for _ in range(3)]
        in_specs = [pl.BlockSpec(memory_space=smem)] + [hbm for _ in sources]
        extra = []
        aliases = {}
    else:
        owner, pw_in, ws_in, rx_in, ifg_in, coh_in, pw_base = known
        nknown, tiles = pw_in.shape[0], owner.shape[0]
        out_shape = full + [jax.ShapeDtypeStruct((tiles, SLOT, lanes), jnp.float32)]
        out_specs = [anyspace, anyspace, anyspace]
        in_specs = [pl.BlockSpec(memory_space=smem), pl.BlockSpec(memory_space=smem)] + [
            anyspace for _ in range(5)
        ] + [hbm for _ in sources]
        extra = [owner, pw_in, ws_in, rx_in, ifg_in, coh_in]
        aliases = {5: 0, 6: 1}
        scratch += [pltpu.VMEM((tiles, SLOT, lanes), jnp.float32), pltpu.VMEM((3, groups, lanes), jnp.float32)]
    scratch[1] = pltpu.VMEM((total - nknown, groups, cols), jnp.float32)
    scratch += [pltpu.SemaphoreType.DMA((6,))]
    return pl.pallas_call(
        make_kernel(images, first, dates, rows, cols, nknown, tiles, date0, pw_base),
        out_shape=tuple(out_shape),
        in_specs=in_specs,
        out_specs=tuple(out_specs),
        scratch_shapes=scratch,
        input_output_aliases=aliases,
        compiler_params=pltpu.CompilerParams(vmem_limit_bytes=48 * 1024 * 1024),
    )(offsets, *extra, *sources)


def rim_step(offsets, racc_in, slc, rim, step, inner):
    _, _, rows, cols = slc.shape
    groups = rows // LR
    ctiles = cols // 128
    lanes = 128
    own = slc.shape[0] - inner

    def kernel(off_ref, slc_ref, rim_ref, racc_in_ref, racc_ref, pw_ref, xf, pacc):
        for t in range(own):
            xf[t] = slc_ref[inner + t].astype(jnp.float32)
        xf[own] = rim_ref[0].astype(jnp.float32)
        line = lax.broadcasted_iota(jnp.int32, (cols, lanes), 0)
        cell = lax.broadcasted_iota(jnp.int32, (cols, lanes), 1)
        pool = jnp.where(line // LA == cell, 1.0 / (LR * LA), 0.0).astype(jnp.bfloat16)
        sub = lax.broadcasted_iota(jnp.int32, (8, 128), 0)
        masks = {k: (sub % (2 * k)) < k for k in (4, 2, 1)}

        def combine(x, y, k):
            m = masks[k]
            return jnp.where(m, x + pltpu.roll(x, 8 - k, 0), y + pltpu.roll(y, k, 0))

        def fold(parts):
            q = [combine(parts[g], parts[g + 4], 4) for g in range(4)]
            r = [combine(q[0], q[2], 2), combine(q[1], q[3], 2)]
            return combine(r[0], r[1], 1)

        def rows_of(j, comp, g, ct):
            return xf[j, comp, pl.ds(g * LR, LR), pl.ds(ct * 128, 128)]

        def half(v):
            return v[:8] + v[8:]

        for ct in range(ctiles):
            for blk in range(groups // 8):
                parts = []
                for g in range(blk * 8, blk * 8 + 8):
                    x0 = rows_of(own, 0, g, ct)
                    x1 = rows_of(own, 1, g, ct)
                    parts.append(half(x0 * x0 + x1 * x1))
                pacc[pl.ds(blk * 8, 8), pl.ds(ct * 128, 128)] = fold(parts)
        pw_ref[0] = split_pool(pacc[...], pool)

        def pairs(i, c):
            for k in range(NB):

                @pl.when(i + off_ref[i, k] == own + step)
                def _():
                    for ct in range(ctiles):
                        for blk in range(groups // 8):
                            re = []
                            im = []
                            for g in range(blk * 8, blk * 8 + 8):
                                a0 = rows_of(i, 0, g, ct)
                                a1 = rows_of(i, 1, g, ct)
                                b0 = rows_of(own, 0, g, ct)
                                b1 = rows_of(own, 1, g, ct)
                                re.append(half(a0 * b0 + a1 * b1))
                                im.append(half(a1 * b0 - a0 * b1))
                            racc_ref[i, k, 0, pl.ds(blk * 8, 8), pl.ds(ct * 128, 128)] = fold(re)
                            racc_ref[i, k, 1, pl.ds(blk * 8, 8), pl.ds(ct * 128, 128)] = fold(im)

            return c

        lax.fori_loop(0, own, pairs, 0)

    vmem = pltpu.VMEM
    return pl.pallas_call(
        kernel,
        out_shape=(
            jax.ShapeDtypeStruct(racc_in.shape, jnp.float32),
            jax.ShapeDtypeStruct((1, groups, lanes), jnp.float32),
        ),
        in_specs=[pl.BlockSpec(memory_space=pltpu.SMEM)] + [pl.BlockSpec(memory_space=vmem) for _ in range(3)],
        out_specs=(pl.BlockSpec(memory_space=vmem), pl.BlockSpec(memory_space=vmem)),
        scratch_shapes=[
            pltpu.VMEM((own + 1, 2, rows, cols), jnp.float32),
            pltpu.VMEM((groups, cols), jnp.float32),
        ],
        input_output_aliases={3: 0},
        compiler_params=pltpu.CompilerParams(vmem_limit_bytes=48 * 1024 * 1024),
    )(offsets, slc, rim, racc_in)


def on_device(slc, offsets, owner):
    count = slc.shape[0]
    inner = count - NB
    rims = [shifted(slc[t : t + 1], "date", -1) for t in range(NB)]
    ifg_a, coh_a, ws_a, pw_a, rx_a = local_math(
        offsets, [slc], [(0, t) for t in range(count)], 0, inner, count, 0
    )
    racc = rx_a
    powers = [pw_a[inner:]]
    for step in range(NB - 1):
        racc, pw_step = rim_step(offsets[inner:], racc, slc, rims[step], step, inner)
        powers.append(pw_step)
    interferograms, coherence, slotted = local_math(
        offsets[inner:],
        [slc] + rims,
        [(0, inner + t) for t in range(NB)] + [(1 + t, 0) for t in range(NB)],
        0,
        NB,
        count,
        inner,
        known=(owner, jnp.concatenate(powers, 0), ws_a, racc, ifg_a, coh_a, 0),
    )
    width = ifg_a.shape[-1] // owner.shape[0]
    sums = lax.all_to_all(slotted, "date", split_axis=0, concat_axis=0, tiled=True).sum(0)
    halves = ifg_a.shape[3] // SLOT

    def field(f):
        return jnp.concatenate(
            [sums[:, (h * 3 + f) * width : (h * 3 + f + 1) * width] for h in range(halves)], 0
        )

    network_mean = (jnp.stack([field(0), field(1)], 0) / (1.0 + field(2)))[None]
    return (interferograms, coherence, network_mean)


def solution(mesh):
    placed = (P("date", None, "strip", None), P("date", None), P())
    return jax.shard_map(
        on_device,
        mesh=mesh,
        in_specs=placed,
        out_specs=(
            P("date", None, None, "strip", None),
            P("date", None, "strip", None),
            P("date", None, "strip", None),
        ),
        check_vma=False,
    )
```

```python
import jax
import jax.numpy as jnp
from jax import lax
from jax.experimental import pallas as pl
from jax.experimental.pallas import tpu as pltpu
from jax.sharding import PartitionSpec as P

NB = 3
LR = 16
LA = 4
SLOT = 4


def shifted(value, axis, steps):
    count = lax.axis_size(axis)
    pairs = [(source, (source + steps) % count) for source in range(count)]
    return lax.ppermute(value, axis, pairs)


def split_pool(field, pool):
    hi = field.astype(jnp.bfloat16)
    rest = field - hi.astype(jnp.float32)
    mid = rest.astype(jnp.bfloat16)
    lo = (rest - mid.astype(jnp.float32)).astype(jnp.bfloat16)
    out = jnp.dot(hi, pool, preferred_element_type=jnp.float32)
    out = out + jnp.dot(mid, pool, preferred_element_type=jnp.float32)
    return out + jnp.dot(lo, pool, preferred_element_type=jnp.float32)


def make_kernel(images, first, dates, rows, cols, known, tiles, date0, pw_base):
    groups = rows // LR
    cells = cols // LA
    total = len(images)
    ctiles = cols // 128
    lanes = 128
    nsrc = len(set(src for src, _ in images))

    def kernel(*refs):
        off_ref = refs[0]
        if known:
            owner_ref, pw_in, ws_in, rx_in = refs[1:5]
            srcs = refs[7 : 7 + nsrc]
            rest = refs[7 + nsrc :]
            ifg_ref, coh_ref, last_ref = rest[:3]
            xf, pacc, racc, pw, racc_pooled, ifg_s, coh_s, pay, ws_s, osem = rest[3:]
        else:
            srcs = refs[1 : 1 + nsrc]
            rest = refs[1 + nsrc :]
            ifg_ref, coh_ref, last_ref, pw_out, racc_x = rest[:5]
            xf, pacc, racc, pw, racc_pooled, ifg_s, coh_s, osem = rest[5:]
        if known:
            pw_cp = pltpu.make_async_copy(pw_in.at[pl.ds(pw_base, known)], pw.at[pl.ds(0, known)], osem.at[0])
            ws_cp = pltpu.make_async_copy(ws_in, ws_s, osem.at[1])
            rx_cp = pltpu.make_async_copy(rx_in, racc, osem.at[2])
            pw_cp.start()
            ws_cp.start()
            rx_cp.start()
        for t, (src, lead) in enumerate(images):
            if t >= known or (t < NB and t + NB >= known):
                xf[t] = srcs[src][lead].astype(jnp.float32)

        line = lax.broadcasted_iota(jnp.int32, (cols, lanes), 0)
        cell = lax.broadcasted_iota(jnp.int32, (cols, lanes), 1)
        pool = jnp.where(line // LA == cell, 1.0 / (LR * LA), 0.0).astype(jnp.bfloat16)
        sub = lax.broadcasted_iota(jnp.int32, (8, 128), 0)
        masks = {k: (sub % (2 * k)) < k for k in (4, 2, 1)}

        def combine(x, y, k):
            m = masks[k]
            return jnp.where(m, x + pltpu.roll(x, 8 - k, 0), y + pltpu.roll(y, k, 0))

        def fold(parts):
            q = [combine(parts[g], parts[g + 4], 4) for g in range(4)]
            r = [combine(q[0], q[2], 2), combine(q[1], q[3], 2)]
            return combine(r[0], r[1], 1)

        def rows_of(j, comp, g, ct):
            return xf[j, comp, pl.ds(g * LR, LR), pl.ds(ct * 128, 128)]

        def half(v):
            return v[:8] + v[8:]

        def power(j, c):
            for ct in range(ctiles):
                for blk in range(groups // 8):
                    parts = []
                    for g in range(blk * 8, blk * 8 + 8):
                        x0 = rows_of(j, 0, g, ct)
                        x1 = rows_of(j, 1, g, ct)
                        parts.append(half(x0 * x0 + x1 * x1))
                    pacc[j - known, pl.ds(blk * 8, 8), pl.ds(ct * 128, 128)] = fold(parts)
            return c

        lax.fori_loop(known, total, power, 0)
        fresh = total - known
        pw[pl.ds(known, fresh)] = split_pool(pacc[...].reshape(fresh * groups, cols), pool).reshape(
            fresh, groups, lanes
        )
        if known:
            pw_cp.wait()
        else:
            pw_out[...] = pw[...]

        def partner(i, k):
            return jnp.clip(first + i + off_ref[i, k], 0, total - 1)

        def wanted(i, k):
            reach = first + i + off_ref[i, k]
            if known:
                return reach >= known
            return jnp.logical_or(i < dates, reach <= total - 1)

        def pairs(i, c):
            for k in range(NB):
                j = partner(i, k)

                @pl.when(wanted(i, k))
                def _():
                    for ct in range(ctiles):
                        for blk in range(groups // 8):
                            re = []
                            im = []
                            for g in range(blk * 8, blk * 8 + 8):
                                a0 = rows_of(first + i, 0, g, ct)
                                a1 = rows_of(first + i, 1, g, ct)
                                b0 = rows_of(j, 0, g, ct)
                                b1 = rows_of(j, 1, g, ct)
                                re.append(half(a0 * b0 + a1 * b1))
                                im.append(half(a1 * b0 - a0 * b1))
                            racc[i, k, 0, pl.ds(blk * 8, 8), pl.ds(ct * 128, 128)] = fold(re)
                            racc[i, k, 1, pl.ds(blk * 8, 8), pl.ds(ct * 128, 128)] = fold(im)

            return c

        if known:
            rx_cp.wait()
        lax.fori_loop(0, racc.shape[0], pairs, 0)
        if not known:
            racc_x[...] = racc[pl.ds(dates, racc.shape[0] - dates)]
        pooled = split_pool(racc[pl.ds(0, dates)].reshape(dates * NB * 2 * groups, cols), pool)
        pooled = pooled.reshape(dates, NB, 2, groups, lanes)
        ifg_s[...] = pooled[..., :cells]

        def coher(i, ws):
            wr, wi, wc = ws
            pa = pw[first + i]
            for k in range(NB):
                pb = pw[partner(i, k)]
                re = pooled_at(i, k, 0)
                im = pooled_at(i, k, 1)
                co = jnp.sqrt(re * re + im * im) / jnp.sqrt(pa * pb + 1e-06)
                coh_s[i, k] = co[:, :cells]
                wr = wr + co * re
                wi = wi + co * im
                wc = wc + co
            return (wr, wi, wc)

        racc_pooled[...] = pooled

        def pooled_at(i, k, comp):
            return racc_pooled[i, k, comp]

        zero = jnp.zeros((groups, lanes), jnp.float32)
        if known:
            ws_cp.wait()
            start = (ws_s[0], ws_s[1], ws_s[2])
        else:
            start = (zero, zero, zero)
        wr, wi, wc = lax.fori_loop(0, dates, coher, start)
        outs = [
            pltpu.make_async_copy(ifg_s, ifg_ref.at[pl.ds(date0, dates)], osem.at[3]),
            pltpu.make_async_copy(coh_s, coh_ref.at[pl.ds(date0, dates)], osem.at[4]),
        ]
        for cp in outs:
            cp.start()
        if not known:
            last_ref[0] = wr
            last_ref[1] = wi
            last_ref[2] = wc
            for cp in outs:
                cp.wait()
            return
        width = cells // tiles
        lane = lax.broadcasted_iota(jnp.int32, (SLOT, lanes), 1)
        sums = (wr, wi, wc)
        for t in range(tiles):
            base = t * width
            block = jnp.zeros((SLOT, lanes), jnp.float32)
            for h in range(groups // SLOT):
                for f in range(3):
                    at = (h * 3 + f) * width
                    moved = pltpu.roll(sums[f][h * SLOT : h * SLOT + SLOT], (lanes + at - base) % lanes, 1)
                    block = jnp.where((lane >= at) & (lane < at + width), moved, block)
            pay[owner_ref[t]] = block
        pay_cp = pltpu.make_async_copy(pay, last_ref, osem.at[5])
        pay_cp.start()
        for cp in outs:
            cp.wait()
        pay_cp.wait()

    return kernel


def local_math(offsets, sources, images, first, dates, count, date0, known=None):
    pair_dates = offsets.shape[0]
    _, _, rows, cols = sources[0].shape
    groups = rows // LR
    cells = cols // LA
    total = len(images)
    lanes = 128
    vmem = pltpu.VMEM
    smem = pltpu.SMEM
    anyspace = pl.BlockSpec(memory_space=pl.ANY)
    hbm = pl.BlockSpec(memory_space=vmem)
    full = [
        jax.ShapeDtypeStruct((count, NB, 2, groups, cells), jnp.float32),
        jax.ShapeDtypeStruct((count, NB, groups, cells), jnp.float32),
    ]
    scratch = [
        pltpu.VMEM((total, 2, rows, cols), jnp.float32),
        None,
        pltpu.VMEM((pair_dates, NB, 2, groups, cols), jnp.float32),
        pltpu.VMEM((total, groups, lanes), jnp.float32),
        pltpu.VMEM((dates, NB, 2, groups, lanes), jnp.float32),
        pltpu.VMEM((dates, NB, 2, groups, cells), jnp.float32),
        pltpu.VMEM((dates, NB, groups, cells), jnp.float32),
    ]
    if known is None:
        nknown, tiles, pw_base = 0, 0, 0
        out_shape = full + [
            jax.ShapeDtypeStruct((3, groups, lanes), jnp.float32),
            jax.ShapeDtypeStruct((total, groups, lanes), jnp.float32),
            jax.ShapeDtypeStruct((pair_dates - dates, NB, 2, groups, cols), jnp.float32),
        ]
        out_specs = [anyspace, anyspace] + [pl.BlockSpec(memory_space=vmem) for _ in range(3)]
        in_specs = [pl.BlockSpec(memory_space=smem)] + [hbm for _ in sources]
        extra = []
        aliases = {}
    else:
        owner, pw_in, ws_in, rx_in, ifg_in, coh_in, pw_base = known
        nknown, tiles = pw_in.shape[0], owner.shape[0]
        out_shape = full + [jax.ShapeDtypeStruct((tiles, SLOT, lanes), jnp.float32)]
        out_specs = [anyspace, anyspace, anyspace]
        in_specs = [pl.BlockSpec(memory_space=smem), pl.BlockSpec(memory_space=smem)] + [
            anyspace for _ in range(5)
        ] + [hbm for _ in sources]
        extra = [owner, pw_in, ws_in, rx_in, ifg_in, coh_in]
        aliases = {5: 0, 6: 1}
        scratch += [pltpu.VMEM((tiles, SLOT, lanes), jnp.float32), pltpu.VMEM((3, groups, lanes), jnp.float32)]
    scratch[1] = pltpu.VMEM((total - nknown, groups, cols), jnp.float32)
    scratch += [pltpu.SemaphoreType.DMA((6,))]
    return pl.pallas_call(
        make_kernel(images, first, dates, rows, cols, nknown, tiles, date0, pw_base),
        out_shape=tuple(out_shape),
        in_specs=in_specs,
        out_specs=tuple(out_specs),
        scratch_shapes=scratch,
        input_output_aliases=aliases,
        compiler_params=pltpu.CompilerParams(vmem_limit_bytes=48 * 1024 * 1024),
    )(offsets, *extra, *sources)


def rim_step(offsets, racc_in, slc, rim, step, inner):
    _, _, rows, cols = slc.shape
    groups = rows // LR
    ctiles = cols // 128
    lanes = 128
    own = slc.shape[0] - inner

    def kernel(off_ref, slc_ref, rim_ref, racc_in_ref, racc_ref, pw_ref, xf, pacc):
        for t in range(own):
            xf[t] = slc_ref[inner + t].astype(jnp.float32)
        xf[own] = rim_ref[0].astype(jnp.float32)
        line = lax.broadcasted_iota(jnp.int32, (cols, lanes), 0)
        cell = lax.broadcasted_iota(jnp.int32, (cols, lanes), 1)
        pool = jnp.where(line // LA == cell, 1.0 / (LR * LA), 0.0).astype(jnp.bfloat16)
        sub = lax.broadcasted_iota(jnp.int32, (8, 128), 0)
        masks = {k: (sub % (2 * k)) < k for k in (4, 2, 1)}

        def combine(x, y, k):
            m = masks[k]
            return jnp.where(m, x + pltpu.roll(x, 8 - k, 0), y + pltpu.roll(y, k, 0))

        def fold(parts):
            q = [combine(parts[g], parts[g + 4], 4) for g in range(4)]
            r = [combine(q[0], q[2], 2), combine(q[1], q[3], 2)]
            return combine(r[0], r[1], 1)

        def rows_of(j, comp, g, ct):
            return xf[j, comp, pl.ds(g * LR, LR), pl.ds(ct * 128, 128)]

        def half(v):
            return v[:8] + v[8:]

        for ct in range(ctiles):
            for blk in range(groups // 8):
                parts = []
                for g in range(blk * 8, blk * 8 + 8):
                    x0 = rows_of(own, 0, g, ct)
                    x1 = rows_of(own, 1, g, ct)
                    parts.append(half(x0 * x0 + x1 * x1))
                pacc[pl.ds(blk * 8, 8), pl.ds(ct * 128, 128)] = fold(parts)
        pw_ref[0] = split_pool(pacc[...], pool)

        def pairs(i, c):
            for k in range(NB):

                @pl.when(i + off_ref[i, k] == own + step)
                def _():
                    for ct in range(ctiles):
                        for blk in range(groups // 8):
                            re = []
                            im = []
                            for g in range(blk * 8, blk * 8 + 8):
                                a0 = rows_of(i, 0, g, ct)
                                a1 = rows_of(i, 1, g, ct)
                                b0 = rows_of(own, 0, g, ct)
                                b1 = rows_of(own, 1, g, ct)
                                re.append(half(a0 * b0 + a1 * b1))
                                im.append(half(a1 * b0 - a0 * b1))
                            racc_ref[i, k, 0, pl.ds(blk * 8, 8), pl.ds(ct * 128, 128)] = fold(re)
                            racc_ref[i, k, 1, pl.ds(blk * 8, 8), pl.ds(ct * 128, 128)] = fold(im)

            return c

        lax.fori_loop(0, own, pairs, 0)

    vmem = pltpu.VMEM
    return pl.pallas_call(
        kernel,
        out_shape=(
            jax.ShapeDtypeStruct(racc_in.shape, jnp.float32),
            jax.ShapeDtypeStruct((1, groups, lanes), jnp.float32),
        ),
        in_specs=[pl.BlockSpec(memory_space=pltpu.SMEM)] + [pl.BlockSpec(memory_space=vmem) for _ in range(3)],
        out_specs=(pl.BlockSpec(memory_space=vmem), pl.BlockSpec(memory_space=vmem)),
        scratch_shapes=[
            pltpu.VMEM((own + 1, 2, rows, cols), jnp.float32),
            pltpu.VMEM((groups, cols), jnp.float32),
        ],
        input_output_aliases={3: 0},
        compiler_params=pltpu.CompilerParams(vmem_limit_bytes=48 * 1024 * 1024),
    )(offsets, slc, rim, racc_in)


def on_device(slc, offsets, owner):
    count = slc.shape[0]
    inner = count - NB
    rims = [shifted(slc[t : t + 1], "date", -1) for t in range(NB)]
    ifg_a, coh_a, ws_a, pw_a, rx_a = local_math(
        offsets, [slc], [(0, t) for t in range(count)], 0, inner, count, 0
    )
    racc = rx_a
    powers = [pw_a[inner:]]
    for step in range(NB - 1):
        racc, pw_step = rim_step(offsets[inner:], racc, slc, rims[step], step, inner)
        powers.append(pw_step)
    interferograms, coherence, slotted = local_math(
        offsets[inner:],
        [slc] + rims,
        [(0, inner + t) for t in range(NB)] + [(1 + t, 0) for t in range(NB)],
        0,
        NB,
        count,
        inner,
        known=(owner, jnp.concatenate(powers, 0), ws_a, racc, ifg_a, coh_a, 0),
    )
    width = ifg_a.shape[-1] // owner.shape[0]
    sums = lax.all_to_all(slotted, "date", split_axis=0, concat_axis=0, tiled=True).sum(0)
    halves = ifg_a.shape[3] // SLOT

    def field(f):
        return jnp.concatenate(
            [sums[:, (h * 3 + f) * width : (h * 3 + f + 1) * width] for h in range(halves)], 0
        )

    network_mean = (jnp.stack([field(0), field(1)], 0) / (1.0 + field(2)))[None]
    return (interferograms, coherence, network_mean)


def solution(mesh):
    placed = (P("date", None, "strip", None), P("date", None), P())
    return jax.shard_map(
        on_device,
        mesh=mesh,
        in_specs=placed,
        out_specs=(
            P("date", None, None, "strip", None),
            P("date", None, "strip", None),
            P("date", None, "strip", None),
        ),
        check_vma=False,
    )
```

```python
import jax
import jax.numpy as jnp
from jax import lax
from jax.experimental import pallas as pl
from jax.experimental.pallas import tpu as pltpu
from jax.sharding import PartitionSpec as P

NB = 3
LR = 16
LA = 4
SLOT = 4


def shifted(value, axis, steps):
    count = lax.axis_size(axis)
    pairs = [(source, (source + steps) % count) for source in range(count)]
    return lax.ppermute(value, axis, pairs)


def split_pool(field, pool):
    hi = field.astype(jnp.bfloat16)
    rest = field - hi.astype(jnp.float32)
    mid = rest.astype(jnp.bfloat16)
    lo = (rest - mid.astype(jnp.float32)).astype(jnp.bfloat16)
    out = jnp.dot(hi, pool, preferred_element_type=jnp.float32)
    out = out + jnp.dot(mid, pool, preferred_element_type=jnp.float32)
    return out + jnp.dot(lo, pool, preferred_element_type=jnp.float32)


def make_kernel(images, first, dates, rows, cols, known, tiles, date0, pw_base):
    groups = rows // LR
    cells = cols // LA
    total = len(images)
    ctiles = cols // 128
    lanes = 128
    nsrc = len(set(src for src, _ in images))

    def kernel(*refs):
        off_ref = refs[0]
        if known:
            owner_ref, pw_in, ws_in, rx_in = refs[1:5]
            srcs = refs[7 : 7 + nsrc]
            rest = refs[7 + nsrc :]
            ifg_ref, coh_ref, last_ref = rest[:3]
            xf, pacc, racc, pw, racc_pooled, ifg_s, coh_s, pay, ws_s, osem = rest[3:]
        else:
            srcs = refs[1 : 1 + nsrc]
            rest = refs[1 + nsrc :]
            ifg_ref, coh_ref, last_ref, pw_out, racc_x = rest[:5]
            xf, pacc, racc, pw, racc_pooled, ifg_s, coh_s, osem = rest[5:]
        if known:
            pw_cp = pltpu.make_async_copy(pw_in.at[pl.ds(pw_base, known)], pw.at[pl.ds(0, known)], osem.at[0])
            ws_cp = pltpu.make_async_copy(ws_in, ws_s, osem.at[1])
            rx_cp = pltpu.make_async_copy(rx_in, racc, osem.at[2])
            pw_cp.start()
            ws_cp.start()
            rx_cp.start()
        for t, (src, lead) in enumerate(images):
            if t >= known or (t < NB and t + NB >= known):
                xf[t] = srcs[src][lead].astype(jnp.float32)

        line = lax.broadcasted_iota(jnp.int32, (cols, lanes), 0)
        cell = lax.broadcasted_iota(jnp.int32, (cols, lanes), 1)
        pool = jnp.where(line // LA == cell, 1.0 / (LR * LA), 0.0).astype(jnp.bfloat16)
        sub = lax.broadcasted_iota(jnp.int32, (8, 128), 0)
        masks = {k: (sub % (2 * k)) < k for k in (4, 2, 1)}

        def combine(x, y, k):
            m = masks[k]
            return jnp.where(m, x + pltpu.roll(x, 8 - k, 0), y + pltpu.roll(y, k, 0))

        def fold(parts):
            q = [combine(parts[g], parts[g + 4], 4) for g in range(4)]
            r = [combine(q[0], q[2], 2), combine(q[1], q[3], 2)]
            return combine(r[0], r[1], 1)

        def rows_of(j, comp, g, ct):
            return xf[j, comp, pl.ds(g * LR, LR), pl.ds(ct * 128, 128)]

        def half(v):
            return v[:8] + v[8:]

        def power(j, c):
            for ct in range(ctiles):
                for blk in range(groups // 8):
                    parts = []
                    for g in range(blk * 8, blk * 8 + 8):
                        x0 = rows_of(j, 0, g, ct)
                        x1 = rows_of(j, 1, g, ct)
                        parts.append(half(x0 * x0 + x1 * x1))
                    pacc[j - known, pl.ds(blk * 8, 8), pl.ds(ct * 128, 128)] = fold(parts)
            return c

        lax.fori_loop(known, total, power, 0)
        fresh = total - known
        pw[pl.ds(known, fresh)] = split_pool(pacc[...].reshape(fresh * groups, cols), pool).reshape(
            fresh, groups, lanes
        )
        if known:
            pw_cp.wait()
        else:
            pw_out[...] = pw[...]

        def partner(i, k):
            return jnp.clip(first + i + off_ref[i, k], 0, total - 1)

        def wanted(i, k):
            reach = first + i + off_ref[i, k]
            if known:
                return reach >= known
            return jnp.logical_or(i < dates, reach <= total - 1)

        def pairs(i, c):
            for k in range(NB):
                j = partner(i, k)

                @pl.when(wanted(i, k))
                def _():
                    for ct in range(ctiles):
                        for blk in range(groups // 8):
                            re = []
                            im = []
                            for g in range(blk * 8, blk * 8 + 8):
                                a0 = rows_of(first + i, 0, g, ct)
                                a1 = rows_of(first + i, 1, g, ct)
                                b0 = rows_of(j, 0, g, ct)
                                b1 = rows_of(j, 1, g, ct)
                                re.append(half(a0 * b0 + a1 * b1))
                                im.append(half(a1 * b0 - a0 * b1))
                            racc[i, k, 0, pl.ds(blk * 8, 8), pl.ds(ct * 128, 128)] = fold(re)
                            racc[i, k, 1, pl.ds(blk * 8, 8), pl.ds(ct * 128, 128)] = fold(im)

            return c

        if known:
            rx_cp.wait()
        lax.fori_loop(0, racc.shape[0], pairs, 0)
        if not known:
            racc_x[...] = racc[pl.ds(dates, racc.shape[0] - dates)]
        pooled = split_pool(racc[pl.ds(0, dates)].reshape(dates * NB * 2 * groups, cols), pool)
        pooled = pooled.reshape(dates, NB, 2, groups, lanes)
        ifg_s[...] = pooled[..., :cells]

        def coher(i, ws):
            wr, wi, wc = ws
            pa = pw[first + i]
            for k in range(NB):
                pb = pw[partner(i, k)]
                re = pooled_at(i, k, 0)
                im = pooled_at(i, k, 1)
                co = jnp.sqrt(re * re + im * im) / jnp.sqrt(pa * pb + 1e-06)
                coh_s[i, k] = co[:, :cells]
                wr = wr + co * re
                wi = wi + co * im
                wc = wc + co
            return (wr, wi, wc)

        racc_pooled[...] = pooled

        def pooled_at(i, k, comp):
            return racc_pooled[i, k, comp]

        zero = jnp.zeros((groups, lanes), jnp.float32)
        if known:
            ws_cp.wait()
            start = (ws_s[0], ws_s[1], ws_s[2])
        else:
            start = (zero, zero, zero)
        wr, wi, wc = lax.fori_loop(0, dates, coher, start)
        outs = [
            pltpu.make_async_copy(ifg_s, ifg_ref.at[pl.ds(date0, dates)], osem.at[3]),
            pltpu.make_async_copy(coh_s, coh_ref.at[pl.ds(date0, dates)], osem.at[4]),
        ]
        for cp in outs:
            cp.start()
        if not known:
            last_ref[0] = wr
            last_ref[1] = wi
            last_ref[2] = wc
            for cp in outs:
                cp.wait()
            return
        width = cells // tiles
        lane = lax.broadcasted_iota(jnp.int32, (SLOT, lanes), 1)
        sums = (wr, wi, wc)
        for t in range(tiles):
            base = t * width
            block = jnp.zeros((SLOT, lanes), jnp.float32)
            for h in range(groups // SLOT):
                for f in range(3):
                    at = (h * 3 + f) * width
                    moved = pltpu.roll(sums[f][h * SLOT : h * SLOT + SLOT], (lanes + at - base) % lanes, 1)
                    block = jnp.where((lane >= at) & (lane < at + width), moved, block)
            pay[owner_ref[t]] = block
        pay_cp = pltpu.make_async_copy(pay, last_ref, osem.at[5])
        pay_cp.start()
        for cp in outs:
            cp.wait()
        pay_cp.wait()

    return kernel


def local_math(offsets, sources, images, first, dates, count, date0, known=None):
    pair_dates = offsets.shape[0]
    _, _, rows, cols = sources[0].shape
    groups = rows // LR
    cells = cols // LA
    total = len(images)
    lanes = 128
    vmem = pltpu.VMEM
    smem = pltpu.SMEM
    anyspace = pl.BlockSpec(memory_space=pl.ANY)
    hbm = pl.BlockSpec(memory_space=vmem)
    full = [
        jax.ShapeDtypeStruct((count, NB, 2, groups, cells), jnp.float32),
        jax.ShapeDtypeStruct((count, NB, groups, cells), jnp.float32),
    ]
    scratch = [
        pltpu.VMEM((total, 2, rows, cols), jnp.float32),
        None,
        pltpu.VMEM((pair_dates, NB, 2, groups, cols), jnp.float32),
        pltpu.VMEM((total, groups, lanes), jnp.float32),
        pltpu.VMEM((dates, NB, 2, groups, lanes), jnp.float32),
        pltpu.VMEM((dates, NB, 2, groups, cells), jnp.float32),
        pltpu.VMEM((dates, NB, groups, cells), jnp.float32),
    ]
    if known is None:
        nknown, tiles, pw_base = 0, 0, 0
        out_shape = full + [
            jax.ShapeDtypeStruct((3, groups, lanes), jnp.float32),
            jax.ShapeDtypeStruct((total, groups, lanes), jnp.float32),
            jax.ShapeDtypeStruct((pair_dates - dates, NB, 2, groups, cols), jnp.float32),
        ]
        out_specs = [anyspace, anyspace] + [pl.BlockSpec(memory_space=vmem) for _ in range(3)]
        in_specs = [pl.BlockSpec(memory_space=smem)] + [hbm for _ in sources]
        extra = []
        aliases = {}
    else:
        owner, pw_in, ws_in, rx_in, ifg_in, coh_in, pw_base = known
        nknown, tiles = pw_in.shape[0], owner.shape[0]
        out_shape = full + [jax.ShapeDtypeStruct((tiles, SLOT, lanes), jnp.float32)]
        out_specs = [anyspace, anyspace, anyspace]
        in_specs = [pl.BlockSpec(memory_space=smem), pl.BlockSpec(memory_space=smem)] + [
            anyspace for _ in range(5)
        ] + [hbm for _ in sources]
        extra = [owner, pw_in, ws_in, rx_in, ifg_in, coh_in]
        aliases = {5: 0, 6: 1}
        scratch += [pltpu.VMEM((tiles, SLOT, lanes), jnp.float32), pltpu.VMEM((3, groups, lanes), jnp.float32)]
    scratch[1] = pltpu.VMEM((total - nknown, groups, cols), jnp.float32)
    scratch += [pltpu.SemaphoreType.DMA((6,))]
    return pl.pallas_call(
        make_kernel(images, first, dates, rows, cols, nknown, tiles, date0, pw_base),
        out_shape=tuple(out_shape),
        in_specs=in_specs,
        out_specs=tuple(out_specs),
        scratch_shapes=scratch,
        input_output_aliases=aliases,
        compiler_params=pltpu.CompilerParams(vmem_limit_bytes=48 * 1024 * 1024),
    )(offsets, *extra, *sources)


def rim_step(offsets, racc_in, slc, rim, step, inner):
    _, _, rows, cols = slc.shape
    groups = rows // LR
    ctiles = cols // 128
    lanes = 128
    own = slc.shape[0] - inner

    def kernel(off_ref, slc_ref, rim_ref, racc_in_ref, racc_ref, pw_ref, xf, pacc):
        for t in range(own):
            xf[t] = slc_ref[inner + t].astype(jnp.float32)
        xf[own] = rim_ref[0].astype(jnp.float32)
        line = lax.broadcasted_iota(jnp.int32, (cols, lanes), 0)
        cell = lax.broadcasted_iota(jnp.int32, (cols, lanes), 1)
        pool = jnp.where(line // LA == cell, 1.0 / (LR * LA), 0.0).astype(jnp.bfloat16)
        sub = lax.broadcasted_iota(jnp.int32, (8, 128), 0)
        masks = {k: (sub % (2 * k)) < k for k in (4, 2, 1)}

        def combine(x, y, k):
            m = masks[k]
            return jnp.where(m, x + pltpu.roll(x, 8 - k, 0), y + pltpu.roll(y, k, 0))

        def fold(parts):
            q = [combine(parts[g], parts[g + 4], 4) for g in range(4)]
            r = [combine(q[0], q[2], 2), combine(q[1], q[3], 2)]
            return combine(r[0], r[1], 1)

        def rows_of(j, comp, g, ct):
            return xf[j, comp, pl.ds(g * LR, LR), pl.ds(ct * 128, 128)]

        def half(v):
            return v[:8] + v[8:]

        for ct in range(ctiles):
            for blk in range(groups // 8):
                parts = []
                for g in range(blk * 8, blk * 8 + 8):
                    x0 = rows_of(own, 0, g, ct)
                    x1 = rows_of(own, 1, g, ct)
                    parts.append(half(x0 * x0 + x1 * x1))
                pacc[pl.ds(blk * 8, 8), pl.ds(ct * 128, 128)] = fold(parts)
        pw_ref[0] = split_pool(pacc[...], pool)

        def pairs(i, c):
            for k in range(NB):

                @pl.when(i + off_ref[i, k] == own + step)
                def _():
                    for ct in range(ctiles):
                        for blk in range(groups // 8):
                            re = []
                            im = []
                            for g in range(blk * 8, blk * 8 + 8):
                                a0 = rows_of(i, 0, g, ct)
                                a1 = rows_of(i, 1, g, ct)
                                b0 = rows_of(own, 0, g, ct)
                                b1 = rows_of(own, 1, g, ct)
                                re.append(half(a0 * b0 + a1 * b1))
                                im.append(half(a1 * b0 - a0 * b1))
                            racc_ref[i, k, 0, pl.ds(blk * 8, 8), pl.ds(ct * 128, 128)] = fold(re)
                            racc_ref[i, k, 1, pl.ds(blk * 8, 8), pl.ds(ct * 128, 128)] = fold(im)

            return c

        lax.fori_loop(0, own, pairs, 0)

    vmem = pltpu.VMEM
    return pl.pallas_call(
        kernel,
        out_shape=(
            jax.ShapeDtypeStruct(racc_in.shape, jnp.float32),
            jax.ShapeDtypeStruct((1, groups, lanes), jnp.float32),
        ),
        in_specs=[pl.BlockSpec(memory_space=pltpu.SMEM)] + [pl.BlockSpec(memory_space=vmem) for _ in range(3)],
        out_specs=(pl.BlockSpec(memory_space=vmem), pl.BlockSpec(memory_space=vmem)),
        scratch_shapes=[
            pltpu.VMEM((own + 1, 2, rows, cols), jnp.float32),
            pltpu.VMEM((groups, cols), jnp.float32),
        ],
        input_output_aliases={3: 0},
        compiler_params=pltpu.CompilerParams(vmem_limit_bytes=48 * 1024 * 1024),
    )(offsets, slc, rim, racc_in)


def on_device(slc, offsets, owner):
    count = slc.shape[0]
    inner = count - NB
    later = lax.optimization_barrier(slc)
    rims = [shifted((slc if t == 0 else later)[t : t + 1], "date", -1) for t in range(NB)]
    ifg_a, coh_a, ws_a, pw_a, rx_a = local_math(
        offsets, [slc], [(0, t) for t in range(count)], 0, inner, count, 0
    )
    racc = rx_a
    powers = [pw_a[inner:]]
    for step in range(NB - 1):
        racc, pw_step = rim_step(offsets[inner:], racc, slc, rims[step], step, inner)
        powers.append(pw_step)
    interferograms, coherence, slotted = local_math(
        offsets[inner:],
        [slc] + rims,
        [(0, inner + t) for t in range(NB)] + [(1 + t, 0) for t in range(NB)],
        0,
        NB,
        count,
        inner,
        known=(owner, jnp.concatenate(powers, 0), ws_a, racc, ifg_a, coh_a, 0),
    )
    width = ifg_a.shape[-1] // owner.shape[0]
    sums = lax.all_to_all(slotted, "date", split_axis=0, concat_axis=0, tiled=True).sum(0)
    halves = ifg_a.shape[3] // SLOT

    def field(f):
        return jnp.concatenate(
            [sums[:, (h * 3 + f) * width : (h * 3 + f + 1) * width] for h in range(halves)], 0
        )

    network_mean = (jnp.stack([field(0), field(1)], 0) / (1.0 + field(2)))[None]
    return (interferograms, coherence, network_mean)


def solution(mesh):
    placed = (P("date", None, "strip", None), P("date", None), P())
    return jax.shard_map(
        on_device,
        mesh=mesh,
        in_specs=placed,
        out_specs=(
            P("date", None, None, "strip", None),
            P("date", None, "strip", None),
            P("date", None, "strip", None),
        ),
        check_vma=False,
    )
```

```python
import jax
import jax.numpy as jnp
from jax import lax
from jax.experimental import pallas as pl
from jax.experimental.pallas import tpu as pltpu
from jax.sharding import PartitionSpec as P

NB = 3
LR = 16
LA = 4
SLOT = 4


def shifted(value, axis, steps):
    count = lax.axis_size(axis)
    pairs = [(source, (source + steps) % count) for source in range(count)]
    return lax.ppermute(value, axis, pairs)


def split_pool(field, pool):
    hi = field.astype(jnp.bfloat16)
    rest = field - hi.astype(jnp.float32)
    mid = rest.astype(jnp.bfloat16)
    lo = (rest - mid.astype(jnp.float32)).astype(jnp.bfloat16)
    out = jnp.dot(hi, pool, preferred_element_type=jnp.float32)
    out = out + jnp.dot(mid, pool, preferred_element_type=jnp.float32)
    return out + jnp.dot(lo, pool, preferred_element_type=jnp.float32)


def make_kernel(images, first, dates, rows, cols, known, tiles, date0, pw_base, emit_ws):
    groups = rows // LR
    cells = cols // LA
    total = len(images)
    ctiles = cols // 128
    lanes = 128
    nsrc = len(set(src for src, _ in images))

    def kernel(*refs):
        off_ref = refs[0]
        if known:
            owner_ref, pw_in, ws_in, rx_in = refs[1:5]
            srcs = refs[7 : 7 + nsrc]
            rest = refs[7 + nsrc :]
            ifg_ref, coh_ref, last_ref = rest[:3]
            xf, pacc, racc, pw, racc_pooled, ifg_s, coh_s, pay, ws_s, osem = rest[3:]
        else:
            srcs = refs[1 : 1 + nsrc]
            rest = refs[1 + nsrc :]
            ifg_ref, coh_ref, last_ref, pw_out, racc_x = rest[:5]
            xf, pacc, racc, pw, racc_pooled, ifg_s, coh_s, osem = rest[5:]
        if known:
            pw_cp = pltpu.make_async_copy(pw_in.at[pl.ds(pw_base, known)], pw.at[pl.ds(0, known)], osem.at[0])
            ws_cp = pltpu.make_async_copy(ws_in, ws_s, osem.at[1])
            rx_cp = pltpu.make_async_copy(rx_in, racc, osem.at[2])
            pw_cp.start()
            ws_cp.start()
            rx_cp.start()
        for t, (src, lead) in enumerate(images):
            if t >= known or (t < NB and t + NB >= known):
                xf[t] = srcs[src][lead].astype(jnp.float32)

        line = lax.broadcasted_iota(jnp.int32, (cols, lanes), 0)
        cell = lax.broadcasted_iota(jnp.int32, (cols, lanes), 1)
        pool = jnp.where(line // LA == cell, 1.0 / (LR * LA), 0.0).astype(jnp.bfloat16)
        sub = lax.broadcasted_iota(jnp.int32, (8, 128), 0)
        masks = {k: (sub % (2 * k)) < k for k in (4, 2, 1)}

        def combine(x, y, k):
            m = masks[k]
            return jnp.where(m, x + pltpu.roll(x, 8 - k, 0), y + pltpu.roll(y, k, 0))

        def fold(parts):
            q = [combine(parts[g], parts[g + 4], 4) for g in range(4)]
            r = [combine(q[0], q[2], 2), combine(q[1], q[3], 2)]
            return combine(r[0], r[1], 1)

        def rows_of(j, comp, g, ct):
            return xf[j, comp, pl.ds(g * LR, LR), pl.ds(ct * 128, 128)]

        def half(v):
            return v[:8] + v[8:]

        def power(j, c):
            for ct in range(ctiles):
                for blk in range(groups // 8):
                    parts = []
                    for g in range(blk * 8, blk * 8 + 8):
                        x0 = rows_of(j, 0, g, ct)
                        x1 = rows_of(j, 1, g, ct)
                        parts.append(half(x0 * x0 + x1 * x1))
                    pacc[j - known, pl.ds(blk * 8, 8), pl.ds(ct * 128, 128)] = fold(parts)
            return c

        fresh = total - known
        if fresh:
            lax.fori_loop(known, total, power, 0)
            pw[pl.ds(known, fresh)] = split_pool(pacc[...].reshape(fresh * groups, cols), pool).reshape(
                fresh, groups, lanes
            )
        if known:
            pw_cp.wait()
        else:
            pw_out[...] = pw[...]

        def partner(i, k):
            return jnp.clip(first + i + off_ref[i, k], 0, total - 1)

        def wanted(i, k):
            reach = first + i + off_ref[i, k]
            if known:
                return reach >= known
            return jnp.logical_or(i < dates, reach <= total - 1)

        def pairs(i, c):
            for k in range(NB):
                j = partner(i, k)

                @pl.when(wanted(i, k))
                def _():
                    for ct in range(ctiles):
                        for blk in range(groups // 8):
                            re = []
                            im = []
                            for g in range(blk * 8, blk * 8 + 8):
                                a0 = rows_of(first + i, 0, g, ct)
                                a1 = rows_of(first + i, 1, g, ct)
                                b0 = rows_of(j, 0, g, ct)
                                b1 = rows_of(j, 1, g, ct)
                                re.append(half(a0 * b0 + a1 * b1))
                                im.append(half(a1 * b0 - a0 * b1))
                            racc[i, k, 0, pl.ds(blk * 8, 8), pl.ds(ct * 128, 128)] = fold(re)
                            racc[i, k, 1, pl.ds(blk * 8, 8), pl.ds(ct * 128, 128)] = fold(im)

            return c

        if known:
            rx_cp.wait()
        lax.fori_loop(0, racc.shape[0], pairs, 0)
        if not known:
            racc_x[...] = racc[pl.ds(dates, racc.shape[0] - dates)]
        pooled = split_pool(racc[pl.ds(0, dates)].reshape(dates * NB * 2 * groups, cols), pool)
        pooled = pooled.reshape(dates, NB, 2, groups, lanes)
        ifg_s[...] = pooled[..., :cells]

        def coher(i, ws):
            wr, wi, wc = ws
            pa = pw[first + i]
            for k in range(NB):
                pb = pw[partner(i, k)]
                re = pooled_at(i, k, 0)
                im = pooled_at(i, k, 1)
                co = jnp.sqrt(re * re + im * im) / jnp.sqrt(pa * pb + 1e-06)
                coh_s[i, k] = co[:, :cells]
                wr = wr + co * re
                wi = wi + co * im
                wc = wc + co
            return (wr, wi, wc)

        racc_pooled[...] = pooled

        def pooled_at(i, k, comp):
            return racc_pooled[i, k, comp]

        zero = jnp.zeros((groups, lanes), jnp.float32)
        if known:
            ws_cp.wait()
            start = (ws_s[0], ws_s[1], ws_s[2])
        else:
            start = (zero, zero, zero)
        wr, wi, wc = lax.fori_loop(0, dates, coher, start)
        outs = [
            pltpu.make_async_copy(ifg_s, ifg_ref.at[pl.ds(date0, dates)], osem.at[3]),
            pltpu.make_async_copy(coh_s, coh_ref.at[pl.ds(date0, dates)], osem.at[4]),
        ]
        for cp in outs:
            cp.start()
        if not known or emit_ws:
            last_ref[0] = wr
            last_ref[1] = wi
            last_ref[2] = wc
            for cp in outs:
                cp.wait()
            return
        width = cells // tiles
        lane = lax.broadcasted_iota(jnp.int32, (SLOT, lanes), 1)
        sums = (wr, wi, wc)
        for t in range(tiles):
            base = t * width
            block = jnp.zeros((SLOT, lanes), jnp.float32)
            for h in range(groups // SLOT):
                for f in range(3):
                    at = (h * 3 + f) * width
                    moved = pltpu.roll(sums[f][h * SLOT : h * SLOT + SLOT], (lanes + at - base) % lanes, 1)
                    block = jnp.where((lane >= at) & (lane < at + width), moved, block)
            pay[owner_ref[t]] = block
        pay_cp = pltpu.make_async_copy(pay, last_ref, osem.at[5])
        pay_cp.start()
        for cp in outs:
            cp.wait()
        pay_cp.wait()

    return kernel


def local_math(offsets, sources, images, first, dates, count, date0, known=None, emit_ws=False):
    pair_dates = offsets.shape[0]
    _, _, rows, cols = sources[0].shape
    groups = rows // LR
    cells = cols // LA
    total = len(images)
    lanes = 128
    vmem = pltpu.VMEM
    smem = pltpu.SMEM
    anyspace = pl.BlockSpec(memory_space=pl.ANY)
    hbm = pl.BlockSpec(memory_space=vmem)
    full = [
        jax.ShapeDtypeStruct((count, NB, 2, groups, cells), jnp.float32),
        jax.ShapeDtypeStruct((count, NB, groups, cells), jnp.float32),
    ]
    scratch = [
        pltpu.VMEM((total, 2, rows, cols), jnp.float32),
        None,
        pltpu.VMEM((pair_dates, NB, 2, groups, cols), jnp.float32),
        pltpu.VMEM((total, groups, lanes), jnp.float32),
        pltpu.VMEM((dates, NB, 2, groups, lanes), jnp.float32),
        pltpu.VMEM((dates, NB, 2, groups, cells), jnp.float32),
        pltpu.VMEM((dates, NB, groups, cells), jnp.float32),
    ]
    if known is None:
        nknown, tiles, pw_base = 0, 0, 0
        out_shape = full + [
            jax.ShapeDtypeStruct((3, groups, lanes), jnp.float32),
            jax.ShapeDtypeStruct((total, groups, lanes), jnp.float32),
            jax.ShapeDtypeStruct((pair_dates - dates, NB, 2, groups, cols), jnp.float32),
        ]
        out_specs = [anyspace, anyspace] + [pl.BlockSpec(memory_space=vmem) for _ in range(3)]
        in_specs = [pl.BlockSpec(memory_space=smem)] + [hbm for _ in sources]
        extra = []
        aliases = {}
    else:
        owner, pw_in, ws_in, rx_in, ifg_in, coh_in, pw_base = known
        nknown, tiles = pw_in.shape[0], owner.shape[0]
        if emit_ws:
            out_shape = full + [jax.ShapeDtypeStruct((3, groups, lanes), jnp.float32)]
        else:
            out_shape = full + [jax.ShapeDtypeStruct((tiles, SLOT, lanes), jnp.float32)]
        out_specs = [anyspace, anyspace, pl.BlockSpec(memory_space=vmem) if emit_ws else anyspace]
        in_specs = [pl.BlockSpec(memory_space=smem), pl.BlockSpec(memory_space=smem)] + [
            anyspace for _ in range(5)
        ] + [hbm for _ in sources]
        extra = [owner, pw_in, ws_in, rx_in, ifg_in, coh_in]
        aliases = {5: 0, 6: 1}
        scratch += [pltpu.VMEM((tiles, SLOT, lanes), jnp.float32), pltpu.VMEM((3, groups, lanes), jnp.float32)]
    scratch[1] = pltpu.VMEM((max(1, total - nknown), groups, cols), jnp.float32)
    scratch += [pltpu.SemaphoreType.DMA((6,))]
    return pl.pallas_call(
        make_kernel(images, first, dates, rows, cols, nknown, tiles, date0, pw_base, emit_ws),
        out_shape=tuple(out_shape),
        in_specs=in_specs,
        out_specs=tuple(out_specs),
        scratch_shapes=scratch,
        input_output_aliases=aliases,
        compiler_params=pltpu.CompilerParams(vmem_limit_bytes=48 * 1024 * 1024),
    )(offsets, *extra, *sources)


def rim_step(offsets, racc_in, slc, rim, step, inner):
    _, _, rows, cols = slc.shape
    groups = rows // LR
    ctiles = cols // 128
    lanes = 128
    own = slc.shape[0] - inner

    def kernel(off_ref, slc_ref, rim_ref, racc_in_ref, racc_ref, pw_ref, xf, pacc):
        for t in range(own):
            xf[t] = slc_ref[inner + t].astype(jnp.float32)
        xf[own] = rim_ref[0].astype(jnp.float32)
        line = lax.broadcasted_iota(jnp.int32, (cols, lanes), 0)
        cell = lax.broadcasted_iota(jnp.int32, (cols, lanes), 1)
        pool = jnp.where(line // LA == cell, 1.0 / (LR * LA), 0.0).astype(jnp.bfloat16)
        sub = lax.broadcasted_iota(jnp.int32, (8, 128), 0)
        masks = {k: (sub % (2 * k)) < k for k in (4, 2, 1)}

        def combine(x, y, k):
            m = masks[k]
            return jnp.where(m, x + pltpu.roll(x, 8 - k, 0), y + pltpu.roll(y, k, 0))

        def fold(parts):
            q = [combine(parts[g], parts[g + 4], 4) for g in range(4)]
            r = [combine(q[0], q[2], 2), combine(q[1], q[3], 2)]
            return combine(r[0], r[1], 1)

        def rows_of(j, comp, g, ct):
            return xf[j, comp, pl.ds(g * LR, LR), pl.ds(ct * 128, 128)]

        def half(v):
            return v[:8] + v[8:]

        for ct in range(ctiles):
            for blk in range(groups // 8):
                parts = []
                for g in range(blk * 8, blk * 8 + 8):
                    x0 = rows_of(own, 0, g, ct)
                    x1 = rows_of(own, 1, g, ct)
                    parts.append(half(x0 * x0 + x1 * x1))
                pacc[pl.ds(blk * 8, 8), pl.ds(ct * 128, 128)] = fold(parts)
        pw_ref[0] = split_pool(pacc[...], pool)

        def pairs(i, c):
            for k in range(NB):

                @pl.when(i + off_ref[i, k] == own + step)
                def _():
                    for ct in range(ctiles):
                        for blk in range(groups // 8):
                            re = []
                            im = []
                            for g in range(blk * 8, blk * 8 + 8):
                                a0 = rows_of(i, 0, g, ct)
                                a1 = rows_of(i, 1, g, ct)
                                b0 = rows_of(own, 0, g, ct)
                                b1 = rows_of(own, 1, g, ct)
                                re.append(half(a0 * b0 + a1 * b1))
                                im.append(half(a1 * b0 - a0 * b1))
                            racc_ref[i, k, 0, pl.ds(blk * 8, 8), pl.ds(ct * 128, 128)] = fold(re)
                            racc_ref[i, k, 1, pl.ds(blk * 8, 8), pl.ds(ct * 128, 128)] = fold(im)

            return c

        lax.fori_loop(0, own, pairs, 0)

    vmem = pltpu.VMEM
    return pl.pallas_call(
        kernel,
        out_shape=(
            jax.ShapeDtypeStruct(racc_in.shape, jnp.float32),
            jax.ShapeDtypeStruct((1, groups, lanes), jnp.float32),
        ),
        in_specs=[pl.BlockSpec(memory_space=pltpu.SMEM)] + [pl.BlockSpec(memory_space=vmem) for _ in range(3)],
        out_specs=(pl.BlockSpec(memory_space=vmem), pl.BlockSpec(memory_space=vmem)),
        scratch_shapes=[
            pltpu.VMEM((own + 1, 2, rows, cols), jnp.float32),
            pltpu.VMEM((groups, cols), jnp.float32),
        ],
        input_output_aliases={3: 0},
        compiler_params=pltpu.CompilerParams(vmem_limit_bytes=48 * 1024 * 1024),
    )(offsets, slc, rim, racc_in)


def on_device(slc, offsets, owner):
    count = slc.shape[0]
    inner = count - NB
    later = lax.optimization_barrier(slc)
    rims = [shifted((slc if t == 0 else later)[t : t + 1], "date", -1) for t in range(NB)]
    ifg_a, coh_a, ws_a, pw_a, rx_a = local_math(
        offsets, [slc], [(0, t) for t in range(count)], 0, inner, count, 0
    )
    racc = rx_a
    powers = [pw_a[inner:]]
    for step in range(NB - 1):
        racc, pw_step = rim_step(offsets[inner:], racc, slc, rims[step], step, inner)
        powers.append(pw_step)
    powers = jnp.concatenate(powers, 0)
    own = [(0, inner + t) for t in range(NB)]
    ifg_p, coh_p, ws_p = local_math(
        offsets[inner : count - 1],
        [slc] + rims[: NB - 1],
        own + [(1 + t, 0) for t in range(NB - 1)],
        0,
        NB - 1,
        count,
        inner,
        known=(owner, powers, ws_a, racc[: NB - 1], ifg_a, coh_a, 0),
        emit_ws=True,
    )
    interferograms, coherence, slotted = local_math(
        offsets[count - 1 :],
        [slc] + rims,
        own + [(1 + t, 0) for t in range(NB)],
        NB - 1,
        1,
        count,
        count - 1,
        known=(owner, powers, ws_p, racc[NB - 1 :], ifg_p, coh_p, 0),
    )
    width = ifg_a.shape[-1] // owner.shape[0]
    sums = lax.all_to_all(slotted, "date", split_axis=0, concat_axis=0, tiled=True).sum(0)
    halves = ifg_a.shape[3] // SLOT

    def field(f):
        return jnp.concatenate(
            [sums[:, (h * 3 + f) * width : (h * 3 + f + 1) * width] for h in range(halves)], 0
        )

    network_mean = (jnp.stack([field(0), field(1)], 0) / (1.0 + field(2)))[None]
    return (interferograms, coherence, network_mean)


def solution(mesh):
    placed = (P("date", None, "strip", None), P("date", None), P())
    return jax.shard_map(
        on_device,
        mesh=mesh,
        in_specs=placed,
        out_specs=(
            P("date", None, None, "strip", None),
            P("date", None, "strip", None),
            P("date", None, "strip", None),
        ),
        check_vma=False,
    )
```

```python
import jax
import jax.numpy as jnp
from jax import lax
from jax.experimental import pallas as pl
from jax.experimental.pallas import tpu as pltpu
from jax.sharding import PartitionSpec as P

NB = 3
LR = 16
LA = 4
SLOT = 4


def shifted(value, axis, steps):
    count = lax.axis_size(axis)
    pairs = [(source, (source + steps) % count) for source in range(count)]
    return lax.ppermute(value, axis, pairs)


def split_pool(field, pool):
    hi = field.astype(jnp.bfloat16)
    rest = field - hi.astype(jnp.float32)
    mid = rest.astype(jnp.bfloat16)
    lo = (rest - mid.astype(jnp.float32)).astype(jnp.bfloat16)
    out = jnp.dot(hi, pool, preferred_element_type=jnp.float32)
    out = out + jnp.dot(mid, pool, preferred_element_type=jnp.float32)
    return out + jnp.dot(lo, pool, preferred_element_type=jnp.float32)


def make_kernel(images, first, dates, rows, cols, known, tiles, date0, pw_base, emit_ws):
    groups = rows // LR
    cells = cols // LA
    total = len(images)
    ctiles = cols // 128
    lanes = 128
    nsrc = len(set(src for src, _ in images))

    def kernel(*refs):
        off_ref = refs[0]
        if known:
            owner_ref, pw_in, ws_in, rx_in = refs[1:5]
            srcs = refs[7 : 7 + nsrc]
            rest = refs[7 + nsrc :]
            ifg_ref, coh_ref, last_ref = rest[:3]
            xf, pacc, racc, pw, racc_pooled, ifg_s, coh_s, pay, ws_s, osem = rest[3:]
        else:
            srcs = refs[1 : 1 + nsrc]
            rest = refs[1 + nsrc :]
            ifg_ref, coh_ref, last_ref, pw_out, racc_x = rest[:5]
            xf, pacc, racc, pw, racc_pooled, ifg_s, coh_s, osem = rest[5:]
        if known:
            pw_cp = pltpu.make_async_copy(pw_in.at[pl.ds(pw_base, known)], pw.at[pl.ds(0, known)], osem.at[0])
            ws_cp = pltpu.make_async_copy(ws_in, ws_s, osem.at[1])
            rx_cp = pltpu.make_async_copy(rx_in, racc, osem.at[2])
            pw_cp.start()
            ws_cp.start()
            rx_cp.start()
        for t, (src, lead) in enumerate(images):
            if t >= known or (t < NB and t + NB >= known):
                xf[t] = srcs[src][lead].astype(jnp.float32)

        line = lax.broadcasted_iota(jnp.int32, (cols, lanes), 0)
        cell = lax.broadcasted_iota(jnp.int32, (cols, lanes), 1)
        pool = jnp.where(line // LA == cell, 1.0 / (LR * LA), 0.0).astype(jnp.bfloat16)
        sub = lax.broadcasted_iota(jnp.int32, (8, 128), 0)
        masks = {k: (sub % (2 * k)) < k for k in (4, 2, 1)}

        def combine(x, y, k):
            m = masks[k]
            return jnp.where(m, x + pltpu.roll(x, 8 - k, 0), y + pltpu.roll(y, k, 0))

        def fold(parts):
            q = [combine(parts[g], parts[g + 4], 4) for g in range(4)]
            r = [combine(q[0], q[2], 2), combine(q[1], q[3], 2)]
            return combine(r[0], r[1], 1)

        def rows_of(j, comp, g, ct):
            return xf[j, comp, pl.ds(g * LR, LR), pl.ds(ct * 128, 128)]

        def half(v):
            return v[:8] + v[8:]

        def power(j, c):
            for ct in range(ctiles):
                for blk in range(groups // 8):
                    parts = []
                    for g in range(blk * 8, blk * 8 + 8):
                        x0 = rows_of(j, 0, g, ct)
                        x1 = rows_of(j, 1, g, ct)
                        parts.append(half(x0 * x0 + x1 * x1))
                    pacc[j - known, pl.ds(blk * 8, 8), pl.ds(ct * 128, 128)] = fold(parts)
            return c

        fresh = total - known
        if fresh:
            lax.fori_loop(known, total, power, 0)
            pw[pl.ds(known, fresh)] = split_pool(pacc[...].reshape(fresh * groups, cols), pool).reshape(
                fresh, groups, lanes
            )
        if known:
            pw_cp.wait()
        else:
            pw_out[...] = pw[...]

        def partner(i, k):
            return jnp.clip(first + i + off_ref[i, k], 0, total - 1)

        def wanted(i, k):
            reach = first + i + off_ref[i, k]
            if known:
                return reach >= known
            return jnp.logical_or(i < dates, reach <= total - 1)

        def pairs(i, c):
            for k in range(NB):
                j = partner(i, k)

                @pl.when(wanted(i, k))
                def _():
                    for ct in range(ctiles):
                        for blk in range(groups // 8):
                            re = []
                            im = []
                            for g in range(blk * 8, blk * 8 + 8):
                                a0 = rows_of(first + i, 0, g, ct)
                                a1 = rows_of(first + i, 1, g, ct)
                                b0 = rows_of(j, 0, g, ct)
                                b1 = rows_of(j, 1, g, ct)
                                re.append(half(a0 * b0 + a1 * b1))
                                im.append(half(a1 * b0 - a0 * b1))
                            racc[i, k, 0, pl.ds(blk * 8, 8), pl.ds(ct * 128, 128)] = fold(re)
                            racc[i, k, 1, pl.ds(blk * 8, 8), pl.ds(ct * 128, 128)] = fold(im)

            return c

        if known:
            rx_cp.wait()
        lax.fori_loop(0, racc.shape[0], pairs, 0)
        if not known:
            racc_x[...] = racc[pl.ds(dates, racc.shape[0] - dates)]
        pooled = split_pool(racc[pl.ds(0, dates)].reshape(dates * NB * 2 * groups, cols), pool)
        pooled = pooled.reshape(dates, NB, 2, groups, lanes)
        ifg_s[...] = pooled[..., :cells]

        def coher(i, ws):
            wr, wi, wc = ws
            pa = pw[first + i]
            for k in range(NB):
                pb = pw[partner(i, k)]
                re = pooled_at(i, k, 0)
                im = pooled_at(i, k, 1)
                co = jnp.sqrt(re * re + im * im) / jnp.sqrt(pa * pb + 1e-06)
                coh_s[i, k] = co[:, :cells]
                wr = wr + co * re
                wi = wi + co * im
                wc = wc + co
            return (wr, wi, wc)

        racc_pooled[...] = pooled

        def pooled_at(i, k, comp):
            return racc_pooled[i, k, comp]

        zero = jnp.zeros((groups, lanes), jnp.float32)
        if known:
            ws_cp.wait()
            start = (ws_s[0], ws_s[1], ws_s[2])
        else:
            start = (zero, zero, zero)
        wr, wi, wc = lax.fori_loop(0, dates, coher, start)
        outs = [
            pltpu.make_async_copy(ifg_s, ifg_ref.at[pl.ds(date0, dates)], osem.at[3]),
            pltpu.make_async_copy(coh_s, coh_ref.at[pl.ds(date0, dates)], osem.at[4]),
        ]
        for cp in outs:
            cp.start()
        if not known or emit_ws:
            last_ref[0] = wr
            last_ref[1] = wi
            last_ref[2] = wc
            for cp in outs:
                cp.wait()
            return
        width = cells // tiles
        lane = lax.broadcasted_iota(jnp.int32, (SLOT, lanes), 1)
        sums = (wr, wi, wc)
        for t in range(tiles):
            base = t * width
            block = jnp.zeros((SLOT, lanes), jnp.float32)
            for h in range(groups // SLOT):
                for f in range(3):
                    at = (h * 3 + f) * width
                    moved = pltpu.roll(sums[f][h * SLOT : h * SLOT + SLOT], (lanes + at - base) % lanes, 1)
                    block = jnp.where((lane >= at) & (lane < at + width), moved, block)
            last_ref[owner_ref[t]] = block
        for cp in outs:
            cp.wait()

    return kernel


def local_math(offsets, sources, images, first, dates, count, date0, known=None, emit_ws=False):
    pair_dates = offsets.shape[0]
    _, _, rows, cols = sources[0].shape
    groups = rows // LR
    cells = cols // LA
    total = len(images)
    lanes = 128
    vmem = pltpu.VMEM
    smem = pltpu.SMEM
    anyspace = pl.BlockSpec(memory_space=pl.ANY)
    hbm = pl.BlockSpec(memory_space=vmem)
    full = [
        jax.ShapeDtypeStruct((count, NB, 2, groups, cells), jnp.float32),
        jax.ShapeDtypeStruct((count, NB, groups, cells), jnp.float32),
    ]
    scratch = [
        pltpu.VMEM((total, 2, rows, cols), jnp.float32),
        None,
        pltpu.VMEM((pair_dates, NB, 2, groups, cols), jnp.float32),
        pltpu.VMEM((total, groups, lanes), jnp.float32),
        pltpu.VMEM((dates, NB, 2, groups, lanes), jnp.float32),
        pltpu.VMEM((dates, NB, 2, groups, cells), jnp.float32),
        pltpu.VMEM((dates, NB, groups, cells), jnp.float32),
    ]
    if known is None:
        nknown, tiles, pw_base = 0, 0, 0
        out_shape = full + [
            jax.ShapeDtypeStruct((3, groups, lanes), jnp.float32),
            jax.ShapeDtypeStruct((total, groups, lanes), jnp.float32),
            jax.ShapeDtypeStruct((pair_dates - dates, NB, 2, groups, cols), jnp.float32),
        ]
        out_specs = [anyspace, anyspace] + [pl.BlockSpec(memory_space=vmem) for _ in range(3)]
        in_specs = [pl.BlockSpec(memory_space=smem)] + [hbm for _ in sources]
        extra = []
        aliases = {}
    else:
        owner, pw_in, ws_in, rx_in, ifg_in, coh_in, pw_base = known
        nknown, tiles = pw_in.shape[0], owner.shape[0]
        if emit_ws:
            out_shape = full + [jax.ShapeDtypeStruct((3, groups, lanes), jnp.float32)]
        else:
            out_shape = full + [jax.ShapeDtypeStruct((tiles, SLOT, lanes), jnp.float32)]
        out_specs = [anyspace, anyspace, pl.BlockSpec(memory_space=vmem)]
        in_specs = [pl.BlockSpec(memory_space=smem), pl.BlockSpec(memory_space=smem)] + [
            anyspace for _ in range(5)
        ] + [hbm for _ in sources]
        extra = [owner, pw_in, ws_in, rx_in, ifg_in, coh_in]
        aliases = {5: 0, 6: 1}
        scratch += [pltpu.VMEM((tiles, SLOT, lanes), jnp.float32), pltpu.VMEM((3, groups, lanes), jnp.float32)]
    scratch[1] = pltpu.VMEM((max(1, total - nknown), groups, cols), jnp.float32)
    scratch += [pltpu.SemaphoreType.DMA((6,))]
    return pl.pallas_call(
        make_kernel(images, first, dates, rows, cols, nknown, tiles, date0, pw_base, emit_ws),
        out_shape=tuple(out_shape),
        in_specs=in_specs,
        out_specs=tuple(out_specs),
        scratch_shapes=scratch,
        input_output_aliases=aliases,
        compiler_params=pltpu.CompilerParams(vmem_limit_bytes=48 * 1024 * 1024),
    )(offsets, *extra, *sources)


def rim_step(offsets, racc_in, slc, rim, step, inner):
    _, _, rows, cols = slc.shape
    groups = rows // LR
    ctiles = cols // 128
    lanes = 128
    own = slc.shape[0] - inner

    def kernel(off_ref, slc_ref, rim_ref, racc_in_ref, racc_ref, pw_ref, xf, pacc):
        for t in range(own):
            xf[t] = slc_ref[inner + t].astype(jnp.float32)
        xf[own] = rim_ref[0].astype(jnp.float32)
        line = lax.broadcasted_iota(jnp.int32, (cols, lanes), 0)
        cell = lax.broadcasted_iota(jnp.int32, (cols, lanes), 1)
        pool = jnp.where(line // LA == cell, 1.0 / (LR * LA), 0.0).astype(jnp.bfloat16)
        sub = lax.broadcasted_iota(jnp.int32, (8, 128), 0)
        masks = {k: (sub % (2 * k)) < k for k in (4, 2, 1)}

        def combine(x, y, k):
            m = masks[k]
            return jnp.where(m, x + pltpu.roll(x, 8 - k, 0), y + pltpu.roll(y, k, 0))

        def fold(parts):
            q = [combine(parts[g], parts[g + 4], 4) for g in range(4)]
            r = [combine(q[0], q[2], 2), combine(q[1], q[3], 2)]
            return combine(r[0], r[1], 1)

        def rows_of(j, comp, g, ct):
            return xf[j, comp, pl.ds(g * LR, LR), pl.ds(ct * 128, 128)]

        def half(v):
            return v[:8] + v[8:]

        for ct in range(ctiles):
            for blk in range(groups // 8):
                parts = []
                for g in range(blk * 8, blk * 8 + 8):
                    x0 = rows_of(own, 0, g, ct)
                    x1 = rows_of(own, 1, g, ct)
                    parts.append(half(x0 * x0 + x1 * x1))
                pacc[pl.ds(blk * 8, 8), pl.ds(ct * 128, 128)] = fold(parts)
        pw_ref[0] = split_pool(pacc[...], pool)

        def pairs(i, c):
            for k in range(NB):

                @pl.when(i + off_ref[i, k] == own + step)
                def _():
                    for ct in range(ctiles):
                        for blk in range(groups // 8):
                            re = []
                            im = []
                            for g in range(blk * 8, blk * 8 + 8):
                                a0 = rows_of(i, 0, g, ct)
                                a1 = rows_of(i, 1, g, ct)
                                b0 = rows_of(own, 0, g, ct)
                                b1 = rows_of(own, 1, g, ct)
                                re.append(half(a0 * b0 + a1 * b1))
                                im.append(half(a1 * b0 - a0 * b1))
                            racc_ref[i, k, 0, pl.ds(blk * 8, 8), pl.ds(ct * 128, 128)] = fold(re)
                            racc_ref[i, k, 1, pl.ds(blk * 8, 8), pl.ds(ct * 128, 128)] = fold(im)

            return c

        lax.fori_loop(0, own, pairs, 0)

    vmem = pltpu.VMEM
    return pl.pallas_call(
        kernel,
        out_shape=(
            jax.ShapeDtypeStruct(racc_in.shape, jnp.float32),
            jax.ShapeDtypeStruct((1, groups, lanes), jnp.float32),
        ),
        in_specs=[pl.BlockSpec(memory_space=pltpu.SMEM)] + [pl.BlockSpec(memory_space=vmem) for _ in range(3)],
        out_specs=(pl.BlockSpec(memory_space=vmem), pl.BlockSpec(memory_space=vmem)),
        scratch_shapes=[
            pltpu.VMEM((own + 1, 2, rows, cols), jnp.float32),
            pltpu.VMEM((groups, cols), jnp.float32),
        ],
        input_output_aliases={3: 0},
        compiler_params=pltpu.CompilerParams(vmem_limit_bytes=48 * 1024 * 1024),
    )(offsets, slc, rim, racc_in)


def on_device(slc, offsets, owner):
    count = slc.shape[0]
    inner = count - NB
    later = lax.optimization_barrier(slc)
    rims = [shifted((slc if t == 0 else later)[t : t + 1], "date", -1) for t in range(NB)]
    ifg_a, coh_a, ws_a, pw_a, rx_a = local_math(
        offsets, [slc], [(0, t) for t in range(count)], 0, inner, count, 0
    )
    racc = rx_a
    powers = [pw_a[inner:]]
    for step in range(NB - 1):
        racc, pw_step = rim_step(offsets[inner:], racc, slc, rims[step], step, inner)
        powers.append(pw_step)
    powers = jnp.concatenate(powers, 0)
    own = [(0, inner + t) for t in range(NB)]
    ifg_p, coh_p, ws_p = local_math(
        offsets[inner : count - 1],
        [slc] + rims[: NB - 1],
        own + [(1 + t, 0) for t in range(NB - 1)],
        0,
        NB - 1,
        count,
        inner,
        known=(owner, powers, ws_a, racc[: NB - 1], ifg_a, coh_a, 0),
        emit_ws=True,
    )
    interferograms, coherence, slotted = local_math(
        offsets[count - 1 :],
        [slc] + rims,
        own + [(1 + t, 0) for t in range(NB)],
        NB - 1,
        1,
        count,
        count - 1,
        known=(owner, powers, ws_p, racc[NB - 1 :], ifg_p, coh_p, 0),
    )
    width = ifg_a.shape[-1] // owner.shape[0]
    sums = lax.all_to_all(slotted, "date", split_axis=0, concat_axis=0, tiled=True).sum(0)
    halves = ifg_a.shape[3] // SLOT

    def field(f):
        return jnp.concatenate(
            [sums[:, (h * 3 + f) * width : (h * 3 + f + 1) * width] for h in range(halves)], 0
        )

    network_mean = (jnp.stack([field(0), field(1)], 0) / (1.0 + field(2)))[None]
    return (interferograms, coherence, network_mean)


def solution(mesh):
    placed = (P("date", None, "strip", None), P("date", None), P())
    return jax.shard_map(
        on_device,
        mesh=mesh,
        in_specs=placed,
        out_specs=(
            P("date", None, None, "strip", None),
            P("date", None, "strip", None),
            P("date", None, "strip", None),
        ),
        check_vma=False,
    )
```

```python
import jax
import jax.numpy as jnp
from jax import lax
from jax.experimental import pallas as pl
from jax.experimental.pallas import tpu as pltpu
from jax.sharding import PartitionSpec as P

NB = 3
LR = 16
LA = 4
SLOT = 4


def shifted(value, axis, steps):
    count = lax.axis_size(axis)
    pairs = [(source, (source + steps) % count) for source in range(count)]
    return lax.ppermute(value, axis, pairs)


def split_pool(field, pool):
    hi = field.astype(jnp.bfloat16)
    rest = field - hi.astype(jnp.float32)
    mid = rest.astype(jnp.bfloat16)
    lo = (rest - mid.astype(jnp.float32)).astype(jnp.bfloat16)
    out = jnp.dot(hi, pool, preferred_element_type=jnp.float32)
    out = out + jnp.dot(mid, pool, preferred_element_type=jnp.float32)
    return out + jnp.dot(lo, pool, preferred_element_type=jnp.float32)


def make_kernel(images, first, dates, rows, cols, known, tiles, date0, pw_base, emit_ws):
    groups = rows // LR
    cells = cols // LA
    total = len(images)
    ctiles = cols // 128
    lanes = 128
    nsrc = len(set(src for src, _ in images))

    def kernel(*refs):
        off_ref = refs[0]
        if known:
            owner_ref, pw_in, ws_in, rx_in = refs[1:5]
            srcs = refs[7 : 7 + nsrc]
            rest = refs[7 + nsrc :]
            ifg_ref, coh_ref, last_ref = rest[:3]
            xf, pacc, racc, pw, racc_pooled, ifg_s, coh_s, pay, ws_s, osem = rest[3:]
        else:
            srcs = refs[1 : 1 + nsrc]
            rest = refs[1 + nsrc :]
            ifg_ref, coh_ref, last_ref, pw_out, racc_x = rest[:5]
            xf, pacc, racc, pw, racc_pooled, ifg_s, coh_s, osem = rest[5:]
        if known:
            pw_cp = pltpu.make_async_copy(pw_in.at[pl.ds(pw_base, known)], pw.at[pl.ds(0, known)], osem.at[0])
            ws_cp = pltpu.make_async_copy(ws_in, ws_s, osem.at[1])
            rx_cp = pltpu.make_async_copy(rx_in, racc, osem.at[2])
            pw_cp.start()
            ws_cp.start()
            rx_cp.start()
        for t, (src, lead) in enumerate(images):
            if t >= known or (t < NB and t + NB >= known):
                xf[t] = srcs[src][lead].astype(jnp.float32)

        line = lax.broadcasted_iota(jnp.int32, (cols, lanes), 0)
        cell = lax.broadcasted_iota(jnp.int32, (cols, lanes), 1)
        pool = jnp.where(line // LA == cell, 1.0 / (LR * LA), 0.0).astype(jnp.bfloat16)
        sub = lax.broadcasted_iota(jnp.int32, (8, 128), 0)
        masks = {k: (sub % (2 * k)) < k for k in (4, 2, 1)}

        def combine(x, y, k):
            m = masks[k]
            return jnp.where(m, x + pltpu.roll(x, 8 - k, 0), y + pltpu.roll(y, k, 0))

        def fold(parts):
            q = [combine(parts[g], parts[g + 4], 4) for g in range(4)]
            r = [combine(q[0], q[2], 2), combine(q[1], q[3], 2)]
            return combine(r[0], r[1], 1)

        def rows_of(j, comp, g, ct):
            return xf[j, comp, pl.ds(g * LR, LR), pl.ds(ct * 128, 128)]

        def half(v):
            return v[:8] + v[8:]

        def power(j, c):
            for ct in range(ctiles):
                for blk in range(groups // 8):
                    parts = []
                    for g in range(blk * 8, blk * 8 + 8):
                        x0 = rows_of(j, 0, g, ct)
                        x1 = rows_of(j, 1, g, ct)
                        parts.append(half(x0 * x0 + x1 * x1))
                    pacc[j - known, pl.ds(blk * 8, 8), pl.ds(ct * 128, 128)] = fold(parts)
            return c

        fresh = total - known
        if fresh:
            lax.fori_loop(known, total, power, 0)
            pw[pl.ds(known, fresh)] = split_pool(pacc[...].reshape(fresh * groups, cols), pool).reshape(
                fresh, groups, lanes
            )
        if known:
            pw_cp.wait()
        else:
            pw_out[...] = pw[...]

        def partner(i, k):
            return jnp.clip(first + i + off_ref[i, k], 0, total - 1)

        def wanted(i, k):
            reach = first + i + off_ref[i, k]
            if known:
                return reach >= known
            return jnp.logical_or(i < dates, reach <= total - 1)

        def pairs(i, c):
            for k in range(NB):
                j = partner(i, k)

                @pl.when(wanted(i, k))
                def _():
                    for ct in range(ctiles):
                        for blk in range(groups // 8):
                            re = []
                            im = []
                            for g in range(blk * 8, blk * 8 + 8):
                                a0 = rows_of(first + i, 0, g, ct)
                                a1 = rows_of(first + i, 1, g, ct)
                                b0 = rows_of(j, 0, g, ct)
                                b1 = rows_of(j, 1, g, ct)
                                re.append(half(a0 * b0 + a1 * b1))
                                im.append(half(a1 * b0 - a0 * b1))
                            racc[i, k, 0, pl.ds(blk * 8, 8), pl.ds(ct * 128, 128)] = fold(re)
                            racc[i, k, 1, pl.ds(blk * 8, 8), pl.ds(ct * 128, 128)] = fold(im)

            return c

        if known:
            rx_cp.wait()
        lax.fori_loop(0, racc.shape[0], pairs, 0)
        if not known:
            racc_x[...] = racc[pl.ds(dates, racc.shape[0] - dates)]
        pooled = split_pool(racc[pl.ds(0, dates)].reshape(dates * NB * 2 * groups, cols), pool)
        pooled = pooled.reshape(dates, NB, 2, groups, lanes)
        ifg_s[...] = pooled[..., :cells]

        def coher(i, ws):
            wr, wi, wc = ws
            pa = pw[first + i]
            for k in range(NB):
                pb = pw[partner(i, k)]
                re = pooled_at(i, k, 0)
                im = pooled_at(i, k, 1)
                co = jnp.sqrt(re * re + im * im) / jnp.sqrt(pa * pb + 1e-06)
                coh_s[i, k] = co[:, :cells]
                wr = wr + co * re
                wi = wi + co * im
                wc = wc + co
            return (wr, wi, wc)

        racc_pooled[...] = pooled

        def pooled_at(i, k, comp):
            return racc_pooled[i, k, comp]

        zero = jnp.zeros((groups, lanes), jnp.float32)
        if known:
            ws_cp.wait()
            start = (ws_s[0], ws_s[1], ws_s[2])
        else:
            start = (zero, zero, zero)
        wr, wi, wc = lax.fori_loop(0, dates, coher, start)
        outs = [
            pltpu.make_async_copy(ifg_s, ifg_ref.at[pl.ds(date0, dates)], osem.at[3]),
            pltpu.make_async_copy(coh_s, coh_ref.at[pl.ds(date0, dates)], osem.at[4]),
        ]
        for cp in outs:
            cp.start()
        if not known or emit_ws:
            last_ref[0] = wr
            last_ref[1] = wi
            last_ref[2] = wc
            for cp in outs:
                cp.wait()
            return
        width = cells // tiles
        lane = lax.broadcasted_iota(jnp.int32, (SLOT, lanes), 1)
        sums = (wr, wi, wc)
        for t in range(tiles):
            base = t * width
            block = jnp.zeros((SLOT, lanes), jnp.float32)
            for h in range(groups // SLOT):
                for f in range(3):
                    at = (h * 3 + f) * width
                    moved = pltpu.roll(sums[f][h * SLOT : h * SLOT + SLOT], (lanes + at - base) % lanes, 1)
                    block = jnp.where((lane >= at) & (lane < at + width), moved, block)
            pay[owner_ref[t]] = block
        pay_cp = pltpu.make_async_copy(pay, last_ref, osem.at[5])
        pay_cp.start()
        for cp in outs:
            cp.wait()
        pay_cp.wait()

    return kernel


def local_math(offsets, sources, images, first, dates, count, date0, known=None, emit_ws=False):
    pair_dates = offsets.shape[0]
    _, _, rows, cols = sources[0].shape
    groups = rows // LR
    cells = cols // LA
    total = len(images)
    lanes = 128
    vmem = pltpu.VMEM
    smem = pltpu.SMEM
    anyspace = pl.BlockSpec(memory_space=pl.ANY)
    hbm = pl.BlockSpec(memory_space=vmem)
    full = [
        jax.ShapeDtypeStruct((count, NB, 2, groups, cells), jnp.float32),
        jax.ShapeDtypeStruct((count, NB, groups, cells), jnp.float32),
    ]
    scratch = [
        pltpu.VMEM((total, 2, rows, cols), jnp.float32),
        None,
        pltpu.VMEM((pair_dates, NB, 2, groups, cols), jnp.float32),
        pltpu.VMEM((total, groups, lanes), jnp.float32),
        pltpu.VMEM((dates, NB, 2, groups, lanes), jnp.float32),
        pltpu.VMEM((dates, NB, 2, groups, cells), jnp.float32),
        pltpu.VMEM((dates, NB, groups, cells), jnp.float32),
    ]
    if known is None:
        nknown, tiles, pw_base = 0, 0, 0
        out_shape = full + [
            jax.ShapeDtypeStruct((3, groups, lanes), jnp.float32),
            jax.ShapeDtypeStruct((total, groups, lanes), jnp.float32),
            jax.ShapeDtypeStruct((pair_dates - dates, NB, 2, groups, cols), jnp.float32),
        ]
        out_specs = [anyspace, anyspace] + [pl.BlockSpec(memory_space=vmem) for _ in range(3)]
        in_specs = [pl.BlockSpec(memory_space=smem)] + [hbm for _ in sources]
        extra = []
        aliases = {}
    else:
        owner, pw_in, ws_in, rx_in, ifg_in, coh_in, pw_base = known
        nknown, tiles = pw_in.shape[0], owner.shape[0]
        if emit_ws:
            out_shape = full + [jax.ShapeDtypeStruct((3, groups, lanes), jnp.float32)]
        else:
            out_shape = full + [jax.ShapeDtypeStruct((tiles, SLOT, lanes), jnp.float32)]
        out_specs = [anyspace, anyspace, pl.BlockSpec(memory_space=vmem) if emit_ws else anyspace]
        in_specs = [pl.BlockSpec(memory_space=smem), pl.BlockSpec(memory_space=smem)] + [
            anyspace for _ in range(5)
        ] + [hbm for _ in sources]
        extra = [owner, pw_in, ws_in, rx_in, ifg_in, coh_in]
        aliases = {5: 0, 6: 1}
        scratch += [pltpu.VMEM((tiles, SLOT, lanes), jnp.float32), pltpu.VMEM((3, groups, lanes), jnp.float32)]
    scratch[1] = pltpu.VMEM((max(1, total - nknown), groups, cols), jnp.float32)
    scratch += [pltpu.SemaphoreType.DMA((6,))]
    return pl.pallas_call(
        make_kernel(images, first, dates, rows, cols, nknown, tiles, date0, pw_base, emit_ws),
        out_shape=tuple(out_shape),
        in_specs=in_specs,
        out_specs=tuple(out_specs),
        scratch_shapes=scratch,
        input_output_aliases=aliases,
        compiler_params=pltpu.CompilerParams(vmem_limit_bytes=48 * 1024 * 1024),
    )(offsets, *extra, *sources)


def rim_step(offsets, racc_in, slc, rim, step, inner):
    _, _, rows, cols = slc.shape
    groups = rows // LR
    ctiles = cols // 128
    lanes = 128
    own = slc.shape[0] - inner

    def kernel(off_ref, slc_ref, rim_ref, racc_in_ref, racc_ref, pw_ref, xf, pacc):
        for t in range(own):
            xf[t] = slc_ref[inner + t].astype(jnp.float32)
        xf[own] = rim_ref[0].astype(jnp.float32)
        line = lax.broadcasted_iota(jnp.int32, (cols, lanes), 0)
        cell = lax.broadcasted_iota(jnp.int32, (cols, lanes), 1)
        pool = jnp.where(line // LA == cell, 1.0 / (LR * LA), 0.0).astype(jnp.bfloat16)
        sub = lax.broadcasted_iota(jnp.int32, (8, 128), 0)
        masks = {k: (sub % (2 * k)) < k for k in (4, 2, 1)}

        def combine(x, y, k):
            m = masks[k]
            return jnp.where(m, x + pltpu.roll(x, 8 - k, 0), y + pltpu.roll(y, k, 0))

        def fold(parts):
            q = [combine(parts[g], parts[g + 4], 4) for g in range(4)]
            r = [combine(q[0], q[2], 2), combine(q[1], q[3], 2)]
            return combine(r[0], r[1], 1)

        def rows_of(j, comp, g, ct):
            return xf[j, comp, pl.ds(g * LR, LR), pl.ds(ct * 128, 128)]

        def half(v):
            return v[:8] + v[8:]

        for ct in range(ctiles):
            for blk in range(groups // 8):
                parts = []
                for g in range(blk * 8, blk * 8 + 8):
                    x0 = rows_of(own, 0, g, ct)
                    x1 = rows_of(own, 1, g, ct)
                    parts.append(half(x0 * x0 + x1 * x1))
                pacc[pl.ds(blk * 8, 8), pl.ds(ct * 128, 128)] = fold(parts)
        pw_ref[0] = split_pool(pacc[...], pool)

        def pairs(i, c):
            for k in range(NB):

                @pl.when(i + off_ref[i, k] == own + step)
                def _():
                    for ct in range(ctiles):
                        for blk in range(groups // 8):
                            re = []
                            im = []
                            for g in range(blk * 8, blk * 8 + 8):
                                a0 = rows_of(i, 0, g, ct)
                                a1 = rows_of(i, 1, g, ct)
                                b0 = rows_of(own, 0, g, ct)
                                b1 = rows_of(own, 1, g, ct)
                                re.append(half(a0 * b0 + a1 * b1))
                                im.append(half(a1 * b0 - a0 * b1))
                            racc_ref[i, k, 0, pl.ds(blk * 8, 8), pl.ds(ct * 128, 128)] = fold(re)
                            racc_ref[i, k, 1, pl.ds(blk * 8, 8), pl.ds(ct * 128, 128)] = fold(im)

            return c

        lax.fori_loop(0, own, pairs, 0)

    vmem = pltpu.VMEM
    return pl.pallas_call(
        kernel,
        out_shape=(
            jax.ShapeDtypeStruct(racc_in.shape, jnp.float32),
            jax.ShapeDtypeStruct((1, groups, lanes), jnp.float32),
        ),
        in_specs=[pl.BlockSpec(memory_space=pltpu.SMEM)] + [pl.BlockSpec(memory_space=vmem) for _ in range(3)],
        out_specs=(pl.BlockSpec(memory_space=vmem), pl.BlockSpec(memory_space=vmem)),
        scratch_shapes=[
            pltpu.VMEM((own + 1, 2, rows, cols), jnp.float32),
            pltpu.VMEM((groups, cols), jnp.float32),
        ],
        input_output_aliases={3: 0},
        compiler_params=pltpu.CompilerParams(vmem_limit_bytes=48 * 1024 * 1024),
    )(offsets, slc, rim, racc_in)


def on_device(slc, offsets, owner):
    count = slc.shape[0]
    inner = count - NB
    later = lax.optimization_barrier(slc)
    rims = [shifted((slc if t == 0 else later)[t : t + 1], "date", -1) for t in range(NB)]
    ifg_a, coh_a, ws_a, pw_a, rx_a = local_math(
        offsets, [slc], [(0, t) for t in range(count)], 0, inner, count, 0
    )
    racc = rx_a
    powers = [pw_a[inner:]]
    for step in range(NB - 1):
        racc, pw_step = rim_step(offsets[inner:], racc, slc, rims[step], step, inner)
        powers.append(pw_step)
    powers = jnp.concatenate(powers, 0)
    own = [(0, inner + t) for t in range(NB)]
    ifg_p, coh_p, ws_p = local_math(
        offsets[inner : count - 1],
        [slc] + rims[: NB - 1],
        own + [(1 + t, 0) for t in range(NB - 1)],
        0,
        NB - 1,
        count,
        inner,
        known=(owner, powers, ws_a, racc[: NB - 1], ifg_a, coh_a, 0),
        emit_ws=True,
    )
    interferograms, coherence, slotted = local_math(
        offsets[count - 1 :],
        [slc] + rims,
        own + [(1 + t, 0) for t in range(NB)],
        NB - 1,
        1,
        count,
        count - 1,
        known=(owner, powers, ws_p, racc[NB - 1 :], ifg_p, coh_p, 0),
    )
    width = ifg_a.shape[-1] // owner.shape[0]
    sums = lax.all_to_all(slotted, "date", split_axis=0, concat_axis=0, tiled=True).sum(0)
    halves = ifg_a.shape[3] // SLOT

    def field(f):
        return jnp.concatenate(
            [sums[:, (h * 3 + f) * width : (h * 3 + f + 1) * width] for h in range(halves)], 0
        )

    flipped = jnp.stack([field(0).T, field(1).T], 1) / (1.0 + field(2).T[:, None, :])
    network_mean = jnp.transpose(flipped[None], (0, 2, 3, 1))
    return (interferograms, coherence, network_mean)


def solution(mesh):
    placed = (P("date", None, "strip", None), P("date", None), P())
    return jax.shard_map(
        on_device,
        mesh=mesh,
        in_specs=placed,
        out_specs=(
            P("date", None, None, "strip", None),
            P("date", None, "strip", None),
            P("date", None, "strip", None),
        ),
        check_vma=False,
    )
```

```python
import jax
import jax.numpy as jnp
from jax import lax
from jax.experimental import pallas as pl
from jax.experimental.pallas import tpu as pltpu
from jax.sharding import PartitionSpec as P

NB = 3
LR = 16
LA = 4
SLOT = 4


def shifted(value, axis, steps):
    count = lax.axis_size(axis)
    pairs = [(source, (source + steps) % count) for source in range(count)]
    return lax.ppermute(value, axis, pairs)


def split_pool(field, pool):
    hi = field.astype(jnp.bfloat16)
    rest = field - hi.astype(jnp.float32)
    mid = rest.astype(jnp.bfloat16)
    lo = (rest - mid.astype(jnp.float32)).astype(jnp.bfloat16)
    out = jnp.dot(hi, pool, preferred_element_type=jnp.float32)
    out = out + jnp.dot(mid, pool, preferred_element_type=jnp.float32)
    return out + jnp.dot(lo, pool, preferred_element_type=jnp.float32)


def make_kernel(images, first, dates, rows, cols, known, tiles, date0, pw_base, emit_ws):
    groups = rows // LR
    cells = cols // LA
    total = len(images)
    ctiles = cols // 128
    lanes = 128
    nsrc = len(set(src for src, _ in images))

    def kernel(*refs):
        off_ref = refs[0]
        if known:
            owner_ref, pw_in, ws_in, rx_in = refs[1:5]
            srcs = refs[7 : 7 + nsrc]
            rest = refs[7 + nsrc :]
            ifg_ref, coh_ref, last_ref = rest[:3]
            xf, pacc, racc, pw, racc_pooled, ifg_s, coh_s, pay, ws_s, osem = rest[3:]
        else:
            srcs = refs[1 : 1 + nsrc]
            rest = refs[1 + nsrc :]
            ifg_ref, coh_ref, last_ref, pw_out, racc_x = rest[:5]
            xf, pacc, racc, pw, racc_pooled, ifg_s, coh_s, osem = rest[5:]
        if known:
            pw_cp = pltpu.make_async_copy(pw_in.at[pl.ds(pw_base, known)], pw.at[pl.ds(0, known)], osem.at[0])
            ws_cp = pltpu.make_async_copy(ws_in, ws_s, osem.at[1])
            rx_cp = pltpu.make_async_copy(rx_in, racc, osem.at[2])
            pw_cp.start()
            ws_cp.start()
            rx_cp.start()
        need = jnp.bool_(True)
        if known:
            need = jnp.bool_(False)
            for i in range(racc.shape[0]):
                for k in range(NB):
                    need = jnp.logical_or(need, first + i + off_ref[i, k] >= known)

        @pl.when(need)
        def _():
            for t, (src, lead) in enumerate(images):
                if t >= known or (t < NB and t + NB >= known):
                    xf[t] = srcs[src][lead].astype(jnp.float32)

        line = lax.broadcasted_iota(jnp.int32, (cols, lanes), 0)
        cell = lax.broadcasted_iota(jnp.int32, (cols, lanes), 1)
        pool = jnp.where(line // LA == cell, 1.0 / (LR * LA), 0.0).astype(jnp.bfloat16)
        sub = lax.broadcasted_iota(jnp.int32, (8, 128), 0)
        masks = {k: (sub % (2 * k)) < k for k in (4, 2, 1)}

        def combine(x, y, k):
            m = masks[k]
            return jnp.where(m, x + pltpu.roll(x, 8 - k, 0), y + pltpu.roll(y, k, 0))

        def fold(parts):
            q = [combine(parts[g], parts[g + 4], 4) for g in range(4)]
            r = [combine(q[0], q[2], 2), combine(q[1], q[3], 2)]
            return combine(r[0], r[1], 1)

        def rows_of(j, comp, g, ct):
            return xf[j, comp, pl.ds(g * LR, LR), pl.ds(ct * 128, 128)]

        def half(v):
            return v[:8] + v[8:]

        def power(j, c):
            for ct in range(ctiles):
                for blk in range(groups // 8):
                    parts = []
                    for g in range(blk * 8, blk * 8 + 8):
                        x0 = rows_of(j, 0, g, ct)
                        x1 = rows_of(j, 1, g, ct)
                        parts.append(half(x0 * x0 + x1 * x1))
                    pacc[j - known, pl.ds(blk * 8, 8), pl.ds(ct * 128, 128)] = fold(parts)
            return c

        fresh = total - known
        if fresh:

            @pl.when(need)
            def _():
                lax.fori_loop(known, total, power, 0)
                pw[pl.ds(known, fresh)] = split_pool(pacc[...].reshape(fresh * groups, cols), pool).reshape(
                    fresh, groups, lanes
                )
        if known:
            pw_cp.wait()
        else:
            pw_out[...] = pw[...]

        def partner(i, k):
            return jnp.clip(first + i + off_ref[i, k], 0, total - 1)

        def wanted(i, k):
            reach = first + i + off_ref[i, k]
            if known:
                return reach >= known
            return jnp.logical_or(i < dates, reach <= total - 1)

        def pairs(i, c):
            for k in range(NB):
                j = partner(i, k)

                @pl.when(wanted(i, k))
                def _():
                    for ct in range(ctiles):
                        for blk in range(groups // 8):
                            re = []
                            im = []
                            for g in range(blk * 8, blk * 8 + 8):
                                a0 = rows_of(first + i, 0, g, ct)
                                a1 = rows_of(first + i, 1, g, ct)
                                b0 = rows_of(j, 0, g, ct)
                                b1 = rows_of(j, 1, g, ct)
                                re.append(half(a0 * b0 + a1 * b1))
                                im.append(half(a1 * b0 - a0 * b1))
                            racc[i, k, 0, pl.ds(blk * 8, 8), pl.ds(ct * 128, 128)] = fold(re)
                            racc[i, k, 1, pl.ds(blk * 8, 8), pl.ds(ct * 128, 128)] = fold(im)

            return c

        if known:
            rx_cp.wait()
        lax.fori_loop(0, racc.shape[0], pairs, 0)
        if not known:
            racc_x[...] = racc[pl.ds(dates, racc.shape[0] - dates)]
        pooled = split_pool(racc[pl.ds(0, dates)].reshape(dates * NB * 2 * groups, cols), pool)
        pooled = pooled.reshape(dates, NB, 2, groups, lanes)
        ifg_s[...] = pooled[..., :cells]

        def coher(i, ws):
            wr, wi, wc = ws
            pa = pw[first + i]
            for k in range(NB):
                pb = pw[partner(i, k)]
                re = pooled_at(i, k, 0)
                im = pooled_at(i, k, 1)
                co = jnp.sqrt(re * re + im * im) / jnp.sqrt(pa * pb + 1e-06)
                coh_s[i, k] = co[:, :cells]
                wr = wr + co * re
                wi = wi + co * im
                wc = wc + co
            return (wr, wi, wc)

        racc_pooled[...] = pooled

        def pooled_at(i, k, comp):
            return racc_pooled[i, k, comp]

        zero = jnp.zeros((groups, lanes), jnp.float32)
        if known:
            ws_cp.wait()
            start = (ws_s[0], ws_s[1], ws_s[2])
        else:
            start = (zero, zero, zero)
        wr, wi, wc = lax.fori_loop(0, dates, coher, start)
        outs = [
            pltpu.make_async_copy(ifg_s, ifg_ref.at[pl.ds(date0, dates)], osem.at[3]),
            pltpu.make_async_copy(coh_s, coh_ref.at[pl.ds(date0, dates)], osem.at[4]),
        ]
        for cp in outs:
            cp.start()
        if not known or emit_ws:
            last_ref[0] = wr
            last_ref[1] = wi
            last_ref[2] = wc
            for cp in outs:
                cp.wait()
            return
        width = cells // tiles
        lane = lax.broadcasted_iota(jnp.int32, (SLOT, lanes), 1)
        sums = (wr, wi, wc)
        for t in range(tiles):
            base = t * width
            block = jnp.zeros((SLOT, lanes), jnp.float32)
            for h in range(groups // SLOT):
                for f in range(3):
                    at = (h * 3 + f) * width
                    moved = pltpu.roll(sums[f][h * SLOT : h * SLOT + SLOT], (lanes + at - base) % lanes, 1)
                    block = jnp.where((lane >= at) & (lane < at + width), moved, block)
            pay[owner_ref[t]] = block
        pay_cp = pltpu.make_async_copy(pay, last_ref, osem.at[5])
        pay_cp.start()
        for cp in outs:
            cp.wait()
        pay_cp.wait()

    return kernel


def local_math(offsets, sources, images, first, dates, count, date0, known=None, emit_ws=False):
    pair_dates = offsets.shape[0]
    _, _, rows, cols = sources[0].shape
    groups = rows // LR
    cells = cols // LA
    total = len(images)
    lanes = 128
    vmem = pltpu.VMEM
    smem = pltpu.SMEM
    anyspace = pl.BlockSpec(memory_space=pl.ANY)
    hbm = pl.BlockSpec(memory_space=vmem)
    full = [
        jax.ShapeDtypeStruct((count, NB, 2, groups, cells), jnp.float32),
        jax.ShapeDtypeStruct((count, NB, groups, cells), jnp.float32),
    ]
    scratch = [
        pltpu.VMEM((total, 2, rows, cols), jnp.float32),
        None,
        pltpu.VMEM((pair_dates, NB, 2, groups, cols), jnp.float32),
        pltpu.VMEM((total, groups, lanes), jnp.float32),
        pltpu.VMEM((dates, NB, 2, groups, lanes), jnp.float32),
        pltpu.VMEM((dates, NB, 2, groups, cells), jnp.float32),
        pltpu.VMEM((dates, NB, groups, cells), jnp.float32),
    ]
    if known is None:
        nknown, tiles, pw_base = 0, 0, 0
        out_shape = full + [
            jax.ShapeDtypeStruct((3, groups, lanes), jnp.float32),
            jax.ShapeDtypeStruct((total, groups, lanes), jnp.float32),
            jax.ShapeDtypeStruct((pair_dates - dates, NB, 2, groups, cols), jnp.float32),
        ]
        out_specs = [anyspace, anyspace] + [pl.BlockSpec(memory_space=vmem) for _ in range(3)]
        in_specs = [pl.BlockSpec(memory_space=smem)] + [hbm for _ in sources]
        extra = []
        aliases = {}
    else:
        owner, pw_in, ws_in, rx_in, ifg_in, coh_in, pw_base = known
        nknown, tiles = pw_in.shape[0], owner.shape[0]
        if emit_ws:
            out_shape = full + [jax.ShapeDtypeStruct((3, groups, lanes), jnp.float32)]
        else:
            out_shape = full + [jax.ShapeDtypeStruct((tiles, SLOT, lanes), jnp.float32)]
        out_specs = [anyspace, anyspace, pl.BlockSpec(memory_space=vmem) if emit_ws else anyspace]
        in_specs = [pl.BlockSpec(memory_space=smem), pl.BlockSpec(memory_space=smem)] + [
            anyspace for _ in range(5)
        ] + [hbm for _ in sources]
        extra = [owner, pw_in, ws_in, rx_in, ifg_in, coh_in]
        aliases = {5: 0, 6: 1}
        scratch += [pltpu.VMEM((tiles, SLOT, lanes), jnp.float32), pltpu.VMEM((3, groups, lanes), jnp.float32)]
    scratch[1] = pltpu.VMEM((max(1, total - nknown), groups, cols), jnp.float32)
    scratch += [pltpu.SemaphoreType.DMA((6,))]
    return pl.pallas_call(
        make_kernel(images, first, dates, rows, cols, nknown, tiles, date0, pw_base, emit_ws),
        out_shape=tuple(out_shape),
        in_specs=in_specs,
        out_specs=tuple(out_specs),
        scratch_shapes=scratch,
        input_output_aliases=aliases,
        compiler_params=pltpu.CompilerParams(vmem_limit_bytes=48 * 1024 * 1024),
    )(offsets, *extra, *sources)


def rim_step(offsets, racc_in, slc, rim, step, inner):
    _, _, rows, cols = slc.shape
    groups = rows // LR
    ctiles = cols // 128
    lanes = 128
    own = slc.shape[0] - inner

    def kernel(off_ref, slc_ref, rim_ref, racc_in_ref, racc_ref, pw_ref, xf, pacc):
        for t in range(own):
            xf[t] = slc_ref[inner + t].astype(jnp.float32)
        xf[own] = rim_ref[0].astype(jnp.float32)
        line = lax.broadcasted_iota(jnp.int32, (cols, lanes), 0)
        cell = lax.broadcasted_iota(jnp.int32, (cols, lanes), 1)
        pool = jnp.where(line // LA == cell, 1.0 / (LR * LA), 0.0).astype(jnp.bfloat16)
        sub = lax.broadcasted_iota(jnp.int32, (8, 128), 0)
        masks = {k: (sub % (2 * k)) < k for k in (4, 2, 1)}

        def combine(x, y, k):
            m = masks[k]
            return jnp.where(m, x + pltpu.roll(x, 8 - k, 0), y + pltpu.roll(y, k, 0))

        def fold(parts):
            q = [combine(parts[g], parts[g + 4], 4) for g in range(4)]
            r = [combine(q[0], q[2], 2), combine(q[1], q[3], 2)]
            return combine(r[0], r[1], 1)

        def rows_of(j, comp, g, ct):
            return xf[j, comp, pl.ds(g * LR, LR), pl.ds(ct * 128, 128)]

        def half(v):
            return v[:8] + v[8:]

        for ct in range(ctiles):
            for blk in range(groups // 8):
                parts = []
                for g in range(blk * 8, blk * 8 + 8):
                    x0 = rows_of(own, 0, g, ct)
                    x1 = rows_of(own, 1, g, ct)
                    parts.append(half(x0 * x0 + x1 * x1))
                pacc[pl.ds(blk * 8, 8), pl.ds(ct * 128, 128)] = fold(parts)
        pw_ref[0] = split_pool(pacc[...], pool)

        def pairs(i, c):
            for k in range(NB):

                @pl.when(i + off_ref[i, k] == own + step)
                def _():
                    for ct in range(ctiles):
                        for blk in range(groups // 8):
                            re = []
                            im = []
                            for g in range(blk * 8, blk * 8 + 8):
                                a0 = rows_of(i, 0, g, ct)
                                a1 = rows_of(i, 1, g, ct)
                                b0 = rows_of(own, 0, g, ct)
                                b1 = rows_of(own, 1, g, ct)
                                re.append(half(a0 * b0 + a1 * b1))
                                im.append(half(a1 * b0 - a0 * b1))
                            racc_ref[i, k, 0, pl.ds(blk * 8, 8), pl.ds(ct * 128, 128)] = fold(re)
                            racc_ref[i, k, 1, pl.ds(blk * 8, 8), pl.ds(ct * 128, 128)] = fold(im)

            return c

        lax.fori_loop(0, own, pairs, 0)

    vmem = pltpu.VMEM
    return pl.pallas_call(
        kernel,
        out_shape=(
            jax.ShapeDtypeStruct(racc_in.shape, jnp.float32),
            jax.ShapeDtypeStruct((1, groups, lanes), jnp.float32),
        ),
        in_specs=[pl.BlockSpec(memory_space=pltpu.SMEM)] + [pl.BlockSpec(memory_space=vmem) for _ in range(3)],
        out_specs=(pl.BlockSpec(memory_space=vmem), pl.BlockSpec(memory_space=vmem)),
        scratch_shapes=[
            pltpu.VMEM((own + 1, 2, rows, cols), jnp.float32),
            pltpu.VMEM((groups, cols), jnp.float32),
        ],
        input_output_aliases={3: 0},
        compiler_params=pltpu.CompilerParams(vmem_limit_bytes=48 * 1024 * 1024),
    )(offsets, slc, rim, racc_in)


def on_device(slc, offsets, owner):
    count = slc.shape[0]
    inner = count - NB
    later = lax.optimization_barrier(slc)
    rims = [shifted((slc if t == 0 else later)[t : t + 1], "date", -1) for t in range(NB)]
    ifg_a, coh_a, ws_a, pw_a, rx_a = local_math(
        offsets, [slc], [(0, t) for t in range(count)], 0, inner, count, 0
    )
    racc = rx_a
    powers = [pw_a[inner:]]
    for step in range(NB - 1):
        racc, pw_step = rim_step(offsets[inner:], racc, slc, rims[step], step, inner)
        powers.append(pw_step)
    powers = jnp.concatenate(powers, 0)
    own = [(0, inner + t) for t in range(NB)]
    ifg_p, coh_p, ws_p = local_math(
        offsets[inner : count - 1],
        [slc] + rims[: NB - 1],
        own + [(1 + t, 0) for t in range(NB - 1)],
        0,
        NB - 1,
        count,
        inner,
        known=(owner, powers, ws_a, racc[: NB - 1], ifg_a, coh_a, 0),
        emit_ws=True,
    )
    interferograms, coherence, slotted = local_math(
        offsets[count - 1 :],
        [slc] + rims,
        own + [(1 + t, 0) for t in range(NB)],
        NB - 1,
        1,
        count,
        count - 1,
        known=(owner, powers, ws_p, racc[NB - 1 :], ifg_p, coh_p, 0),
    )
    width = ifg_a.shape[-1] // owner.shape[0]
    sums = lax.all_to_all(slotted, "date", split_axis=0, concat_axis=0, tiled=True).sum(0)
    halves = ifg_a.shape[3] // SLOT

    def field(f):
        return jnp.concatenate(
            [sums[:, (h * 3 + f) * width : (h * 3 + f + 1) * width] for h in range(halves)], 0
        )

    flipped = jnp.stack([field(0).T, field(1).T], 1) / (1.0 + field(2).T[:, None, :])
    network_mean = jnp.transpose(flipped[None], (0, 2, 3, 1))
    return (interferograms, coherence, network_mean)


def solution(mesh):
    placed = (P("date", None, "strip", None), P("date", None), P())
    return jax.shard_map(
        on_device,
        mesh=mesh,
        in_specs=placed,
        out_specs=(
            P("date", None, None, "strip", None),
            P("date", None, "strip", None),
            P("date", None, "strip", None),
        ),
        check_vma=False,
    )
```

```python
import jax
import jax.numpy as jnp
from jax import lax
from jax.experimental import pallas as pl
from jax.experimental.pallas import tpu as pltpu
from jax.sharding import PartitionSpec as P

NB = 3
LR = 16
LA = 4
SLOT = 4


def shifted(value, axis, steps):
    count = lax.axis_size(axis)
    pairs = [(source, (source + steps) % count) for source in range(count)]
    return lax.ppermute(value, axis, pairs)


def split_pool(field, pool):
    hi = field.astype(jnp.bfloat16)
    rest = field - hi.astype(jnp.float32)
    mid = rest.astype(jnp.bfloat16)
    lo = (rest - mid.astype(jnp.float32)).astype(jnp.bfloat16)
    out = jnp.dot(hi, pool, preferred_element_type=jnp.float32)
    out = out + jnp.dot(mid, pool, preferred_element_type=jnp.float32)
    return out + jnp.dot(lo, pool, preferred_element_type=jnp.float32)


def make_kernel(images, first, dates, rows, cols, known, tiles, date0, pw_base, emit_ws):
    groups = rows // LR
    cells = cols // LA
    total = len(images)
    ctiles = cols // 128
    lanes = 128
    nsrc = len(set(src for src, _ in images))

    def kernel(*refs):
        off_ref = refs[0]
        if known:
            owner_ref, pw_in, ws_in, rx_in = refs[1:5]
            srcs = refs[7 : 7 + nsrc]
            rest = refs[7 + nsrc :]
            ifg_ref, coh_ref, last_ref = rest[:3]
            xf, pacc, racc, pw, racc_pooled, ifg_s, coh_s, pay, ws_s, osem = rest[3:]
        else:
            srcs = refs[1 : 1 + nsrc]
            rest = refs[1 + nsrc :]
            ifg_ref, coh_ref, last_ref, pw_out, racc_x = rest[:5]
            xf, pacc, racc, pw, racc_pooled, ifg_s, coh_s, osem = rest[5:]
        if known:
            pw_cp = pltpu.make_async_copy(pw_in.at[pl.ds(pw_base, known)], pw.at[pl.ds(0, known)], osem.at[0])
            ws_cp = pltpu.make_async_copy(ws_in, ws_s, osem.at[1])
            rx_cp = pltpu.make_async_copy(rx_in, racc, osem.at[2])
            pw_cp.start()
            ws_cp.start()
            rx_cp.start()
        for t, (src, lead) in enumerate(images):
            if t >= known or (t < NB and t + NB >= known):
                xf[t] = srcs[src][lead].astype(jnp.float32)

        line = lax.broadcasted_iota(jnp.int32, (cols, lanes), 0)
        cell = lax.broadcasted_iota(jnp.int32, (cols, lanes), 1)
        pool = jnp.where(line // LA == cell, 1.0 / (LR * LA), 0.0).astype(jnp.bfloat16)
        sub = lax.broadcasted_iota(jnp.int32, (8, 128), 0)
        masks = {k: (sub % (2 * k)) < k for k in (4, 2, 1)}

        def combine(x, y, k):
            m = masks[k]
            return jnp.where(m, x + pltpu.roll(x, 8 - k, 0), y + pltpu.roll(y, k, 0))

        def fold(parts):
            q = [combine(parts[g], parts[g + 4], 4) for g in range(4)]
            r = [combine(q[0], q[2], 2), combine(q[1], q[3], 2)]
            return combine(r[0], r[1], 1)

        def rows_of(j, comp, g, ct):
            return xf[j, comp, pl.ds(g * LR, LR), pl.ds(ct * 128, 128)]

        def half(v):
            return v[:8] + v[8:]

        def power(j, c):
            for ct in range(ctiles):
                for blk in range(groups // 8):
                    parts = []
                    for g in range(blk * 8, blk * 8 + 8):
                        x0 = rows_of(j, 0, g, ct)
                        x1 = rows_of(j, 1, g, ct)
                        parts.append(half(x0 * x0 + x1 * x1))
                    pacc[j - known, pl.ds(blk * 8, 8), pl.ds(ct * 128, 128)] = fold(parts)
            return c

        fresh = total - known
        if fresh:
            lax.fori_loop(known, total, power, 0)
            if not known:
                pw[pl.ds(known, fresh)] = split_pool(pacc[...].reshape(fresh * groups, cols), pool).reshape(
                    fresh, groups, lanes
                )
        if known:
            pw_cp.wait()
        else:
            pw_out[...] = pw[...]

        def partner(i, k):
            return jnp.clip(first + i + off_ref[i, k], 0, total - 1)

        def wanted(i, k):
            reach = first + i + off_ref[i, k]
            if known:
                return reach >= known
            return jnp.logical_or(i < dates, reach <= total - 1)

        def pairs(i, c):
            for k in range(NB):
                j = partner(i, k)

                @pl.when(wanted(i, k))
                def _():
                    for ct in range(ctiles):
                        for blk in range(groups // 8):
                            re = []
                            im = []
                            for g in range(blk * 8, blk * 8 + 8):
                                a0 = rows_of(first + i, 0, g, ct)
                                a1 = rows_of(first + i, 1, g, ct)
                                b0 = rows_of(j, 0, g, ct)
                                b1 = rows_of(j, 1, g, ct)
                                re.append(half(a0 * b0 + a1 * b1))
                                im.append(half(a1 * b0 - a0 * b1))
                            racc[i, k, 0, pl.ds(blk * 8, 8), pl.ds(ct * 128, 128)] = fold(re)
                            racc[i, k, 1, pl.ds(blk * 8, 8), pl.ds(ct * 128, 128)] = fold(im)

            return c

        if known:
            rx_cp.wait()
        lax.fori_loop(0, racc.shape[0], pairs, 0)
        if not known:
            racc_x[...] = racc[pl.ds(dates, racc.shape[0] - dates)]
        pair_rows = racc[pl.ds(0, dates)].reshape(dates * NB * 2 * groups, cols)
        if known and fresh:
            both = split_pool(jnp.concatenate([pacc[...].reshape(fresh * groups, cols), pair_rows], 0), pool)
            pw[pl.ds(known, fresh)] = both[: fresh * groups].reshape(fresh, groups, lanes)
            pooled = both[fresh * groups :]
        else:
            pooled = split_pool(pair_rows, pool)
        pooled = pooled.reshape(dates, NB, 2, groups, lanes)
        ifg_s[...] = pooled[..., :cells]

        def coher(i, ws):
            wr, wi, wc = ws
            pa = pw[first + i]
            for k in range(NB):
                pb = pw[partner(i, k)]
                re = pooled_at(i, k, 0)
                im = pooled_at(i, k, 1)
                co = jnp.sqrt(re * re + im * im) / jnp.sqrt(pa * pb + 1e-06)
                coh_s[i, k] = co[:, :cells]
                wr = wr + co * re
                wi = wi + co * im
                wc = wc + co
            return (wr, wi, wc)

        racc_pooled[...] = pooled

        def pooled_at(i, k, comp):
            return racc_pooled[i, k, comp]

        zero = jnp.zeros((groups, lanes), jnp.float32)
        if known:
            ws_cp.wait()
            start = (ws_s[0], ws_s[1], ws_s[2])
        else:
            start = (zero, zero, zero)
        wr, wi, wc = lax.fori_loop(0, dates, coher, start)
        outs = [
            pltpu.make_async_copy(ifg_s, ifg_ref.at[pl.ds(date0, dates)], osem.at[3]),
            pltpu.make_async_copy(coh_s, coh_ref.at[pl.ds(date0, dates)], osem.at[4]),
        ]
        for cp in outs:
            cp.start()
        if not known or emit_ws:
            last_ref[0] = wr
            last_ref[1] = wi
            last_ref[2] = wc
            for cp in outs:
                cp.wait()
            return
        width = cells // tiles
        lane = lax.broadcasted_iota(jnp.int32, (SLOT, lanes), 1)
        sums = (wr, wi, wc)
        for t in range(tiles):
            base = t * width
            block = jnp.zeros((SLOT, lanes), jnp.float32)
            for h in range(groups // SLOT):
                for f in range(3):
                    at = (h * 3 + f) * width
                    moved = pltpu.roll(sums[f][h * SLOT : h * SLOT + SLOT], (lanes + at - base) % lanes, 1)
                    block = jnp.where((lane >= at) & (lane < at + width), moved, block)
            pay[owner_ref[t]] = block
        pay_cp = pltpu.make_async_copy(pay, last_ref, osem.at[5])
        pay_cp.start()
        for cp in outs:
            cp.wait()
        pay_cp.wait()

    return kernel


def local_math(offsets, sources, images, first, dates, count, date0, known=None, emit_ws=False):
    pair_dates = offsets.shape[0]
    _, _, rows, cols = sources[0].shape
    groups = rows // LR
    cells = cols // LA
    total = len(images)
    lanes = 128
    vmem = pltpu.VMEM
    smem = pltpu.SMEM
    anyspace = pl.BlockSpec(memory_space=pl.ANY)
    hbm = pl.BlockSpec(memory_space=vmem)
    full = [
        jax.ShapeDtypeStruct((count, NB, 2, groups, cells), jnp.float32),
        jax.ShapeDtypeStruct((count, NB, groups, cells), jnp.float32),
    ]
    scratch = [
        pltpu.VMEM((total, 2, rows, cols), jnp.float32),
        None,
        pltpu.VMEM((pair_dates, NB, 2, groups, cols), jnp.float32),
        pltpu.VMEM((total, groups, lanes), jnp.float32),
        pltpu.VMEM((dates, NB, 2, groups, lanes), jnp.float32),
        pltpu.VMEM((dates, NB, 2, groups, cells), jnp.float32),
        pltpu.VMEM((dates, NB, groups, cells), jnp.float32),
    ]
    if known is None:
        nknown, tiles, pw_base = 0, 0, 0
        out_shape = full + [
            jax.ShapeDtypeStruct((3, groups, lanes), jnp.float32),
            jax.ShapeDtypeStruct((total, groups, lanes), jnp.float32),
            jax.ShapeDtypeStruct((pair_dates - dates, NB, 2, groups, cols), jnp.float32),
        ]
        out_specs = [anyspace, anyspace] + [pl.BlockSpec(memory_space=vmem) for _ in range(3)]
        in_specs = [pl.BlockSpec(memory_space=smem)] + [hbm for _ in sources]
        extra = []
        aliases = {}
    else:
        owner, pw_in, ws_in, rx_in, ifg_in, coh_in, pw_base = known
        nknown, tiles = pw_in.shape[0], owner.shape[0]
        if emit_ws:
            out_shape = full + [jax.ShapeDtypeStruct((3, groups, lanes), jnp.float32)]
        else:
            out_shape = full + [jax.ShapeDtypeStruct((tiles, SLOT, lanes), jnp.float32)]
        out_specs = [anyspace, anyspace, pl.BlockSpec(memory_space=vmem) if emit_ws else anyspace]
        in_specs = [pl.BlockSpec(memory_space=smem), pl.BlockSpec(memory_space=smem)] + [
            anyspace for _ in range(5)
        ] + [hbm for _ in sources]
        extra = [owner, pw_in, ws_in, rx_in, ifg_in, coh_in]
        aliases = {5: 0, 6: 1}
        scratch += [pltpu.VMEM((tiles, SLOT, lanes), jnp.float32), pltpu.VMEM((3, groups, lanes), jnp.float32)]
    scratch[1] = pltpu.VMEM((max(1, total - nknown), groups, cols), jnp.float32)
    scratch += [pltpu.SemaphoreType.DMA((6,))]
    return pl.pallas_call(
        make_kernel(images, first, dates, rows, cols, nknown, tiles, date0, pw_base, emit_ws),
        out_shape=tuple(out_shape),
        in_specs=in_specs,
        out_specs=tuple(out_specs),
        scratch_shapes=scratch,
        input_output_aliases=aliases,
        compiler_params=pltpu.CompilerParams(vmem_limit_bytes=48 * 1024 * 1024),
    )(offsets, *extra, *sources)


def rim_step(offsets, racc_in, slc, rim, step, inner):
    _, _, rows, cols = slc.shape
    groups = rows // LR
    ctiles = cols // 128
    lanes = 128
    own = slc.shape[0] - inner

    def kernel(off_ref, slc_ref, rim_ref, racc_in_ref, racc_ref, pw_ref, xf, pacc):
        for t in range(own):
            xf[t] = slc_ref[inner + t].astype(jnp.float32)
        xf[own] = rim_ref[0].astype(jnp.float32)
        line = lax.broadcasted_iota(jnp.int32, (cols, lanes), 0)
        cell = lax.broadcasted_iota(jnp.int32, (cols, lanes), 1)
        pool = jnp.where(line // LA == cell, 1.0 / (LR * LA), 0.0).astype(jnp.bfloat16)
        sub = lax.broadcasted_iota(jnp.int32, (8, 128), 0)
        masks = {k: (sub % (2 * k)) < k for k in (4, 2, 1)}

        def combine(x, y, k):
            m = masks[k]
            return jnp.where(m, x + pltpu.roll(x, 8 - k, 0), y + pltpu.roll(y, k, 0))

        def fold(parts):
            q = [combine(parts[g], parts[g + 4], 4) for g in range(4)]
            r = [combine(q[0], q[2], 2), combine(q[1], q[3], 2)]
            return combine(r[0], r[1], 1)

        def rows_of(j, comp, g, ct):
            return xf[j, comp, pl.ds(g * LR, LR), pl.ds(ct * 128, 128)]

        def half(v):
            return v[:8] + v[8:]

        for ct in range(ctiles):
            for blk in range(groups // 8):
                parts = []
                for g in range(blk * 8, blk * 8 + 8):
                    x0 = rows_of(own, 0, g, ct)
                    x1 = rows_of(own, 1, g, ct)
                    parts.append(half(x0 * x0 + x1 * x1))
                pacc[pl.ds(blk * 8, 8), pl.ds(ct * 128, 128)] = fold(parts)
        pw_ref[0] = split_pool(pacc[...], pool)

        def pairs(i, c):
            for k in range(NB):

                @pl.when(i + off_ref[i, k] == own + step)
                def _():
                    for ct in range(ctiles):
                        for blk in range(groups // 8):
                            re = []
                            im = []
                            for g in range(blk * 8, blk * 8 + 8):
                                a0 = rows_of(i, 0, g, ct)
                                a1 = rows_of(i, 1, g, ct)
                                b0 = rows_of(own, 0, g, ct)
                                b1 = rows_of(own, 1, g, ct)
                                re.append(half(a0 * b0 + a1 * b1))
                                im.append(half(a1 * b0 - a0 * b1))
                            racc_ref[i, k, 0, pl.ds(blk * 8, 8), pl.ds(ct * 128, 128)] = fold(re)
                            racc_ref[i, k, 1, pl.ds(blk * 8, 8), pl.ds(ct * 128, 128)] = fold(im)

            return c

        lax.fori_loop(0, own, pairs, 0)

    vmem = pltpu.VMEM
    return pl.pallas_call(
        kernel,
        out_shape=(
            jax.ShapeDtypeStruct(racc_in.shape, jnp.float32),
            jax.ShapeDtypeStruct((1, groups, lanes), jnp.float32),
        ),
        in_specs=[pl.BlockSpec(memory_space=pltpu.SMEM)] + [pl.BlockSpec(memory_space=vmem) for _ in range(3)],
        out_specs=(pl.BlockSpec(memory_space=vmem), pl.BlockSpec(memory_space=vmem)),
        scratch_shapes=[
            pltpu.VMEM((own + 1, 2, rows, cols), jnp.float32),
            pltpu.VMEM((groups, cols), jnp.float32),
        ],
        input_output_aliases={3: 0},
        compiler_params=pltpu.CompilerParams(vmem_limit_bytes=48 * 1024 * 1024),
    )(offsets, slc, rim, racc_in)


def on_device(slc, offsets, owner):
    count = slc.shape[0]
    inner = count - NB
    later = lax.optimization_barrier(slc)
    rims = [shifted((slc if t == 0 else later)[t : t + 1], "date", -1) for t in range(NB)]
    ifg_a, coh_a, ws_a, pw_a, rx_a = local_math(
        offsets, [slc], [(0, t) for t in range(count)], 0, inner, count, 0
    )
    racc = rx_a
    powers = [pw_a[inner:]]
    for step in range(NB - 1):
        racc, pw_step = rim_step(offsets[inner:], racc, slc, rims[step], step, inner)
        powers.append(pw_step)
    powers = jnp.concatenate(powers, 0)
    own = [(0, inner + t) for t in range(NB)]
    ifg_p, coh_p, ws_p = local_math(
        offsets[inner : count - 1],
        [slc] + rims[: NB - 1],
        own + [(1 + t, 0) for t in range(NB - 1)],
        0,
        NB - 1,
        count,
        inner,
        known=(owner, powers, ws_a, racc[: NB - 1], ifg_a, coh_a, 0),
        emit_ws=True,
    )
    interferograms, coherence, slotted = local_math(
        offsets[count - 1 :],
        [slc] + rims,
        own + [(1 + t, 0) for t in range(NB)],
        NB - 1,
        1,
        count,
        count - 1,
        known=(owner, powers, ws_p, racc[NB - 1 :], ifg_p, coh_p, 0),
    )
    width = ifg_a.shape[-1] // owner.shape[0]
    sums = lax.all_to_all(slotted, "date", split_axis=0, concat_axis=0, tiled=True).sum(0)
    halves = ifg_a.shape[3] // SLOT

    def field(f):
        return jnp.concatenate(
            [sums[:, (h * 3 + f) * width : (h * 3 + f + 1) * width] for h in range(halves)], 0
        )

    flipped = jnp.stack([field(0).T, field(1).T], 1) / (1.0 + field(2).T[:, None, :])
    network_mean = jnp.transpose(flipped[None], (0, 2, 3, 1))
    return (interferograms, coherence, network_mean)


def solution(mesh):
    placed = (P("date", None, "strip", None), P("date", None), P())
    return jax.shard_map(
        on_device,
        mesh=mesh,
        in_specs=placed,
        out_specs=(
            P("date", None, None, "strip", None),
            P("date", None, "strip", None),
            P("date", None, "strip", None),
        ),
        check_vma=False,
    )
```
